128 devices in a mesh: src: 16 (over y_hi, z, core), tgt: 8 (over y_lo, x).
Axes of the slice: x: 4, y: 4 (y_hi: 2, y_lo: 2; y = y_hi * 2 + y_lo), z: 4, core: 2. Of those that a mesh axis runs over, the one named last changes fastest.
Arguments:
- positions: float32 [3, 16384], P(None, ('src', 'tgt')), as said below
- contact_bodies: int32 [2, 131072], P(None, ('src', 'tgt')), may hold values from 0 to 16383, as said below
- contact_frame: float32 [9, 131072], P(None, ('src', 'tgt')), as said below
- gaps: float32 [131072], P(('src', 'tgt')), may hold values from -1 to 1
- impulse_now: float32 [131072], P(('src', 'tgt')), may hold values from 0 to 1
- impulse_prev: float32 [131072], P(('src', 'tgt')), may hold values from 0 to 1
- step_sizes: float32 [2], replicated, may hold values from 0.05 to 0.2
Outputs:
- impulse: float32 [131072], P(('src', 'tgt'))
- body_velocity: float32 [6, 16384], P(None, ('src', 'tgt'))
The draws below stay inside these ranges and needn't reach their ends.
Inputs may be any that keep to these rules, and one draw needn't show every extreme that they name: `contact_bodies`: each contact joins a body i with body i + 1, i + 32 or i + 1024, modulo 16384. `positions`: body k lies within 0.45 of the point 3 (k mod 32, k // 32 mod 32, k // 1024) along each coordinate. `contact_frame`: rows 0 to 2 of each column are a unit vector; rows 3 to 8 lie in -2 to 2.
All inputs are finite; a program needn't handle non-finite values.
Results may differ from the reference program's by a relative error of at most 0.0003.
Values sent between devices are 32-bit elements; how exact they have to be, the bound alone decides.
No kernel may reach another device: no remote copies, remote signals or barrier semaphores. Data moves between devices by JAX's collectives and lax.ppermute only.
A program may use at most 64 MiB of HBM per device.

```python
import math
import jax
import jax.numpy as jnp
from jax import lax

ITERS = 2
BODIES = 16384
CONTACTS = 131072


def draw_positions(key, part):
    body_ids = jnp.arange(BODIES, dtype=jnp.int32)
    lattice = jnp.stack([body_ids % 32, body_ids // 32 % 32, body_ids // 1024]).astype(jnp.float32) * 3.0
    jitter = jax.random.uniform(key, (3, BODIES), jnp.float32, -0.4, 0.4)
    return lattice + jitter


def draw_contact_bodies(key, part):
    key_first, key_direction = jax.random.split(key)
    first = jax.random.randint(key_first, (CONTACTS,), 0, BODIES, jnp.int32)
    direction = jax.random.randint(key_direction, (CONTACTS,), 0, 3, jnp.int32)
    direction = direction.at[1].set(0)
    first = first.at[0].set(BODIES - 1).at[1].set(BODIES - 1)
    offset = jnp.where(direction == 0, 1, jnp.where(direction == 1, 32, 1024))
    second = (first + offset) % BODIES
    return jnp.stack([first, second]).astype(jnp.int32)


def draw_contact_frame(key, part):
    key_polar, key_azimuth, key_arms = jax.random.split(key, 3)
    polar = jax.random.uniform(key_polar, (CONTACTS,), jnp.float32, 0.0, 3.14159265)
    azimuth = jax.random.uniform(key_azimuth, (CONTACTS,), jnp.float32, -3.14159265, 3.14159265)
    normal = jnp.stack([jnp.sin(polar) * jnp.cos(azimuth), jnp.sin(polar) * jnp.sin(azimuth), jnp.cos(polar)])
    levers = jnp.clip(0.8 * jax.random.normal(key_arms, (6, CONTACTS), jnp.float32), -2.0, 2.0)
    return jnp.concatenate([normal, levers]).astype(jnp.float32)


def level_of(stream_key, extent, cuts, smallest, largest):
    level = 1.0
    for position, parts in cuts:
        draws = jax.random.uniform(jax.random.fold_in(jax.random.fold_in(stream_key, 6), position), (parts,), jnp.float32, smallest / len(cuts), largest / len(cuts))
        level = level * jnp.repeat(jnp.exp(draws), extent[position] // parts).reshape((-1,) + (1,) * (len(extent) - 1 - position))
    return level


def setup_inputs(seed: int = 0) -> dict:
    arg_keys = jax.random.split(jax.random.key(seed), 8)
    return {
        "positions": draw_positions(jax.random.fold_in(arg_keys[7], 71), 0),
        "contact_bodies": draw_contact_bodies(jax.random.fold_in(arg_keys[7], 71), 0),
        "contact_frame": draw_contact_frame(jax.random.fold_in(arg_keys[7], 71), 0),
        "gaps": jnp.clip(jax.random.uniform(arg_keys[3], (CONTACTS,), jnp.float32, -1.0, 1.0) * level_of(arg_keys[3], (CONTACTS,), ((0, 128),), -0.4, 0.0), -1.0, 1.0),
        "impulse_now": jnp.clip(1.0 * jax.random.uniform(arg_keys[4], (CONTACTS,), jnp.float32) ** level_of(arg_keys[4], (CONTACTS,), ((0, 128),), -0.2, 0.2), 0.0, 1.0),
        "impulse_prev": jnp.clip(1.0 * jax.random.uniform(arg_keys[5], (CONTACTS,), jnp.float32) ** level_of(arg_keys[5], (CONTACTS,), ((0, 128),), -0.2, 0.2), 0.0, 1.0),
        "step_sizes": jnp.clip(jax.random.uniform(arg_keys[6], (ITERS,), jnp.float32, 0.05, 0.2), 0.05, 0.2),
    }


MOMENTUM = 0.4

def cross_product(first, second):
    return jnp.stack([first[1] * second[2] - first[2] * second[1], first[2] * second[0] - first[0] * second[2], first[0] * second[1] - first[1] * second[0]])

def contact_rows(frame):
    normal = frame[0:3]
    lever_first = cross_product(frame[3:6], normal)
    lever_second = cross_product(frame[6:9], normal)
    return (jnp.concatenate([-normal, -lever_first]), jnp.concatenate([normal, lever_second]))

def pair_block(target_pos, target_ids, source_pos, source_ids, forces):
    delta_x = target_pos[0][:, None] - source_pos[0][None, :]
    delta_y = target_pos[1][:, None] - source_pos[1][None, :]
    delta_z = target_pos[2][:, None] - source_pos[2][None, :]
    coincide = target_ids[:, None] == source_ids[None, :]
    dist_sq = jnp.where(coincide, 1.0, delta_x * delta_x + delta_y * delta_y + delta_z * delta_z)
    inverse = jnp.where(coincide, 0.0, lax.rsqrt(dist_sq))
    self_term = jnp.where(coincide, 1.0, 0.0)
    unit_x = delta_x * inverse
    unit_y = delta_y * inverse
    unit_z = delta_z * inverse
    force_x, force_y, force_z = (forces[0][None, :], forces[1][None, :], forces[2][None, :])
    torque_x, torque_y, torque_z = (forces[3][None, :], forces[4][None, :], forces[5][None, :])
    inverse_sq = inverse * inverse
    c_one = 0.75 * inverse
    c_two = 0.75 * inverse_sq
    c_three = 0.375 * inverse_sq * inverse
    along_force = unit_x * force_x + unit_y * force_y + unit_z * force_z
    along_torque = unit_x * torque_x + unit_y * torque_y + unit_z * torque_z
    isotropic = c_one * (1.0 + inverse_sq * (2.0 / 3.0)) + self_term
    dyadic = c_one * (1.0 - 2.0 * inverse_sq) * along_force
    vel_x = isotropic * force_x + dyadic * unit_x + c_two * (torque_y * unit_z - torque_z * unit_y)
    vel_y = isotropic * force_y + dyadic * unit_y + c_two * (torque_z * unit_x - torque_x * unit_z)
    vel_z = isotropic * force_z + dyadic * unit_z + c_two * (torque_x * unit_y - torque_y * unit_x)
    spin_self = 0.75 * self_term - c_three
    spin_x = c_two * (force_y * unit_z - force_z * unit_y) + c_three * 3.0 * unit_x * along_torque + spin_self * torque_x
    spin_y = c_two * (force_z * unit_x - force_x * unit_z) + c_three * 3.0 * unit_y * along_torque + spin_self * torque_y
    spin_z = c_two * (force_x * unit_y - force_y * unit_x) + c_three * 3.0 * unit_z * along_torque + spin_self * torque_z
    return jnp.stack([lax.optimization_barrier(jnp.sum(vel_x, 1)), lax.optimization_barrier(jnp.sum(vel_y, 1)), lax.optimization_barrier(jnp.sum(vel_z, 1)), lax.optimization_barrier(jnp.sum(spin_x, 1)), lax.optimization_barrier(jnp.sum(spin_y, 1)), lax.optimization_barrier(jnp.sum(spin_z, 1))])

def mobility(positions, body_ids, forces):
    body_count = positions.shape[1]
    block_size = math.gcd(body_count, 256)
    blocks = body_count // block_size
    target_pos = positions.reshape(3, blocks, block_size).transpose(1, 0, 2)
    target_ids = body_ids.reshape(blocks, block_size)

    def one_block(pair):
        return pair_block(pair[0], pair[1], positions, body_ids, forces)
    result = lax.map(one_block, (target_pos, target_ids))
    return result.transpose(1, 0, 2).reshape(6, body_count)

def reference(positions, contact_bodies, contact_frame, gaps, impulse_now, impulse_prev, step_sizes):
    body_count = positions.shape[1]
    body_ids = jnp.arange(body_count, dtype=jnp.int32)
    first_rows, second_rows = contact_rows(contact_frame)
    current = impulse_now
    shifted = impulse_now + MOMENTUM * (impulse_now - impulse_prev)
    velocity = jnp.zeros((6, body_count), jnp.float32)
    for k in range(ITERS):
        forces = jnp.zeros((6, body_count), jnp.float32)
        forces = forces.at[:, contact_bodies[0]].add(first_rows * shifted[None, :])
        forces = forces.at[:, contact_bodies[1]].add(second_rows * shifted[None, :])
        velocity = mobility(positions, body_ids, forces)
        normal_rate = lax.optimization_barrier(jnp.sum(first_rows * velocity[:, contact_bodies[0]], 0)) + lax.optimization_barrier(jnp.sum(second_rows * velocity[:, contact_bodies[1]], 0))
        updated = jnp.maximum(shifted - step_sizes[k] * (gaps + normal_rate), 0.0)
        shifted = updated + MOMENTUM * (updated - current)
        current = updated
    return (current, velocity)
```

```python
import jax
import jax.numpy as jnp
from jax import lax
from jax.sharding import PartitionSpec as P

ITERS = 2
MOMENTUM = 0.4
AXES = ("src", "tgt")
SOURCE_BLOCK = 1024


def cross_product(first, second):
    return jnp.stack(
        [
            first[1] * second[2] - first[2] * second[1],
            first[2] * second[0] - first[0] * second[2],
            first[0] * second[1] - first[1] * second[0],
        ]
    )


def contact_rows(frame):
    normal = frame[0:3]
    lever_first = cross_product(frame[3:6], normal)
    lever_second = cross_product(frame[6:9], normal)
    return (jnp.concatenate([-normal, -lever_first]), jnp.concatenate([normal, lever_second]))


def pair_block(target_pos, target_ids, source_pos, source_ids, forces):
    delta_x = target_pos[0][None, :] - source_pos[0][:, None]
    delta_y = target_pos[1][None, :] - source_pos[1][:, None]
    delta_z = target_pos[2][None, :] - source_pos[2][:, None]
    coincide = target_ids[None, :] == source_ids[:, None]
    dist_sq = jnp.where(coincide, 1.0, delta_x * delta_x + delta_y * delta_y + delta_z * delta_z)
    inverse = jnp.where(coincide, 0.0, lax.rsqrt(dist_sq))
    self_term = jnp.where(coincide, 1.0, 0.0)
    unit_x = delta_x * inverse
    unit_y = delta_y * inverse
    unit_z = delta_z * inverse
    force_x, force_y, force_z = (forces[0][:, None], forces[1][:, None], forces[2][:, None])
    torque_x, torque_y, torque_z = (forces[3][:, None], forces[4][:, None], forces[5][:, None])
    inverse_sq = inverse * inverse
    c_one = 0.75 * inverse
    c_two = 0.75 * inverse_sq
    c_three = 0.375 * inverse_sq * inverse
    along_force = unit_x * force_x + unit_y * force_y + unit_z * force_z
    along_torque = unit_x * torque_x + unit_y * torque_y + unit_z * torque_z
    isotropic = c_one * (1.0 + inverse_sq * (2.0 / 3.0)) + self_term
    dyadic = c_one * (1.0 - 2.0 * inverse_sq) * along_force
    vel_x = isotropic * force_x + dyadic * unit_x + c_two * (torque_y * unit_z - torque_z * unit_y)
    vel_y = isotropic * force_y + dyadic * unit_y + c_two * (torque_z * unit_x - torque_x * unit_z)
    vel_z = isotropic * force_z + dyadic * unit_z + c_two * (torque_x * unit_y - torque_y * unit_x)
    spin_self = 0.75 * self_term - c_three
    spin_x = (
        c_two * (force_y * unit_z - force_z * unit_y)
        + c_three * 3.0 * unit_x * along_torque
        + spin_self * torque_x
    )
    spin_y = (
        c_two * (force_z * unit_x - force_x * unit_z)
        + c_three * 3.0 * unit_y * along_torque
        + spin_self * torque_y
    )
    spin_z = (
        c_two * (force_x * unit_y - force_y * unit_x)
        + c_three * 3.0 * unit_z * along_torque
        + spin_self * torque_z
    )
    return jnp.stack(
        [
            jnp.sum(vel_x, 0),
            jnp.sum(vel_y, 0),
            jnp.sum(vel_z, 0),
            jnp.sum(spin_x, 0),
            jnp.sum(spin_y, 0),
            jnp.sum(spin_z, 0),
        ]
    )


def gather_all(block, devices):
    rows, width = block.shape
    spread = jnp.broadcast_to(block[None], (devices, rows, width))
    spread = lax.all_to_all(spread, AXES, 0, 0, tiled=True)
    return spread.transpose(1, 0, 2).reshape(rows, devices * width)


def scatter_sum(full, devices):
    rows, length = full.shape
    width = length // devices
    pieces = full.reshape(rows, devices, width).transpose(1, 0, 2)
    pieces = lax.all_to_all(pieces, AXES, 0, 0, tiled=True)
    return jnp.sum(pieces, 0)


def per_device(
    positions, contact_bodies, contact_frame, gaps, impulse_now, impulse_prev, step_sizes
):
    devices = lax.axis_size("src") * lax.axis_size("tgt")
    me = lax.axis_index("src") * lax.axis_size("tgt") + lax.axis_index("tgt")
    own_rows = positions.shape[1]
    body_count = own_rows * devices
    all_pos = gather_all(positions, devices)
    target_ids = me * own_rows + jnp.arange(own_rows, dtype=jnp.int32)
    first_rows, second_rows = contact_rows(contact_frame)
    current = impulse_now
    shifted = impulse_now + MOMENTUM * (impulse_now - impulse_prev)
    own_velocity = jnp.zeros((6, own_rows), jnp.float32)
    block = min(SOURCE_BLOCK, body_count)
    blocks = body_count // block
    for k in range(ITERS):
        forces = jnp.zeros((6, body_count), jnp.float32)
        forces = forces.at[:, contact_bodies[0]].add(first_rows * shifted[None, :])
        forces = forces.at[:, contact_bodies[1]].add(second_rows * shifted[None, :])
        own_forces = scatter_sum(forces, devices)
        all_forces = gather_all(own_forces, devices)

        def one_block(block_index, running_sum):
            start = block_index * block
            force_block = lax.dynamic_slice_in_dim(all_forces, start, block, 1)
            place_block = lax.dynamic_slice_in_dim(all_pos, start, block, 1)
            ids_block = start + jnp.arange(block, dtype=jnp.int32)
            return running_sum + pair_block(
                positions, target_ids, place_block, ids_block, force_block
            )

        own_velocity = lax.fori_loop(
            0, blocks, one_block, jnp.zeros((6, own_rows), jnp.float32)
        )
        gathered = gather_all(own_velocity, devices)
        normal_rate = jnp.sum(first_rows * gathered[:, contact_bodies[0]], 0) + jnp.sum(
            second_rows * gathered[:, contact_bodies[1]], 0
        )
        updated = jnp.maximum(shifted - step_sizes[k] * (gaps + normal_rate), 0.0)
        shifted = updated + MOMENTUM * (updated - current)
        current = updated
    return (current, own_velocity)


def solution(mesh):
    placed = (
        P(None, AXES),
        P(None, AXES),
        P(None, AXES),
        P(AXES),
        P(AXES),
        P(AXES),
        P(),
    )
    return jax.shard_map(
        per_device,
        mesh=mesh,
        in_specs=placed,
        out_specs=(P(AXES), P(None, AXES)),
        check_vma=False,
    )
```

```python
import jax
import jax.numpy as jnp
from jax import lax
from jax.sharding import PartitionSpec as P

ITERS = 2
MOMENTUM = 0.4
AXES = ("src", "tgt")
SOURCE_BLOCK = 1024


def cross_product(first, second):
    return jnp.stack(
        [
            first[1] * second[2] - first[2] * second[1],
            first[2] * second[0] - first[0] * second[2],
            first[0] * second[1] - first[1] * second[0],
        ]
    )


def contact_rows(frame):
    normal = frame[0:3]
    lever_first = cross_product(frame[3:6], normal)
    lever_second = cross_product(frame[6:9], normal)
    return (jnp.concatenate([-normal, -lever_first]), jnp.concatenate([normal, lever_second]))


def pair_block(target_pos, target_ids, source_pos, source_ids, forces):
    delta_x = target_pos[0][None, :] - source_pos[0][:, None]
    delta_y = target_pos[1][None, :] - source_pos[1][:, None]
    delta_z = target_pos[2][None, :] - source_pos[2][:, None]
    coincide = target_ids[None, :] == source_ids[:, None]
    dist_sq = jnp.where(coincide, 1.0, delta_x * delta_x + delta_y * delta_y + delta_z * delta_z)
    inverse = jnp.where(coincide, 0.0, lax.rsqrt(dist_sq))
    self_term = jnp.where(coincide, 1.0, 0.0)
    unit_x = delta_x * inverse
    unit_y = delta_y * inverse
    unit_z = delta_z * inverse
    force_x, force_y, force_z = (forces[0][:, None], forces[1][:, None], forces[2][:, None])
    torque_x, torque_y, torque_z = (forces[3][:, None], forces[4][:, None], forces[5][:, None])
    inverse_sq = inverse * inverse
    c_one = 0.75 * inverse
    c_two = 0.75 * inverse_sq
    c_three = 0.375 * inverse_sq * inverse
    along_force = unit_x * force_x + unit_y * force_y + unit_z * force_z
    along_torque = unit_x * torque_x + unit_y * torque_y + unit_z * torque_z
    isotropic = c_one * (1.0 + inverse_sq * (2.0 / 3.0)) + self_term
    dyadic = c_one * (1.0 - 2.0 * inverse_sq) * along_force
    vel_x = isotropic * force_x + dyadic * unit_x + c_two * (torque_y * unit_z - torque_z * unit_y)
    vel_y = isotropic * force_y + dyadic * unit_y + c_two * (torque_z * unit_x - torque_x * unit_z)
    vel_z = isotropic * force_z + dyadic * unit_z + c_two * (torque_x * unit_y - torque_y * unit_x)
    spin_self = 0.75 * self_term - c_three
    spin_x = (
        c_two * (force_y * unit_z - force_z * unit_y)
        + c_three * 3.0 * unit_x * along_torque
        + spin_self * torque_x
    )
    spin_y = (
        c_two * (force_z * unit_x - force_x * unit_z)
        + c_three * 3.0 * unit_y * along_torque
        + spin_self * torque_y
    )
    spin_z = (
        c_two * (force_x * unit_y - force_y * unit_x)
        + c_three * 3.0 * unit_z * along_torque
        + spin_self * torque_z
    )
    return jnp.stack(
        [
            jnp.sum(vel_x, 0),
            jnp.sum(vel_y, 0),
            jnp.sum(vel_z, 0),
            jnp.sum(spin_x, 0),
            jnp.sum(spin_y, 0),
            jnp.sum(spin_z, 0),
        ]
    )


def gather_all(block, devices):
    rows, width = block.shape
    spread = jnp.broadcast_to(block[None], (devices, rows, width))
    spread = lax.all_to_all(spread, AXES, 0, 0, tiled=True)
    return spread.transpose(1, 0, 2).reshape(rows, devices * width)


def scatter_sum(full, devices):
    rows, length = full.shape
    width = length // devices
    pieces = full.reshape(rows, devices, width).transpose(1, 0, 2)
    pieces = lax.all_to_all(pieces, AXES, 0, 0, tiled=True)
    return jnp.sum(pieces, 0)


def per_device(
    positions, contact_bodies, contact_frame, gaps, impulse_now, impulse_prev, step_sizes
):
    devices = lax.axis_size("src") * lax.axis_size("tgt")
    me = lax.axis_index("src") * lax.axis_size("tgt") + lax.axis_index("tgt")
    own_rows = positions.shape[1]
    body_count = own_rows * devices
    all_pos = gather_all(positions, devices)
    target_ids = me * own_rows + jnp.arange(own_rows, dtype=jnp.int32)
    first_rows, second_rows = contact_rows(contact_frame)
    contacts = contact_bodies.shape[1]
    end_bodies = jnp.concatenate([contact_bodies[0], contact_bodies[1]])
    end_rows = jnp.concatenate([first_rows, second_rows], axis=1).T
    owner_hot = (
        (end_bodies // own_rows)[:, None] == jnp.arange(devices, dtype=jnp.int32)[None, :]
    ).astype(jnp.float32)
    slot_hot = (
        (end_bodies % own_rows)[:, None] == jnp.arange(own_rows, dtype=jnp.int32)[None, :]
    ).astype(jnp.float32)
    exact = lax.Precision.HIGHEST
    current = impulse_now
    shifted = impulse_now + MOMENTUM * (impulse_now - impulse_prev)
    own_velocity = jnp.zeros((6, own_rows), jnp.float32)
    block = min(SOURCE_BLOCK, body_count)
    blocks = body_count // block
    for k in range(ITERS):
        end_force = end_rows * jnp.concatenate([shifted, shifted])[:, None]
        spread = (owner_hot[:, :, None] * end_force[:, None, :]).reshape(2 * contacts, devices * 6)
        pieces = jnp.dot(spread.T, slot_hot, precision=exact).reshape(devices, 6, own_rows)
        pieces = lax.all_to_all(pieces, AXES, 0, 0, tiled=True)
        own_forces = jnp.sum(pieces, 0)
        all_forces = gather_all(own_forces, devices)

        def one_block(block_index, running_sum):
            start = block_index * block
            force_block = lax.dynamic_slice_in_dim(all_forces, start, block, 1)
            place_block = lax.dynamic_slice_in_dim(all_pos, start, block, 1)
            ids_block = start + jnp.arange(block, dtype=jnp.int32)
            return running_sum + pair_block(
                positions, target_ids, place_block, ids_block, force_block
            )

        own_velocity = lax.fori_loop(
            0, blocks, one_block, jnp.zeros((6, own_rows), jnp.float32)
        )
        every = jnp.broadcast_to(own_velocity[None], (devices, 6, own_rows))
        every = lax.all_to_all(every, AXES, 0, 0, tiled=True).reshape(devices, 6 * own_rows)
        picked = jnp.dot(owner_hot, every, precision=exact).reshape(2 * contacts, 6, own_rows)
        end_velocity = jnp.sum(picked * slot_hot[:, None, :], 2)
        end_rate = jnp.sum(end_rows * end_velocity, 1)
        normal_rate = end_rate[:contacts] + end_rate[contacts:]
        updated = jnp.maximum(shifted - step_sizes[k] * (gaps + normal_rate), 0.0)
        shifted = updated + MOMENTUM * (updated - current)
        current = updated
    return (current, own_velocity)


def solution(mesh):
    placed = (
        P(None, AXES),
        P(None, AXES),
        P(None, AXES),
        P(AXES),
        P(AXES),
        P(AXES),
        P(),
    )
    return jax.shard_map(
        per_device,
        mesh=mesh,
        in_specs=placed,
        out_specs=(P(AXES), P(None, AXES)),
        check_vma=False,
    )
```

```python
import jax
import jax.numpy as jnp
from jax import lax
from jax.experimental import pallas as pl
from jax.sharding import PartitionSpec as P

ITERS = 2
MOMENTUM = 0.4
AXES = ("src", "tgt")
SOURCE_BLOCK = 1024


def cross_product(first, second):
    return jnp.stack(
        [
            first[1] * second[2] - first[2] * second[1],
            first[2] * second[0] - first[0] * second[2],
            first[0] * second[1] - first[1] * second[0],
        ]
    )


def contact_rows(frame):
    normal = frame[0:3]
    lever_first = cross_product(frame[3:6], normal)
    lever_second = cross_product(frame[6:9], normal)
    return (jnp.concatenate([-normal, -lever_first]), jnp.concatenate([normal, lever_second]))


def pair_block(target_pos, target_ids, source_pos, source_ids, forces):
    delta_x = target_pos[0][None, :] - source_pos[0][:, None]
    delta_y = target_pos[1][None, :] - source_pos[1][:, None]
    delta_z = target_pos[2][None, :] - source_pos[2][:, None]
    coincide = target_ids[None, :] == source_ids[:, None]
    dist_sq = jnp.where(coincide, 1.0, delta_x * delta_x + delta_y * delta_y + delta_z * delta_z)
    inverse = jnp.where(coincide, 0.0, lax.rsqrt(dist_sq))
    self_term = jnp.where(coincide, 1.0, 0.0)
    unit_x = delta_x * inverse
    unit_y = delta_y * inverse
    unit_z = delta_z * inverse
    force_x, force_y, force_z = (forces[0][:, None], forces[1][:, None], forces[2][:, None])
    torque_x, torque_y, torque_z = (forces[3][:, None], forces[4][:, None], forces[5][:, None])
    inverse_sq = inverse * inverse
    c_one = 0.75 * inverse
    c_two = 0.75 * inverse_sq
    c_three = 0.375 * inverse_sq * inverse
    along_force = unit_x * force_x + unit_y * force_y + unit_z * force_z
    along_torque = unit_x * torque_x + unit_y * torque_y + unit_z * torque_z
    isotropic = c_one * (1.0 + inverse_sq * (2.0 / 3.0)) + self_term
    dyadic = c_one * (1.0 - 2.0 * inverse_sq) * along_force
    vel_x = isotropic * force_x + dyadic * unit_x + c_two * (torque_y * unit_z - torque_z * unit_y)
    vel_y = isotropic * force_y + dyadic * unit_y + c_two * (torque_z * unit_x - torque_x * unit_z)
    vel_z = isotropic * force_z + dyadic * unit_z + c_two * (torque_x * unit_y - torque_y * unit_x)
    spin_self = 0.75 * self_term - c_three
    spin_x = (
        c_two * (force_y * unit_z - force_z * unit_y)
        + c_three * 3.0 * unit_x * along_torque
        + spin_self * torque_x
    )
    spin_y = (
        c_two * (force_z * unit_x - force_x * unit_z)
        + c_three * 3.0 * unit_y * along_torque
        + spin_self * torque_y
    )
    spin_z = (
        c_two * (force_x * unit_y - force_y * unit_x)
        + c_three * 3.0 * unit_z * along_torque
        + spin_self * torque_z
    )
    return jnp.stack(
        [
            jnp.sum(vel_x, 0),
            jnp.sum(vel_y, 0),
            jnp.sum(vel_z, 0),
            jnp.sum(spin_x, 0),
            jnp.sum(spin_y, 0),
            jnp.sum(spin_z, 0),
        ]
    )


def split_three(value):
    high = lax.reduce_precision(value, exponent_bits=8, mantissa_bits=7)
    rest = value - high
    middle = lax.reduce_precision(rest, exponent_bits=8, mantissa_bits=7)
    low = rest - middle
    return jnp.stack([high, middle, low]).astype(jnp.bfloat16)


def scatter_kernel(owner_ref, slot_ref, parts_ref, out_ref):
    slots = slot_ref.shape[0]
    owner = owner_ref[...]
    slot = slot_ref[...]
    for k in range(6):
        total = None
        for p in range(3):
            weighted = slot * parts_ref[p, k : k + 1, :]
            term = lax.dot_general(
                owner, weighted, (((1,), (1,)), ((), ())), preferred_element_type=jnp.float32
            )
            total = term if total is None else total + term
        out_ref[:, k * slots : (k + 1) * slots] = total


def gather_kernel(owner_ref, slot_ref, parts_ref, out_ref):
    slots = slot_ref.shape[0]
    owner = owner_ref[...]
    slot = slot_ref[...].astype(jnp.float32)
    for k in range(6):
        picked = None
        for p in range(3):
            part = parts_ref[p, k * slots : (k + 1) * slots, :]
            term = jnp.dot(part, owner, preferred_element_type=jnp.float32)
            picked = term if picked is None else picked + term
        out_ref[k : k + 1, :] = jnp.sum(picked * slot, axis=0, keepdims=True)


def scatter_forces(owner_t, slot_t, end_force):
    owners, ends = owner_t.shape
    slots = slot_t.shape[0]
    parts = split_three(end_force)
    return pl.pallas_call(
        scatter_kernel,
        out_shape=jax.ShapeDtypeStruct((owners, 6 * slots), jnp.float32),
        cost_estimate=pl.CostEstimate(
            flops=2 * 18 * owners * slots * ends, transcendentals=0, bytes_accessed=4 * ends * 300
        ),
    )(owner_t, slot_t, parts)


def gather_velocity(owner_t, slot_t, table):
    owners, ends = owner_t.shape
    slots = slot_t.shape[0]
    return pl.pallas_call(
        gather_kernel,
        out_shape=jax.ShapeDtypeStruct((6, ends), jnp.float32),
        cost_estimate=pl.CostEstimate(
            flops=2 * 18 * owners * slots * ends, transcendentals=0, bytes_accessed=4 * ends * 300
        ),
    )(owner_t, slot_t, split_three(table))


def gather_all(block, devices):
    rows, width = block.shape
    spread = jnp.broadcast_to(block[None], (devices, rows, width))
    spread = lax.all_to_all(spread, AXES, 0, 0, tiled=True)
    return spread.transpose(1, 0, 2).reshape(rows, devices * width)


def scatter_sum(full, devices):
    rows, length = full.shape
    width = length // devices
    pieces = full.reshape(rows, devices, width).transpose(1, 0, 2)
    pieces = lax.all_to_all(pieces, AXES, 0, 0, tiled=True)
    return jnp.sum(pieces, 0)


def per_device(
    positions, contact_bodies, contact_frame, gaps, impulse_now, impulse_prev, step_sizes
):
    devices = lax.axis_size("src") * lax.axis_size("tgt")
    me = lax.axis_index("src") * lax.axis_size("tgt") + lax.axis_index("tgt")
    own_rows = positions.shape[1]
    body_count = own_rows * devices
    all_pos = gather_all(positions, devices)
    target_ids = me * own_rows + jnp.arange(own_rows, dtype=jnp.int32)
    first_rows, second_rows = contact_rows(contact_frame)
    contacts = contact_bodies.shape[1]
    end_bodies = jnp.concatenate([contact_bodies[0], contact_bodies[1]])
    end_rows = jnp.concatenate([first_rows, second_rows], axis=1)
    owner_t = (
        jnp.arange(devices, dtype=jnp.int32)[:, None] == (end_bodies // own_rows)[None, :]
    ).astype(jnp.bfloat16)
    slot_t = (
        jnp.arange(own_rows, dtype=jnp.int32)[:, None] == (end_bodies % own_rows)[None, :]
    ).astype(jnp.bfloat16)
    current = impulse_now
    shifted = impulse_now + MOMENTUM * (impulse_now - impulse_prev)
    own_velocity = jnp.zeros((6, own_rows), jnp.float32)
    block = min(SOURCE_BLOCK, body_count)
    blocks = body_count // block
    for k in range(ITERS):
        end_force = end_rows * jnp.concatenate([shifted, shifted])[None, :]
        pieces = scatter_forces(owner_t, slot_t, end_force)
        pieces = lax.all_to_all(pieces, AXES, 0, 0, tiled=True)
        own_forces = jnp.sum(pieces, 0).reshape(6, own_rows)
        all_forces = gather_all(own_forces, devices)

        def one_block(block_index, running_sum):
            start = block_index * block
            force_block = lax.dynamic_slice_in_dim(all_forces, start, block, 1)
            place_block = lax.dynamic_slice_in_dim(all_pos, start, block, 1)
            ids_block = start + jnp.arange(block, dtype=jnp.int32)
            return running_sum + pair_block(
                positions, target_ids, place_block, ids_block, force_block
            )

        own_velocity = lax.fori_loop(
            0, blocks, one_block, jnp.zeros((6, own_rows), jnp.float32)
        )
        every = jnp.broadcast_to(own_velocity.reshape(1, 6 * own_rows), (devices, 6 * own_rows))
        every = lax.all_to_all(every, AXES, 0, 0, tiled=True)
        end_velocity = gather_velocity(owner_t, slot_t, every.T)
        end_rate = jnp.sum(end_rows * end_velocity, 0)
        normal_rate = end_rate[:contacts] + end_rate[contacts:]
        updated = jnp.maximum(shifted - step_sizes[k] * (gaps + normal_rate), 0.0)
        shifted = updated + MOMENTUM * (updated - current)
        current = updated
    return (current, own_velocity)


def solution(mesh):
    placed = (
        P(None, AXES),
        P(None, AXES),
        P(None, AXES),
        P(AXES),
        P(AXES),
        P(AXES),
        P(),
    )
    return jax.shard_map(
        per_device,
        mesh=mesh,
        in_specs=placed,
        out_specs=(P(AXES), P(None, AXES)),
        check_vma=False,
    )
```

```python
import jax
import jax.numpy as jnp
from jax import lax
from jax.experimental import pallas as pl
from jax.sharding import PartitionSpec as P

ITERS = 2
MOMENTUM = 0.4
AXES = ("src", "tgt")
SOURCE_BLOCK = 1024


def cross_product(first, second):
    return jnp.stack(
        [
            first[1] * second[2] - first[2] * second[1],
            first[2] * second[0] - first[0] * second[2],
            first[0] * second[1] - first[1] * second[0],
        ]
    )


def contact_rows(frame):
    normal = frame[0:3]
    lever_first = cross_product(frame[3:6], normal)
    lever_second = cross_product(frame[6:9], normal)
    return (jnp.concatenate([-normal, -lever_first]), jnp.concatenate([normal, lever_second]))


def pair_block(target_pos, target_ids, source_pos, source_ids, forces):
    delta_x = target_pos[0][None, :] - source_pos[0][:, None]
    delta_y = target_pos[1][None, :] - source_pos[1][:, None]
    delta_z = target_pos[2][None, :] - source_pos[2][:, None]
    coincide = target_ids[None, :] == source_ids[:, None]
    dist_sq = jnp.where(coincide, 1.0, delta_x * delta_x + delta_y * delta_y + delta_z * delta_z)
    inverse = jnp.where(coincide, 0.0, lax.rsqrt(dist_sq))
    self_term = jnp.where(coincide, 1.0, 0.0)
    unit_x = delta_x * inverse
    unit_y = delta_y * inverse
    unit_z = delta_z * inverse
    force_x, force_y, force_z = (forces[0][:, None], forces[1][:, None], forces[2][:, None])
    torque_x, torque_y, torque_z = (forces[3][:, None], forces[4][:, None], forces[5][:, None])
    inverse_sq = inverse * inverse
    c_one = 0.75 * inverse
    c_two = 0.75 * inverse_sq
    c_three = 0.375 * inverse_sq * inverse
    along_force = unit_x * force_x + unit_y * force_y + unit_z * force_z
    along_torque = unit_x * torque_x + unit_y * torque_y + unit_z * torque_z
    isotropic = c_one * (1.0 + inverse_sq * (2.0 / 3.0)) + self_term
    dyadic = c_one * (1.0 - 2.0 * inverse_sq) * along_force
    vel_x = isotropic * force_x + dyadic * unit_x + c_two * (torque_y * unit_z - torque_z * unit_y)
    vel_y = isotropic * force_y + dyadic * unit_y + c_two * (torque_z * unit_x - torque_x * unit_z)
    vel_z = isotropic * force_z + dyadic * unit_z + c_two * (torque_x * unit_y - torque_y * unit_x)
    spin_self = 0.75 * self_term - c_three
    spin_x = (
        c_two * (force_y * unit_z - force_z * unit_y)
        + c_three * 3.0 * unit_x * along_torque
        + spin_self * torque_x
    )
    spin_y = (
        c_two * (force_z * unit_x - force_x * unit_z)
        + c_three * 3.0 * unit_y * along_torque
        + spin_self * torque_y
    )
    spin_z = (
        c_two * (force_x * unit_y - force_y * unit_x)
        + c_three * 3.0 * unit_z * along_torque
        + spin_self * torque_z
    )
    return jnp.stack(
        [
            jnp.sum(vel_x, 0),
            jnp.sum(vel_y, 0),
            jnp.sum(vel_z, 0),
            jnp.sum(spin_x, 0),
            jnp.sum(spin_y, 0),
            jnp.sum(spin_z, 0),
        ]
    )


def split_three(value):
    high = lax.reduce_precision(value, exponent_bits=8, mantissa_bits=7)
    rest = value - high
    middle = lax.reduce_precision(rest, exponent_bits=8, mantissa_bits=7)
    low = rest - middle
    return jnp.stack([high, middle, low]).astype(jnp.bfloat16)


def scatter_kernel(owner_ref, slot_ref, parts_ref, out_ref):
    slots = slot_ref.shape[0]
    owner = owner_ref[...]
    slot = slot_ref[...]
    for k in range(6):
        total = None
        for p in range(3):
            weighted = slot * parts_ref[p, k : k + 1, :]
            term = lax.dot_general(
                owner, weighted, (((1,), (1,)), ((), ())), preferred_element_type=jnp.float32
            )
            total = term if total is None else total + term
        out_ref[:, k * slots : (k + 1) * slots] = total


def gather_kernel(owner_ref, slot_ref, parts_ref, out_ref):
    slots = slot_ref.shape[0]
    owner = owner_ref[...]
    slot = slot_ref[...].astype(jnp.float32)
    for k in range(6):
        picked = None
        for p in range(3):
            part = parts_ref[p, k * slots : (k + 1) * slots, :]
            term = jnp.dot(part, owner, preferred_element_type=jnp.float32)
            picked = term if picked is None else picked + term
        out_ref[k : k + 1, :] = jnp.sum(picked * slot, axis=0, keepdims=True)


def scatter_forces(owner_t, slot_t, end_force):
    owners, ends = owner_t.shape
    slots = slot_t.shape[0]
    parts = split_three(end_force)
    return pl.pallas_call(
        scatter_kernel,
        out_shape=jax.ShapeDtypeStruct((owners, 6 * slots), jnp.float32),
        cost_estimate=pl.CostEstimate(
            flops=2 * 18 * owners * slots * ends, transcendentals=0, bytes_accessed=4 * ends * 300
        ),
    )(owner_t, slot_t, parts)


def gather_velocity(owner_t, slot_t, table):
    owners, ends = owner_t.shape
    slots = slot_t.shape[0]
    return pl.pallas_call(
        gather_kernel,
        out_shape=jax.ShapeDtypeStruct((6, ends), jnp.float32),
        cost_estimate=pl.CostEstimate(
            flops=2 * 18 * owners * slots * ends, transcendentals=0, bytes_accessed=4 * ends * 300
        ),
    )(owner_t, slot_t, split_three(table))


def gather_all(block, devices):
    rows, width = block.shape
    spread = jnp.broadcast_to(block[None], (devices, rows, width))
    spread = lax.all_to_all(spread, AXES, 0, 0, tiled=True)
    return spread.transpose(1, 0, 2).reshape(rows, devices * width)


def scatter_sum(full, devices):
    rows, length = full.shape
    width = length // devices
    pieces = full.reshape(rows, devices, width).transpose(1, 0, 2)
    pieces = lax.all_to_all(pieces, AXES, 0, 0, tiled=True)
    return jnp.sum(pieces, 0)


def per_device(
    positions, contact_bodies, contact_frame, gaps, impulse_now, impulse_prev, step_sizes
):
    devices = lax.axis_size("src") * lax.axis_size("tgt")
    me = lax.axis_index("src") * lax.axis_size("tgt") + lax.axis_index("tgt")
    own_rows = positions.shape[1]
    body_count = own_rows * devices
    target_ids = me * own_rows + jnp.arange(own_rows, dtype=jnp.int32)
    first_rows, second_rows = contact_rows(contact_frame)
    contacts = contact_bodies.shape[1]
    end_bodies = jnp.concatenate([contact_bodies[0], contact_bodies[1]])
    end_rows = jnp.concatenate([first_rows, second_rows], axis=1)
    owner_t = (
        jnp.arange(devices, dtype=jnp.int32)[:, None] == (end_bodies // own_rows)[None, :]
    ).astype(jnp.bfloat16)
    slot_t = (
        jnp.arange(own_rows, dtype=jnp.int32)[:, None] == (end_bodies % own_rows)[None, :]
    ).astype(jnp.bfloat16)
    current = impulse_now
    shifted = impulse_now + MOMENTUM * (impulse_now - impulse_prev)
    own_velocity = jnp.zeros((6, own_rows), jnp.float32)
    block = min(SOURCE_BLOCK, body_count)
    blocks = body_count // block
    for k in range(ITERS):
        end_force = end_rows * jnp.concatenate([shifted, shifted])[None, :]
        pieces = scatter_forces(owner_t, slot_t, end_force)
        pieces = lax.all_to_all(pieces, AXES, 0, 0, tiled=True)
        own_forces = jnp.sum(pieces, 0).reshape(6, own_rows)
        if k == 0:
            both = gather_all(jnp.concatenate([own_forces, positions]), devices)
            all_forces, all_pos = both[:6], both[6:]
        else:
            all_forces = gather_all(own_forces, devices)

        def one_block(block_index, running_sum):
            start = block_index * block
            force_block = lax.dynamic_slice_in_dim(all_forces, start, block, 1)
            place_block = lax.dynamic_slice_in_dim(all_pos, start, block, 1)
            ids_block = start + jnp.arange(block, dtype=jnp.int32)
            return running_sum + pair_block(
                positions, target_ids, place_block, ids_block, force_block
            )

        own_velocity = lax.fori_loop(
            0, blocks, one_block, jnp.zeros((6, own_rows), jnp.float32)
        )
        every = jnp.broadcast_to(own_velocity.reshape(1, 6 * own_rows), (devices, 6 * own_rows))
        every = lax.all_to_all(every, AXES, 0, 0, tiled=True)
        end_velocity = gather_velocity(owner_t, slot_t, every.T)
        end_rate = jnp.sum(end_rows * end_velocity, 0)
        normal_rate = end_rate[:contacts] + end_rate[contacts:]
        updated = jnp.maximum(shifted - step_sizes[k] * (gaps + normal_rate), 0.0)
        shifted = updated + MOMENTUM * (updated - current)
        current = updated
    return (current, own_velocity)


def solution(mesh):
    placed = (
        P(None, AXES),
        P(None, AXES),
        P(None, AXES),
        P(AXES),
        P(AXES),
        P(AXES),
        P(),
    )
    return jax.shard_map(
        per_device,
        mesh=mesh,
        in_specs=placed,
        out_specs=(P(AXES), P(None, AXES)),
        check_vma=False,
    )
```

```python
import jax
import jax.numpy as jnp
from jax import lax
from jax.experimental import pallas as pl
from jax.sharding import PartitionSpec as P

ITERS = 2
MOMENTUM = 0.4
AXES = ("src", "tgt")
SOURCE_BLOCK = 1024


def cross_product(first, second):
    return jnp.stack(
        [
            first[1] * second[2] - first[2] * second[1],
            first[2] * second[0] - first[0] * second[2],
            first[0] * second[1] - first[1] * second[0],
        ]
    )


def contact_rows(frame):
    normal = frame[0:3]
    lever_first = cross_product(frame[3:6], normal)
    lever_second = cross_product(frame[6:9], normal)
    return (jnp.concatenate([-normal, -lever_first]), jnp.concatenate([normal, lever_second]))


def pair_block(target_pos, target_ids, source_pos, source_ids, forces):
    delta_x = target_pos[0][None, :] - source_pos[0][:, None]
    delta_y = target_pos[1][None, :] - source_pos[1][:, None]
    delta_z = target_pos[2][None, :] - source_pos[2][:, None]
    coincide = target_ids[None, :] == source_ids[:, None]
    dist_sq = jnp.where(coincide, 1.0, delta_x * delta_x + delta_y * delta_y + delta_z * delta_z)
    inverse = jnp.where(coincide, 0.0, lax.rsqrt(dist_sq))
    self_term = jnp.where(coincide, 1.0, 0.0)
    unit_x = delta_x * inverse
    unit_y = delta_y * inverse
    unit_z = delta_z * inverse
    force_x, force_y, force_z = (forces[0][:, None], forces[1][:, None], forces[2][:, None])
    torque_x, torque_y, torque_z = (forces[3][:, None], forces[4][:, None], forces[5][:, None])
    inverse_sq = inverse * inverse
    c_one = 0.75 * inverse
    c_two = 0.75 * inverse_sq
    c_three = 0.375 * inverse_sq * inverse
    along_force = unit_x * force_x + unit_y * force_y + unit_z * force_z
    along_torque = unit_x * torque_x + unit_y * torque_y + unit_z * torque_z
    isotropic = c_one * (1.0 + inverse_sq * (2.0 / 3.0)) + self_term
    dyadic = c_one * (1.0 - 2.0 * inverse_sq) * along_force
    vel_x = isotropic * force_x + dyadic * unit_x + c_two * (torque_y * unit_z - torque_z * unit_y)
    vel_y = isotropic * force_y + dyadic * unit_y + c_two * (torque_z * unit_x - torque_x * unit_z)
    vel_z = isotropic * force_z + dyadic * unit_z + c_two * (torque_x * unit_y - torque_y * unit_x)
    spin_self = 0.75 * self_term - c_three
    spin_x = (
        c_two * (force_y * unit_z - force_z * unit_y)
        + c_three * 3.0 * unit_x * along_torque
        + spin_self * torque_x
    )
    spin_y = (
        c_two * (force_z * unit_x - force_x * unit_z)
        + c_three * 3.0 * unit_y * along_torque
        + spin_self * torque_y
    )
    spin_z = (
        c_two * (force_x * unit_y - force_y * unit_x)
        + c_three * 3.0 * unit_z * along_torque
        + spin_self * torque_z
    )
    return jnp.stack(
        [
            jnp.sum(vel_x, 0),
            jnp.sum(vel_y, 0),
            jnp.sum(vel_z, 0),
            jnp.sum(spin_x, 0),
            jnp.sum(spin_y, 0),
            jnp.sum(spin_z, 0),
        ]
    )


def split_three(value):
    high = lax.reduce_precision(value, exponent_bits=8, mantissa_bits=7)
    rest = value - high
    middle = lax.reduce_precision(rest, exponent_bits=8, mantissa_bits=7)
    low = rest - middle
    return jnp.stack([high, middle, low]).astype(jnp.bfloat16)


def scatter_kernel(owner_ref, slot_ref, parts_ref, out_ref):
    slots = slot_ref.shape[0]
    owner = owner_ref[...]
    slot = slot_ref[...]
    for k in range(6):
        total = None
        for p in range(3):
            weighted = slot * parts_ref[p, k : k + 1, :]
            term = lax.dot_general(
                owner, weighted, (((1,), (1,)), ((), ())), preferred_element_type=jnp.float32
            )
            total = term if total is None else total + term
        out_ref[:, k * slots : (k + 1) * slots] = total


def gather_kernel(owner_ref, slot_ref, parts_ref, out_ref):
    slots = slot_ref.shape[0]
    owner = owner_ref[...]
    slot = slot_ref[...].astype(jnp.float32)
    for k in range(6):
        picked = None
        for p in range(3):
            part = parts_ref[p, k * slots : (k + 1) * slots, :]
            term = jnp.dot(part, owner, preferred_element_type=jnp.float32)
            picked = term if picked is None else picked + term
        out_ref[k : k + 1, :] = jnp.sum(picked * slot, axis=0, keepdims=True)


def scatter_forces(owner_t, slot_t, end_force):
    owners, ends = owner_t.shape
    slots = slot_t.shape[0]
    parts = split_three(end_force)
    return pl.pallas_call(
        scatter_kernel,
        out_shape=jax.ShapeDtypeStruct((owners, 6 * slots), jnp.float32),
        cost_estimate=pl.CostEstimate(
            flops=2 * 18 * owners * slots * ends, transcendentals=0, bytes_accessed=4 * ends * 300
        ),
    )(owner_t, slot_t, parts)


def gather_velocity(owner_t, slot_t, table):
    owners, ends = owner_t.shape
    slots = slot_t.shape[0]
    return pl.pallas_call(
        gather_kernel,
        out_shape=jax.ShapeDtypeStruct((6, ends), jnp.float32),
        cost_estimate=pl.CostEstimate(
            flops=2 * 18 * owners * slots * ends, transcendentals=0, bytes_accessed=4 * ends * 300
        ),
    )(owner_t, slot_t, split_three(table))


def pair_kernel(target_ref, place_ref, force_ref, out_ref):
    targets = target_ref.shape[1]
    chunks = place_ref.shape[1] // 128

    def group(g, carry):
        rows = pl.ds(pl.multiple_of(g * 8, 8), 8)
        target_x = target_ref[0, rows, :]
        target_y = target_ref[1, rows, :]
        target_z = target_ref[2, rows, :]

        def chunk(j, sums):
            lanes = pl.ds(pl.multiple_of(j * 128, 128), 128)
            place = place_ref[:, lanes]
            force = force_ref[:, lanes]
            r_x = target_x - place[0:1]
            r_y = target_y - place[1:2]
            r_z = target_z - place[2:3]
            f_x, f_y, f_z = force[0:1], force[1:2], force[2:3]
            t_x, t_y, t_z = force[3:4], force[4:5], force[5:6]
            dist_sq = r_x * r_x + r_y * r_y + r_z * r_z
            inverse = jnp.where(dist_sq > 0.0, lax.rsqrt(dist_sq), 0.0)
            inverse_sq = inverse * inverse
            inverse_cube = inverse_sq * inverse
            inverse_fifth = inverse_cube * inverse_sq
            c_cross = 0.75 * inverse_cube
            c_iso = 0.75 * inverse + 0.5 * inverse_cube
            c_dyad = c_cross - 1.5 * inverse_fifth
            c_spin = 1.125 * inverse_fifth
            c_self = 0.375 * inverse_cube
            dyad = c_dyad * (r_x * f_x + r_y * f_y + r_z * f_z)
            spin = c_spin * (r_x * t_x + r_y * t_y + r_z * t_z)
            s_x = c_cross * r_x
            s_y = c_cross * r_y
            s_z = c_cross * r_z
            return (
                sums[0] + (c_iso * f_x + dyad * r_x + (t_y * s_z - t_z * s_y)),
                sums[1] + (c_iso * f_y + dyad * r_y + (t_z * s_x - t_x * s_z)),
                sums[2] + (c_iso * f_z + dyad * r_z + (t_x * s_y - t_y * s_x)),
                sums[3] + ((f_y * s_z - f_z * s_y) + spin * r_x - c_self * t_x),
                sums[4] + ((f_z * s_x - f_x * s_z) + spin * r_y - c_self * t_y),
                sums[5] + ((f_x * s_y - f_y * s_x) + spin * r_z - c_self * t_z),
            )

        zero = jnp.zeros((8, 128), jnp.float32)
        sums = lax.fori_loop(0, chunks, chunk, (zero,) * 6, unroll=2)
        for k in range(6):
            out_ref[k, rows, :] = sums[k]
        return carry

    lax.fori_loop(0, targets // 8, group, 0)


def mobility_own(positions, all_pos, all_forces, own_forces):
    own_rows = positions.shape[1]
    sources = all_pos.shape[1]
    spread = jnp.broadcast_to(positions[:, :, None], (3, own_rows, 128))
    partial = pl.pallas_call(
        pair_kernel,
        out_shape=jax.ShapeDtypeStruct((6, own_rows, 128), jnp.float32),
        cost_estimate=pl.CostEstimate(
            flops=90 * own_rows * sources,
            transcendentals=own_rows * sources,
            bytes_accessed=4 * (9 * sources + 9 * own_rows * 128),
        ),
    )(spread, all_pos, all_forces)
    self_scale = jnp.array([1.0, 1.0, 1.0, 0.75, 0.75, 0.75], jnp.float32)[:, None]
    return jnp.sum(partial, 2) + self_scale * own_forces


def gather_all(block, devices):
    rows, width = block.shape
    spread = jnp.broadcast_to(block[None], (devices, rows, width))
    spread = lax.all_to_all(spread, AXES, 0, 0, tiled=True)
    return spread.transpose(1, 0, 2).reshape(rows, devices * width)


def scatter_sum(full, devices):
    rows, length = full.shape
    width = length // devices
    pieces = full.reshape(rows, devices, width).transpose(1, 0, 2)
    pieces = lax.all_to_all(pieces, AXES, 0, 0, tiled=True)
    return jnp.sum(pieces, 0)


def per_device(
    positions, contact_bodies, contact_frame, gaps, impulse_now, impulse_prev, step_sizes
):
    devices = lax.axis_size("src") * lax.axis_size("tgt")
    me = lax.axis_index("src") * lax.axis_size("tgt") + lax.axis_index("tgt")
    own_rows = positions.shape[1]
    body_count = own_rows * devices
    first_rows, second_rows = contact_rows(contact_frame)
    contacts = contact_bodies.shape[1]
    end_bodies = jnp.concatenate([contact_bodies[0], contact_bodies[1]])
    end_rows = jnp.concatenate([first_rows, second_rows], axis=1)
    owner_t = (
        jnp.arange(devices, dtype=jnp.int32)[:, None] == (end_bodies // own_rows)[None, :]
    ).astype(jnp.bfloat16)
    slot_t = (
        jnp.arange(own_rows, dtype=jnp.int32)[:, None] == (end_bodies % own_rows)[None, :]
    ).astype(jnp.bfloat16)
    current = impulse_now
    shifted = impulse_now + MOMENTUM * (impulse_now - impulse_prev)
    own_velocity = jnp.zeros((6, own_rows), jnp.float32)
    for k in range(ITERS):
        end_force = end_rows * jnp.concatenate([shifted, shifted])[None, :]
        pieces = scatter_forces(owner_t, slot_t, end_force)
        pieces = lax.all_to_all(pieces, AXES, 0, 0, tiled=True)
        own_forces = jnp.sum(pieces, 0).reshape(6, own_rows)
        if k == 0:
            both = gather_all(jnp.concatenate([own_forces, positions]), devices)
            all_forces, all_pos = both[:6], both[6:]
        else:
            all_forces = gather_all(own_forces, devices)

        own_velocity = mobility_own(positions, all_pos, all_forces, own_forces)
        every = jnp.broadcast_to(own_velocity.reshape(1, 6 * own_rows), (devices, 6 * own_rows))
        every = lax.all_to_all(every, AXES, 0, 0, tiled=True)
        end_velocity = gather_velocity(owner_t, slot_t, every.T)
        end_rate = jnp.sum(end_rows * end_velocity, 0)
        normal_rate = end_rate[:contacts] + end_rate[contacts:]
        updated = jnp.maximum(shifted - step_sizes[k] * (gaps + normal_rate), 0.0)
        shifted = updated + MOMENTUM * (updated - current)
        current = updated
    return (current, own_velocity)


def solution(mesh):
    placed = (
        P(None, AXES),
        P(None, AXES),
        P(None, AXES),
        P(AXES),
        P(AXES),
        P(AXES),
        P(),
    )
    return jax.shard_map(
        per_device,
        mesh=mesh,
        in_specs=placed,
        out_specs=(P(AXES), P(None, AXES)),
        check_vma=False,
    )
```

```python
import jax
import jax.numpy as jnp
from jax import lax
from jax.experimental import pallas as pl
from jax.sharding import PartitionSpec as P

ITERS = 2
MOMENTUM = 0.4
AXES = ("src", "tgt")
SOURCE_BLOCK = 1024


def cross_product(first, second):
    return jnp.stack(
        [
            first[1] * second[2] - first[2] * second[1],
            first[2] * second[0] - first[0] * second[2],
            first[0] * second[1] - first[1] * second[0],
        ]
    )


def contact_rows(frame):
    normal = frame[0:3]
    lever_first = cross_product(frame[3:6], normal)
    lever_second = cross_product(frame[6:9], normal)
    return (jnp.concatenate([-normal, -lever_first]), jnp.concatenate([normal, lever_second]))


def pair_block(target_pos, target_ids, source_pos, source_ids, forces):
    delta_x = target_pos[0][None, :] - source_pos[0][:, None]
    delta_y = target_pos[1][None, :] - source_pos[1][:, None]
    delta_z = target_pos[2][None, :] - source_pos[2][:, None]
    coincide = target_ids[None, :] == source_ids[:, None]
    dist_sq = jnp.where(coincide, 1.0, delta_x * delta_x + delta_y * delta_y + delta_z * delta_z)
    inverse = jnp.where(coincide, 0.0, lax.rsqrt(dist_sq))
    self_term = jnp.where(coincide, 1.0, 0.0)
    unit_x = delta_x * inverse
    unit_y = delta_y * inverse
    unit_z = delta_z * inverse
    force_x, force_y, force_z = (forces[0][:, None], forces[1][:, None], forces[2][:, None])
    torque_x, torque_y, torque_z = (forces[3][:, None], forces[4][:, None], forces[5][:, None])
    inverse_sq = inverse * inverse
    c_one = 0.75 * inverse
    c_two = 0.75 * inverse_sq
    c_three = 0.375 * inverse_sq * inverse
    along_force = unit_x * force_x + unit_y * force_y + unit_z * force_z
    along_torque = unit_x * torque_x + unit_y * torque_y + unit_z * torque_z
    isotropic = c_one * (1.0 + inverse_sq * (2.0 / 3.0)) + self_term
    dyadic = c_one * (1.0 - 2.0 * inverse_sq) * along_force
    vel_x = isotropic * force_x + dyadic * unit_x + c_two * (torque_y * unit_z - torque_z * unit_y)
    vel_y = isotropic * force_y + dyadic * unit_y + c_two * (torque_z * unit_x - torque_x * unit_z)
    vel_z = isotropic * force_z + dyadic * unit_z + c_two * (torque_x * unit_y - torque_y * unit_x)
    spin_self = 0.75 * self_term - c_three
    spin_x = (
        c_two * (force_y * unit_z - force_z * unit_y)
        + c_three * 3.0 * unit_x * along_torque
        + spin_self * torque_x
    )
    spin_y = (
        c_two * (force_z * unit_x - force_x * unit_z)
        + c_three * 3.0 * unit_y * along_torque
        + spin_self * torque_y
    )
    spin_z = (
        c_two * (force_x * unit_y - force_y * unit_x)
        + c_three * 3.0 * unit_z * along_torque
        + spin_self * torque_z
    )
    return jnp.stack(
        [
            jnp.sum(vel_x, 0),
            jnp.sum(vel_y, 0),
            jnp.sum(vel_z, 0),
            jnp.sum(spin_x, 0),
            jnp.sum(spin_y, 0),
            jnp.sum(spin_z, 0),
        ]
    )


def split_three(value):
    high = lax.reduce_precision(value, exponent_bits=8, mantissa_bits=7)
    rest = value - high
    middle = lax.reduce_precision(rest, exponent_bits=8, mantissa_bits=7)
    low = rest - middle
    return jnp.stack([high, middle, low]).astype(jnp.bfloat16)


def scatter_kernel(owner_ref, slot_ref, parts_ref, out_ref):
    slots = slot_ref.shape[0]
    owner = owner_ref[...]
    slot = slot_ref[...]
    for k in range(6):
        total = None
        for p in range(3):
            weighted = slot * parts_ref[p, k : k + 1, :]
            term = lax.dot_general(
                owner, weighted, (((1,), (1,)), ((), ())), preferred_element_type=jnp.float32
            )
            total = term if total is None else total + term
        out_ref[:, k * slots : (k + 1) * slots] = total


def gather_kernel(owner_ref, slot_ref, parts_ref, out_ref):
    slots = slot_ref.shape[0]
    owner = owner_ref[...]
    slot = slot_ref[...].astype(jnp.float32)
    for k in range(6):
        picked = None
        for p in range(3):
            part = parts_ref[p, k * slots : (k + 1) * slots, :]
            term = jnp.dot(part, owner, preferred_element_type=jnp.float32)
            picked = term if picked is None else picked + term
        out_ref[k : k + 1, :] = jnp.sum(picked * slot, axis=0, keepdims=True)


def scatter_forces(owner_t, slot_t, end_force):
    owners, ends = owner_t.shape
    slots = slot_t.shape[0]
    parts = split_three(end_force)
    return pl.pallas_call(
        scatter_kernel,
        out_shape=jax.ShapeDtypeStruct((owners, 6 * slots), jnp.float32),
        cost_estimate=pl.CostEstimate(
            flops=2 * 18 * owners * slots * ends, transcendentals=0, bytes_accessed=4 * ends * 300
        ),
    )(owner_t, slot_t, parts)


def gather_velocity(owner_t, slot_t, table):
    owners, ends = owner_t.shape
    slots = slot_t.shape[0]
    return pl.pallas_call(
        gather_kernel,
        out_shape=jax.ShapeDtypeStruct((6, ends), jnp.float32),
        cost_estimate=pl.CostEstimate(
            flops=2 * 18 * owners * slots * ends, transcendentals=0, bytes_accessed=4 * ends * 300
        ),
    )(owner_t, slot_t, split_three(table))


def pair_kernel(target_ref, place_ref, force_ref, out_ref):
    targets = target_ref.shape[1]
    chunks = place_ref.shape[1] // 128

    def group(g, carry):
        rows = pl.ds(pl.multiple_of(g * 8, 8), 8)
        target_x = target_ref[0, rows, :]
        target_y = target_ref[1, rows, :]
        target_z = target_ref[2, rows, :]

        def chunk(j, sums):
            lanes = pl.ds(pl.multiple_of(j * 128, 128), 128)
            place = place_ref[:, lanes]
            force = force_ref[:, lanes]
            r_x = target_x - place[0:1]
            r_y = target_y - place[1:2]
            r_z = target_z - place[2:3]
            f_x, f_y, f_z = force[0:1], force[1:2], force[2:3]
            t_x, t_y, t_z = force[3:4], force[4:5], force[5:6]
            dist_sq = r_x * r_x + r_y * r_y + r_z * r_z
            inverse = jnp.where(dist_sq > 0.0, lax.rsqrt(dist_sq), 0.0)
            inverse_sq = inverse * inverse
            inverse_cube = inverse_sq * inverse
            inverse_fifth = inverse_cube * inverse_sq
            c_cross = 0.75 * inverse_cube
            c_iso = 0.75 * inverse + 0.5 * inverse_cube
            c_dyad = c_cross - 1.5 * inverse_fifth
            c_spin = 1.125 * inverse_fifth
            c_self = 0.375 * inverse_cube
            dyad = c_dyad * (r_x * f_x + r_y * f_y + r_z * f_z)
            spin = c_spin * (r_x * t_x + r_y * t_y + r_z * t_z)
            s_x = c_cross * r_x
            s_y = c_cross * r_y
            s_z = c_cross * r_z
            return (
                sums[0] + (c_iso * f_x + dyad * r_x + (t_y * s_z - t_z * s_y)),
                sums[1] + (c_iso * f_y + dyad * r_y + (t_z * s_x - t_x * s_z)),
                sums[2] + (c_iso * f_z + dyad * r_z + (t_x * s_y - t_y * s_x)),
                sums[3] + ((f_y * s_z - f_z * s_y) + spin * r_x - c_self * t_x),
                sums[4] + ((f_z * s_x - f_x * s_z) + spin * r_y - c_self * t_y),
                sums[5] + ((f_x * s_y - f_y * s_x) + spin * r_z - c_self * t_z),
            )

        zero = jnp.zeros((8, 128), jnp.float32)
        sums = lax.fori_loop(0, chunks, chunk, (zero,) * 6, unroll=32)
        for k in range(6):
            out_ref[k, rows, :] = sums[k]
        return carry

    lax.fori_loop(0, targets // 8, group, 0)


def mobility_own(positions, all_pos, all_forces, own_forces):
    own_rows = positions.shape[1]
    sources = all_pos.shape[1]
    spread = jnp.broadcast_to(positions[:, :, None], (3, own_rows, 128))
    partial = pl.pallas_call(
        pair_kernel,
        out_shape=jax.ShapeDtypeStruct((6, own_rows, 128), jnp.float32),
        cost_estimate=pl.CostEstimate(
            flops=90 * own_rows * sources,
            transcendentals=own_rows * sources,
            bytes_accessed=4 * (9 * sources + 9 * own_rows * 128),
        ),
    )(spread, all_pos, all_forces)
    self_scale = jnp.array([1.0, 1.0, 1.0, 0.75, 0.75, 0.75], jnp.float32)[:, None]
    return jnp.sum(partial, 2) + self_scale * own_forces


def gather_all(block, devices):
    rows, width = block.shape
    spread = jnp.broadcast_to(block[None], (devices, rows, width))
    spread = lax.all_to_all(spread, AXES, 0, 0, tiled=True)
    return spread.transpose(1, 0, 2).reshape(rows, devices * width)


def scatter_sum(full, devices):
    rows, length = full.shape
    width = length // devices
    pieces = full.reshape(rows, devices, width).transpose(1, 0, 2)
    pieces = lax.all_to_all(pieces, AXES, 0, 0, tiled=True)
    return jnp.sum(pieces, 0)


def per_device(
    positions, contact_bodies, contact_frame, gaps, impulse_now, impulse_prev, step_sizes
):
    devices = lax.axis_size("src") * lax.axis_size("tgt")
    me = lax.axis_index("src") * lax.axis_size("tgt") + lax.axis_index("tgt")
    own_rows = positions.shape[1]
    body_count = own_rows * devices
    first_rows, second_rows = contact_rows(contact_frame)
    contacts = contact_bodies.shape[1]
    end_bodies = jnp.concatenate([contact_bodies[0], contact_bodies[1]])
    end_rows = jnp.concatenate([first_rows, second_rows], axis=1)
    owner_t = (
        jnp.arange(devices, dtype=jnp.int32)[:, None] == (end_bodies // own_rows)[None, :]
    ).astype(jnp.bfloat16)
    slot_t = (
        jnp.arange(own_rows, dtype=jnp.int32)[:, None] == (end_bodies % own_rows)[None, :]
    ).astype(jnp.bfloat16)
    current = impulse_now
    shifted = impulse_now + MOMENTUM * (impulse_now - impulse_prev)
    own_velocity = jnp.zeros((6, own_rows), jnp.float32)
    for k in range(ITERS):
        end_force = end_rows * jnp.concatenate([shifted, shifted])[None, :]
        pieces = scatter_forces(owner_t, slot_t, end_force)
        pieces = lax.all_to_all(pieces, AXES, 0, 0, tiled=True)
        own_forces = jnp.sum(pieces, 0).reshape(6, own_rows)
        if k == 0:
            both = gather_all(jnp.concatenate([own_forces, positions]), devices)
            all_forces, all_pos = both[:6], both[6:]
        else:
            all_forces = gather_all(own_forces, devices)

        own_velocity = mobility_own(positions, all_pos, all_forces, own_forces)
        every = jnp.broadcast_to(own_velocity.reshape(1, 6 * own_rows), (devices, 6 * own_rows))
        every = lax.all_to_all(every, AXES, 0, 0, tiled=True)
        end_velocity = gather_velocity(owner_t, slot_t, every.T)
        end_rate = jnp.sum(end_rows * end_velocity, 0)
        normal_rate = end_rate[:contacts] + end_rate[contacts:]
        updated = jnp.maximum(shifted - step_sizes[k] * (gaps + normal_rate), 0.0)
        shifted = updated + MOMENTUM * (updated - current)
        current = updated
    return (current, own_velocity)


def solution(mesh):
    placed = (
        P(None, AXES),
        P(None, AXES),
        P(None, AXES),
        P(AXES),
        P(AXES),
        P(AXES),
        P(),
    )
    return jax.shard_map(
        per_device,
        mesh=mesh,
        in_specs=placed,
        out_specs=(P(AXES), P(None, AXES)),
        check_vma=False,
    )
```

```python
import jax
import jax.numpy as jnp
from jax import lax
from jax.experimental import pallas as pl
from jax.sharding import PartitionSpec as P

ITERS = 2
MOMENTUM = 0.4
AXES = ("src", "tgt")
SOURCE_BLOCK = 1024


def cross_product(first, second):
    return jnp.stack(
        [
            first[1] * second[2] - first[2] * second[1],
            first[2] * second[0] - first[0] * second[2],
            first[0] * second[1] - first[1] * second[0],
        ]
    )


def contact_rows(frame):
    normal = frame[0:3]
    lever_first = cross_product(frame[3:6], normal)
    lever_second = cross_product(frame[6:9], normal)
    return (jnp.concatenate([-normal, -lever_first]), jnp.concatenate([normal, lever_second]))


def pair_block(target_pos, target_ids, source_pos, source_ids, forces):
    delta_x = target_pos[0][None, :] - source_pos[0][:, None]
    delta_y = target_pos[1][None, :] - source_pos[1][:, None]
    delta_z = target_pos[2][None, :] - source_pos[2][:, None]
    coincide = target_ids[None, :] == source_ids[:, None]
    dist_sq = jnp.where(coincide, 1.0, delta_x * delta_x + delta_y * delta_y + delta_z * delta_z)
    inverse = jnp.where(coincide, 0.0, lax.rsqrt(dist_sq))
    self_term = jnp.where(coincide, 1.0, 0.0)
    unit_x = delta_x * inverse
    unit_y = delta_y * inverse
    unit_z = delta_z * inverse
    force_x, force_y, force_z = (forces[0][:, None], forces[1][:, None], forces[2][:, None])
    torque_x, torque_y, torque_z = (forces[3][:, None], forces[4][:, None], forces[5][:, None])
    inverse_sq = inverse * inverse
    c_one = 0.75 * inverse
    c_two = 0.75 * inverse_sq
    c_three = 0.375 * inverse_sq * inverse
    along_force = unit_x * force_x + unit_y * force_y + unit_z * force_z
    along_torque = unit_x * torque_x + unit_y * torque_y + unit_z * torque_z
    isotropic = c_one * (1.0 + inverse_sq * (2.0 / 3.0)) + self_term
    dyadic = c_one * (1.0 - 2.0 * inverse_sq) * along_force
    vel_x = isotropic * force_x + dyadic * unit_x + c_two * (torque_y * unit_z - torque_z * unit_y)
    vel_y = isotropic * force_y + dyadic * unit_y + c_two * (torque_z * unit_x - torque_x * unit_z)
    vel_z = isotropic * force_z + dyadic * unit_z + c_two * (torque_x * unit_y - torque_y * unit_x)
    spin_self = 0.75 * self_term - c_three
    spin_x = (
        c_two * (force_y * unit_z - force_z * unit_y)
        + c_three * 3.0 * unit_x * along_torque
        + spin_self * torque_x
    )
    spin_y = (
        c_two * (force_z * unit_x - force_x * unit_z)
        + c_three * 3.0 * unit_y * along_torque
        + spin_self * torque_y
    )
    spin_z = (
        c_two * (force_x * unit_y - force_y * unit_x)
        + c_three * 3.0 * unit_z * along_torque
        + spin_self * torque_z
    )
    return jnp.stack(
        [
            jnp.sum(vel_x, 0),
            jnp.sum(vel_y, 0),
            jnp.sum(vel_z, 0),
            jnp.sum(spin_x, 0),
            jnp.sum(spin_y, 0),
            jnp.sum(spin_z, 0),
        ]
    )


def split_two(value):
    high = lax.reduce_precision(value, exponent_bits=8, mantissa_bits=7)
    low = value - high
    return jnp.stack([high, low]).astype(jnp.bfloat16)


def scatter_kernel(owner_ref, slot_ref, parts_ref, out_ref):
    slots = slot_ref.shape[0]
    owner = owner_ref[...]
    slot = slot_ref[...]
    for k in range(6):
        total = None
        for p in range(2):
            weighted = slot * parts_ref[p, k : k + 1, :]
            term = lax.dot_general(
                owner, weighted, (((1,), (1,)), ((), ())), preferred_element_type=jnp.float32
            )
            total = term if total is None else total + term
        out_ref[:, k * slots : (k + 1) * slots] = total


def gather_kernel(owner_ref, slot_ref, parts_ref, out_ref):
    slots = slot_ref.shape[0]
    owner = owner_ref[...]
    slot = slot_ref[...].astype(jnp.float32)
    for k in range(6):
        picked = None
        for p in range(2):
            part = parts_ref[p, k * slots : (k + 1) * slots, :]
            term = jnp.dot(part, owner, preferred_element_type=jnp.float32)
            picked = term if picked is None else picked + term
        out_ref[k : k + 1, :] = jnp.sum(picked * slot, axis=0, keepdims=True)


def scatter_forces(owner_t, slot_t, end_force):
    owners, ends = owner_t.shape
    slots = slot_t.shape[0]
    parts = split_two(end_force)
    return pl.pallas_call(
        scatter_kernel,
        out_shape=jax.ShapeDtypeStruct((owners, 6 * slots), jnp.float32),
        cost_estimate=pl.CostEstimate(
            flops=2 * 12 * owners * slots * ends, transcendentals=0, bytes_accessed=4 * ends * 300
        ),
    )(owner_t, slot_t, parts)


def gather_velocity(owner_t, slot_t, table):
    owners, ends = owner_t.shape
    slots = slot_t.shape[0]
    return pl.pallas_call(
        gather_kernel,
        out_shape=jax.ShapeDtypeStruct((6, ends), jnp.float32),
        cost_estimate=pl.CostEstimate(
            flops=2 * 12 * owners * slots * ends, transcendentals=0, bytes_accessed=4 * ends * 300
        ),
    )(owner_t, slot_t, split_two(table))


def pair_kernel(target_ref, place_ref, force_ref, out_ref):
    targets = target_ref.shape[1]
    chunks = place_ref.shape[1] // 128

    def group(g, carry):
        rows = pl.ds(pl.multiple_of(g * 8, 8), 8)
        target_x = target_ref[0, rows, :]
        target_y = target_ref[1, rows, :]
        target_z = target_ref[2, rows, :]

        def chunk(j, sums):
            lanes = pl.ds(pl.multiple_of(j * 128, 128), 128)
            place = place_ref[:, lanes]
            force = force_ref[:, lanes]
            r_x = target_x - place[0:1]
            r_y = target_y - place[1:2]
            r_z = target_z - place[2:3]
            f_x, f_y, f_z = force[0:1], force[1:2], force[2:3]
            t_x, t_y, t_z = force[3:4], force[4:5], force[5:6]
            dist_sq = r_x * r_x + r_y * r_y + r_z * r_z
            inverse = jnp.where(dist_sq > 0.0, lax.rsqrt(dist_sq), 0.0)
            inverse_sq = inverse * inverse
            inverse_cube = inverse_sq * inverse
            inverse_fifth = inverse_cube * inverse_sq
            c_cross = 0.75 * inverse_cube
            c_iso = 0.75 * inverse + 0.5 * inverse_cube
            c_dyad = c_cross - 1.5 * inverse_fifth
            c_spin = 1.125 * inverse_fifth
            c_self = 0.375 * inverse_cube
            dyad = c_dyad * (r_x * f_x + r_y * f_y + r_z * f_z)
            spin = c_spin * (r_x * t_x + r_y * t_y + r_z * t_z)
            s_x = c_cross * r_x
            s_y = c_cross * r_y
            s_z = c_cross * r_z
            return (
                sums[0] + (c_iso * f_x + dyad * r_x + (t_y * s_z - t_z * s_y)),
                sums[1] + (c_iso * f_y + dyad * r_y + (t_z * s_x - t_x * s_z)),
                sums[2] + (c_iso * f_z + dyad * r_z + (t_x * s_y - t_y * s_x)),
                sums[3] + ((f_y * s_z - f_z * s_y) + spin * r_x - c_self * t_x),
                sums[4] + ((f_z * s_x - f_x * s_z) + spin * r_y - c_self * t_y),
                sums[5] + ((f_x * s_y - f_y * s_x) + spin * r_z - c_self * t_z),
            )

        zero = jnp.zeros((8, 128), jnp.float32)
        sums = lax.fori_loop(0, chunks, chunk, (zero,) * 6, unroll=32)
        for k in range(6):
            out_ref[k, rows, :] = sums[k]
        return carry

    lax.fori_loop(0, targets // 8, group, 0)


def mobility_own(positions, all_pos, all_forces, own_forces):
    own_rows = positions.shape[1]
    sources = all_pos.shape[1]
    spread = jnp.broadcast_to(positions[:, :, None], (3, own_rows, 128))
    partial = pl.pallas_call(
        pair_kernel,
        out_shape=jax.ShapeDtypeStruct((6, own_rows, 128), jnp.float32),
        cost_estimate=pl.CostEstimate(
            flops=90 * own_rows * sources,
            transcendentals=own_rows * sources,
            bytes_accessed=4 * (9 * sources + 9 * own_rows * 128),
        ),
    )(spread, all_pos, all_forces)
    self_scale = jnp.array([1.0, 1.0, 1.0, 0.75, 0.75, 0.75], jnp.float32)[:, None]
    return jnp.sum(partial, 2) + self_scale * own_forces


def gather_all(block, devices):
    rows, width = block.shape
    spread = jnp.broadcast_to(block[None], (devices, rows, width))
    spread = lax.all_to_all(spread, AXES, 0, 0, tiled=True)
    return spread.transpose(1, 0, 2).reshape(rows, devices * width)


def scatter_sum(full, devices):
    rows, length = full.shape
    width = length // devices
    pieces = full.reshape(rows, devices, width).transpose(1, 0, 2)
    pieces = lax.all_to_all(pieces, AXES, 0, 0, tiled=True)
    return jnp.sum(pieces, 0)


def per_device(
    positions, contact_bodies, contact_frame, gaps, impulse_now, impulse_prev, step_sizes
):
    devices = lax.axis_size("src") * lax.axis_size("tgt")
    me = lax.axis_index("src") * lax.axis_size("tgt") + lax.axis_index("tgt")
    own_rows = positions.shape[1]
    body_count = own_rows * devices
    first_rows, second_rows = contact_rows(contact_frame)
    contacts = contact_bodies.shape[1]
    end_bodies = jnp.concatenate([contact_bodies[0], contact_bodies[1]])
    end_rows = jnp.concatenate([first_rows, second_rows], axis=1)
    owner_t = (
        jnp.arange(devices, dtype=jnp.int32)[:, None] == (end_bodies // own_rows)[None, :]
    ).astype(jnp.bfloat16)
    slot_t = (
        jnp.arange(own_rows, dtype=jnp.int32)[:, None] == (end_bodies % own_rows)[None, :]
    ).astype(jnp.bfloat16)
    current = impulse_now
    shifted = impulse_now + MOMENTUM * (impulse_now - impulse_prev)
    own_velocity = jnp.zeros((6, own_rows), jnp.float32)
    for k in range(ITERS):
        end_force = end_rows * jnp.concatenate([shifted, shifted])[None, :]
        pieces = scatter_forces(owner_t, slot_t, end_force)
        pieces = lax.all_to_all(pieces, AXES, 0, 0, tiled=True)
        own_forces = jnp.sum(pieces, 0).reshape(6, own_rows)
        if k == 0:
            both = gather_all(jnp.concatenate([own_forces, positions]), devices)
            all_forces, all_pos = both[:6], both[6:]
        else:
            all_forces = gather_all(own_forces, devices)

        own_velocity = mobility_own(positions, all_pos, all_forces, own_forces)
        every = jnp.broadcast_to(own_velocity.reshape(1, 6 * own_rows), (devices, 6 * own_rows))
        every = lax.all_to_all(every, AXES, 0, 0, tiled=True)
        end_velocity = gather_velocity(owner_t, slot_t, every.T)
        end_rate = jnp.sum(end_rows * end_velocity, 0)
        normal_rate = end_rate[:contacts] + end_rate[contacts:]
        updated = jnp.maximum(shifted - step_sizes[k] * (gaps + normal_rate), 0.0)
        shifted = updated + MOMENTUM * (updated - current)
        current = updated
    return (current, own_velocity)


def solution(mesh):
    placed = (
        P(None, AXES),
        P(None, AXES),
        P(None, AXES),
        P(AXES),
        P(AXES),
        P(AXES),
        P(),
    )
    return jax.shard_map(
        per_device,
        mesh=mesh,
        in_specs=placed,
        out_specs=(P(AXES), P(None, AXES)),
        check_vma=False,
    )
```

```python
import jax
import jax.numpy as jnp
from jax import lax
from jax.experimental import pallas as pl
from jax.experimental.pallas import tpu as pltpu
from jax.sharding import PartitionSpec as P

ITERS = 2
MOMENTUM = 0.4
AXES = ("src", "tgt")
SOURCE_BLOCK = 1024


def cross_product(first, second):
    return jnp.stack(
        [
            first[1] * second[2] - first[2] * second[1],
            first[2] * second[0] - first[0] * second[2],
            first[0] * second[1] - first[1] * second[0],
        ]
    )


def contact_rows(frame):
    normal = frame[0:3]
    lever_first = cross_product(frame[3:6], normal)
    lever_second = cross_product(frame[6:9], normal)
    return (jnp.concatenate([-normal, -lever_first]), jnp.concatenate([normal, lever_second]))


def pair_block(target_pos, target_ids, source_pos, source_ids, forces):
    delta_x = target_pos[0][None, :] - source_pos[0][:, None]
    delta_y = target_pos[1][None, :] - source_pos[1][:, None]
    delta_z = target_pos[2][None, :] - source_pos[2][:, None]
    coincide = target_ids[None, :] == source_ids[:, None]
    dist_sq = jnp.where(coincide, 1.0, delta_x * delta_x + delta_y * delta_y + delta_z * delta_z)
    inverse = jnp.where(coincide, 0.0, lax.rsqrt(dist_sq))
    self_term = jnp.where(coincide, 1.0, 0.0)
    unit_x = delta_x * inverse
    unit_y = delta_y * inverse
    unit_z = delta_z * inverse
    force_x, force_y, force_z = (forces[0][:, None], forces[1][:, None], forces[2][:, None])
    torque_x, torque_y, torque_z = (forces[3][:, None], forces[4][:, None], forces[5][:, None])
    inverse_sq = inverse * inverse
    c_one = 0.75 * inverse
    c_two = 0.75 * inverse_sq
    c_three = 0.375 * inverse_sq * inverse
    along_force = unit_x * force_x + unit_y * force_y + unit_z * force_z
    along_torque = unit_x * torque_x + unit_y * torque_y + unit_z * torque_z
    isotropic = c_one * (1.0 + inverse_sq * (2.0 / 3.0)) + self_term
    dyadic = c_one * (1.0 - 2.0 * inverse_sq) * along_force
    vel_x = isotropic * force_x + dyadic * unit_x + c_two * (torque_y * unit_z - torque_z * unit_y)
    vel_y = isotropic * force_y + dyadic * unit_y + c_two * (torque_z * unit_x - torque_x * unit_z)
    vel_z = isotropic * force_z + dyadic * unit_z + c_two * (torque_x * unit_y - torque_y * unit_x)
    spin_self = 0.75 * self_term - c_three
    spin_x = (
        c_two * (force_y * unit_z - force_z * unit_y)
        + c_three * 3.0 * unit_x * along_torque
        + spin_self * torque_x
    )
    spin_y = (
        c_two * (force_z * unit_x - force_x * unit_z)
        + c_three * 3.0 * unit_y * along_torque
        + spin_self * torque_y
    )
    spin_z = (
        c_two * (force_x * unit_y - force_y * unit_x)
        + c_three * 3.0 * unit_z * along_torque
        + spin_self * torque_z
    )
    return jnp.stack(
        [
            jnp.sum(vel_x, 0),
            jnp.sum(vel_y, 0),
            jnp.sum(vel_z, 0),
            jnp.sum(spin_x, 0),
            jnp.sum(spin_y, 0),
            jnp.sum(spin_z, 0),
        ]
    )


def split_two(value):
    high = lax.reduce_precision(value, exponent_bits=8, mantissa_bits=7)
    low = value - high
    return jnp.stack([high, low]).astype(jnp.bfloat16)


def scatter_kernel(owner_ref, slot_ref, parts_ref, out_ref):
    slots = slot_ref.shape[0]
    owner = owner_ref[...]
    slot = slot_ref[...]
    for k in range(6):
        total = None
        for p in range(2):
            weighted = slot * parts_ref[p, k : k + 1, :]
            term = lax.dot_general(
                owner, weighted, (((1,), (1,)), ((), ())), preferred_element_type=jnp.float32
            )
            total = term if total is None else total + term
        out_ref[:, k * slots : (k + 1) * slots] = total


def gather_kernel(owner_ref, slot_ref, parts_ref, out_ref):
    slots = slot_ref.shape[0]
    owner = owner_ref[...]
    slot = slot_ref[...].astype(jnp.float32)
    for k in range(6):
        picked = None
        for p in range(2):
            part = parts_ref[p, k * slots : (k + 1) * slots, :]
            term = jnp.dot(part, owner, preferred_element_type=jnp.float32)
            picked = term if picked is None else picked + term
        out_ref[k : k + 1, :] = jnp.sum(picked * slot, axis=0, keepdims=True)


def scatter_forces(owner_t, slot_t, end_force):
    owners, ends = owner_t.shape
    slots = slot_t.shape[0]
    parts = split_two(end_force)
    return pl.pallas_call(
        scatter_kernel,
        out_shape=jax.ShapeDtypeStruct((owners, 6 * slots), jnp.float32),
        cost_estimate=pl.CostEstimate(
            flops=2 * 12 * owners * slots * ends, transcendentals=0, bytes_accessed=4 * ends * 300
        ),
    )(owner_t, slot_t, parts)


def gather_velocity(owner_t, slot_t, table):
    owners, ends = owner_t.shape
    slots = slot_t.shape[0]
    return pl.pallas_call(
        gather_kernel,
        out_shape=jax.ShapeDtypeStruct((6, ends), jnp.float32),
        cost_estimate=pl.CostEstimate(
            flops=2 * 12 * owners * slots * ends, transcendentals=0, bytes_accessed=4 * ends * 300
        ),
    )(owner_t, slot_t, split_two(table))


def pair_kernel(target_ref, place_ref, force_ref, own_ref, out_ref, sums_ref):
    targets = target_ref.shape[1]
    chunks = place_ref.shape[0]
    first_place = place_ref.shape[1] - 3

    def group(g, carry):
        rows = pl.ds(pl.multiple_of(g * 8, 8), 8)
        target_x = target_ref[0, rows, :]
        target_y = target_ref[1, rows, :]
        target_z = target_ref[2, rows, :]

        def chunk(j, sums):
            place = place_ref[j, first_place : first_place + 3, :]
            force = force_ref[j, 0:6, :]
            r_x = target_x - place[0:1]
            r_y = target_y - place[1:2]
            r_z = target_z - place[2:3]
            f_x, f_y, f_z = force[0:1], force[1:2], force[2:3]
            t_x, t_y, t_z = force[3:4], force[4:5], force[5:6]
            dist_sq = r_x * r_x + r_y * r_y + r_z * r_z
            inverse = jnp.where(dist_sq > 0.0, lax.rsqrt(dist_sq), 0.0)
            inverse_sq = inverse * inverse
            inverse_cube = inverse_sq * inverse
            inverse_fifth = inverse_cube * inverse_sq
            c_cross = 0.75 * inverse_cube
            c_iso = 0.75 * inverse + 0.5 * inverse_cube
            c_dyad = c_cross - 1.5 * inverse_fifth
            c_spin = 1.125 * inverse_fifth
            c_self = 0.375 * inverse_cube
            dyad = c_dyad * (r_x * f_x + r_y * f_y + r_z * f_z)
            spin = c_spin * (r_x * t_x + r_y * t_y + r_z * t_z)
            s_x = c_cross * r_x
            s_y = c_cross * r_y
            s_z = c_cross * r_z
            return (
                sums[0] + (c_iso * f_x + dyad * r_x + (t_y * s_z - t_z * s_y)),
                sums[1] + (c_iso * f_y + dyad * r_y + (t_z * s_x - t_x * s_z)),
                sums[2] + (c_iso * f_z + dyad * r_z + (t_x * s_y - t_y * s_x)),
                sums[3] + ((f_y * s_z - f_z * s_y) + spin * r_x - c_self * t_x),
                sums[4] + ((f_z * s_x - f_x * s_z) + spin * r_y - c_self * t_y),
                sums[5] + ((f_x * s_y - f_y * s_x) + spin * r_z - c_self * t_z),
            )

        zero = jnp.zeros((8, 128), jnp.float32)
        sums = lax.fori_loop(0, chunks, chunk, (zero,) * 6, unroll=32)
        for k in range(6):
            sums_ref[k, rows, :] = sums[k]
        return carry

    lax.fori_loop(0, targets // 8, group, 0)
    ones = jnp.ones((8, 128), jnp.bfloat16)
    for k in range(6):
        value = sums_ref[k]
        high = value.astype(jnp.bfloat16)
        rest = value - high.astype(jnp.float32)
        middle = rest.astype(jnp.bfloat16)
        low = (rest - middle.astype(jnp.float32)).astype(jnp.bfloat16)
        total = None
        for part in (high, middle, low):
            term = lax.dot_general(
                ones, part, (((1,), (1,)), ((), ())), preferred_element_type=jnp.float32
            )
            total = term if total is None else total + term
        scale = 1.0 if k < 3 else 0.75
        out_ref[k : k + 1, :] = total[0:1, :] + scale * own_ref[k : k + 1, :]


def mobility_own(spread, places, forces, own_forces):
    own_rows = own_forces.shape[1]
    sources = places.shape[0] * places.shape[2]
    return pl.pallas_call(
        pair_kernel,
        out_shape=jax.ShapeDtypeStruct((6, own_rows), jnp.float32),
        scratch_shapes=[pltpu.VMEM((6, own_rows, 128), jnp.float32)],
        cost_estimate=pl.CostEstimate(
            flops=90 * own_rows * sources,
            transcendentals=own_rows * sources,
            bytes_accessed=4 * (9 * sources + 3 * own_rows * 128),
        ),
    )(spread, places, forces, own_forces)

def gather_all(block, devices):
    rows, width = block.shape
    spread = jnp.broadcast_to(block[None], (devices, rows, width))
    spread = lax.all_to_all(spread, AXES, 0, 0, tiled=True)
    return spread.transpose(1, 0, 2).reshape(rows, devices * width)


def scatter_sum(full, devices):
    rows, length = full.shape
    width = length // devices
    pieces = full.reshape(rows, devices, width).transpose(1, 0, 2)
    pieces = lax.all_to_all(pieces, AXES, 0, 0, tiled=True)
    return jnp.sum(pieces, 0)


def per_device(
    positions, contact_bodies, contact_frame, gaps, impulse_now, impulse_prev, step_sizes
):
    devices = lax.axis_size("src") * lax.axis_size("tgt")
    me = lax.axis_index("src") * lax.axis_size("tgt") + lax.axis_index("tgt")
    own_rows = positions.shape[1]
    body_count = own_rows * devices
    first_rows, second_rows = contact_rows(contact_frame)
    contacts = contact_bodies.shape[1]
    end_bodies = jnp.concatenate([contact_bodies[0], contact_bodies[1]])
    end_rows = jnp.concatenate([first_rows, second_rows], axis=1)
    owner_t = (
        jnp.arange(devices, dtype=jnp.int32)[:, None] == (end_bodies // own_rows)[None, :]
    ).astype(jnp.bfloat16)
    slot_t = (
        jnp.arange(own_rows, dtype=jnp.int32)[:, None] == (end_bodies % own_rows)[None, :]
    ).astype(jnp.bfloat16)
    spread = jnp.broadcast_to(positions[:, :, None], (3, own_rows, 128))
    current = impulse_now
    shifted = impulse_now + MOMENTUM * (impulse_now - impulse_prev)
    own_velocity = jnp.zeros((6, own_rows), jnp.float32)
    for k in range(ITERS):
        end_force = end_rows * jnp.concatenate([shifted, shifted])[None, :]
        pieces = scatter_forces(owner_t, slot_t, end_force)
        pieces = lax.all_to_all(pieces, AXES, 0, 0, tiled=True)
        own_forces = jnp.sum(pieces, 0).reshape(6, own_rows)
        if k == 0:
            places = lax.all_to_all(
                jnp.broadcast_to(jnp.concatenate([own_forces, positions])[None], (devices, 9, own_rows)),
                AXES, 0, 0, tiled=True,
            )
            forces = places
        else:
            forces = lax.all_to_all(
                jnp.broadcast_to(own_forces[None], (devices, 6, own_rows)), AXES, 0, 0, tiled=True
            )
        own_velocity = mobility_own(spread, places, forces, own_forces)
        every = jnp.broadcast_to(own_velocity.reshape(1, 6 * own_rows), (devices, 6 * own_rows))
        every = lax.all_to_all(every, AXES, 0, 0, tiled=True)
        end_velocity = gather_velocity(owner_t, slot_t, every.T)
        end_rate = jnp.sum(end_rows * end_velocity, 0)
        normal_rate = end_rate[:contacts] + end_rate[contacts:]
        updated = jnp.maximum(shifted - step_sizes[k] * (gaps + normal_rate), 0.0)
        shifted = updated + MOMENTUM * (updated - current)
        current = updated
    return (current, own_velocity)


def solution(mesh):
    placed = (
        P(None, AXES),
        P(None, AXES),
        P(None, AXES),
        P(AXES),
        P(AXES),
        P(AXES),
        P(),
    )
    return jax.shard_map(
        per_device,
        mesh=mesh,
        in_specs=placed,
        out_specs=(P(AXES), P(None, AXES)),
        check_vma=False,
    )
```

```python
import jax
import jax.numpy as jnp
from jax import lax
from jax.experimental import pallas as pl
from jax.experimental.pallas import tpu as pltpu
from jax.sharding import PartitionSpec as P

ITERS = 2
MOMENTUM = 0.4
AXES = ("src", "tgt")
SOURCE_BLOCK = 1024


def cross_product(first, second):
    return jnp.stack(
        [
            first[1] * second[2] - first[2] * second[1],
            first[2] * second[0] - first[0] * second[2],
            first[0] * second[1] - first[1] * second[0],
        ]
    )


def contact_rows(frame):
    normal = frame[0:3]
    lever_first = cross_product(frame[3:6], normal)
    lever_second = cross_product(frame[6:9], normal)
    return (jnp.concatenate([-normal, -lever_first]), jnp.concatenate([normal, lever_second]))


def pair_block(target_pos, target_ids, source_pos, source_ids, forces):
    delta_x = target_pos[0][None, :] - source_pos[0][:, None]
    delta_y = target_pos[1][None, :] - source_pos[1][:, None]
    delta_z = target_pos[2][None, :] - source_pos[2][:, None]
    coincide = target_ids[None, :] == source_ids[:, None]
    dist_sq = jnp.where(coincide, 1.0, delta_x * delta_x + delta_y * delta_y + delta_z * delta_z)
    inverse = jnp.where(coincide, 0.0, lax.rsqrt(dist_sq))
    self_term = jnp.where(coincide, 1.0, 0.0)
    unit_x = delta_x * inverse
    unit_y = delta_y * inverse
    unit_z = delta_z * inverse
    force_x, force_y, force_z = (forces[0][:, None], forces[1][:, None], forces[2][:, None])
    torque_x, torque_y, torque_z = (forces[3][:, None], forces[4][:, None], forces[5][:, None])
    inverse_sq = inverse * inverse
    c_one = 0.75 * inverse
    c_two = 0.75 * inverse_sq
    c_three = 0.375 * inverse_sq * inverse
    along_force = unit_x * force_x + unit_y * force_y + unit_z * force_z
    along_torque = unit_x * torque_x + unit_y * torque_y + unit_z * torque_z
    isotropic = c_one * (1.0 + inverse_sq * (2.0 / 3.0)) + self_term
    dyadic = c_one * (1.0 - 2.0 * inverse_sq) * along_force
    vel_x = isotropic * force_x + dyadic * unit_x + c_two * (torque_y * unit_z - torque_z * unit_y)
    vel_y = isotropic * force_y + dyadic * unit_y + c_two * (torque_z * unit_x - torque_x * unit_z)
    vel_z = isotropic * force_z + dyadic * unit_z + c_two * (torque_x * unit_y - torque_y * unit_x)
    spin_self = 0.75 * self_term - c_three
    spin_x = (
        c_two * (force_y * unit_z - force_z * unit_y)
        + c_three * 3.0 * unit_x * along_torque
        + spin_self * torque_x
    )
    spin_y = (
        c_two * (force_z * unit_x - force_x * unit_z)
        + c_three * 3.0 * unit_y * along_torque
        + spin_self * torque_y
    )
    spin_z = (
        c_two * (force_x * unit_y - force_y * unit_x)
        + c_three * 3.0 * unit_z * along_torque
        + spin_self * torque_z
    )
    return jnp.stack(
        [
            jnp.sum(vel_x, 0),
            jnp.sum(vel_y, 0),
            jnp.sum(vel_z, 0),
            jnp.sum(spin_x, 0),
            jnp.sum(spin_y, 0),
            jnp.sum(spin_z, 0),
        ]
    )


def split_two(value):
    high = lax.reduce_precision(value, exponent_bits=8, mantissa_bits=7)
    low = value - high
    return jnp.stack([high, low]).astype(jnp.bfloat16)


def scatter_kernel(owner_ref, slot_ref, parts_ref, out_ref):
    slots = slot_ref.shape[0]
    owner = owner_ref[...]
    slot = slot_ref[...]
    for k in range(6):
        total = None
        for p in range(2):
            weighted = slot * parts_ref[p, k : k + 1, :]
            term = lax.dot_general(
                owner, weighted, (((1,), (1,)), ((), ())), preferred_element_type=jnp.float32
            )
            total = term if total is None else total + term
        out_ref[:, 0, k * slots : (k + 1) * slots] = total


def gather_kernel(owner_ref, slot_ref, parts_ref, out_ref):
    slots = slot_ref.shape[0]
    owner = owner_ref[...]
    slot = slot_ref[...].astype(jnp.float32)
    for k in range(6):
        picked = None
        for p in range(2):
            part = parts_ref[p, k * slots : (k + 1) * slots, :]
            term = jnp.dot(part, owner, preferred_element_type=jnp.float32)
            picked = term if picked is None else picked + term
        out_ref[k : k + 1, :] = jnp.sum(picked * slot, axis=0, keepdims=True)


def scatter_forces(owner_t, slot_t, end_force):
    owners, ends = owner_t.shape
    slots = slot_t.shape[0]
    parts = split_two(end_force)
    return pl.pallas_call(
        scatter_kernel,
        out_shape=jax.ShapeDtypeStruct((owners, 1, 6 * slots), jnp.float32),
        cost_estimate=pl.CostEstimate(
            flops=2 * 12 * owners * slots * ends, transcendentals=0, bytes_accessed=4 * ends * 300
        ),
    )(owner_t, slot_t, parts)


def gather_velocity(owner_t, slot_t, table):
    owners, ends = owner_t.shape
    slots = slot_t.shape[0]
    return pl.pallas_call(
        gather_kernel,
        out_shape=jax.ShapeDtypeStruct((6, ends), jnp.float32),
        cost_estimate=pl.CostEstimate(
            flops=2 * 12 * owners * slots * ends, transcendentals=0, bytes_accessed=4 * ends * 300
        ),
    )(owner_t, slot_t, split_two(table))


def pair_kernel(target_ref, place_ref, force_ref, own_ref, out_ref, sums_ref):
    targets = target_ref.shape[1]
    chunks = place_ref.shape[0]
    first_place = place_ref.shape[2] // 128 - 3

    def group(g, carry):
        rows = pl.ds(pl.multiple_of(g * 8, 8), 8)
        target_x = target_ref[0, rows, :]
        target_y = target_ref[1, rows, :]
        target_z = target_ref[2, rows, :]

        def chunk(j, sums):
            place = place_ref[j]
            force = force_ref[j]

            def lane_row(block, row):
                return block[:, row * 128 : (row + 1) * 128]

            r_x = target_x - lane_row(place, first_place)
            r_y = target_y - lane_row(place, first_place + 1)
            r_z = target_z - lane_row(place, first_place + 2)
            f_x, f_y, f_z = (lane_row(force, 0), lane_row(force, 1), lane_row(force, 2))
            t_x, t_y, t_z = (lane_row(force, 3), lane_row(force, 4), lane_row(force, 5))
            dist_sq = r_x * r_x + r_y * r_y + r_z * r_z
            inverse = jnp.where(dist_sq > 0.0, lax.rsqrt(dist_sq), 0.0)
            inverse_sq = inverse * inverse
            inverse_cube = inverse_sq * inverse
            inverse_fifth = inverse_cube * inverse_sq
            c_cross = 0.75 * inverse_cube
            c_iso = 0.75 * inverse + 0.5 * inverse_cube
            c_dyad = c_cross - 1.5 * inverse_fifth
            c_spin = 1.125 * inverse_fifth
            c_self = 0.375 * inverse_cube
            dyad = c_dyad * (r_x * f_x + r_y * f_y + r_z * f_z)
            spin = c_spin * (r_x * t_x + r_y * t_y + r_z * t_z)
            s_x = c_cross * r_x
            s_y = c_cross * r_y
            s_z = c_cross * r_z
            return (
                sums[0] + (c_iso * f_x + dyad * r_x + (t_y * s_z - t_z * s_y)),
                sums[1] + (c_iso * f_y + dyad * r_y + (t_z * s_x - t_x * s_z)),
                sums[2] + (c_iso * f_z + dyad * r_z + (t_x * s_y - t_y * s_x)),
                sums[3] + ((f_y * s_z - f_z * s_y) + spin * r_x - c_self * t_x),
                sums[4] + ((f_z * s_x - f_x * s_z) + spin * r_y - c_self * t_y),
                sums[5] + ((f_x * s_y - f_y * s_x) + spin * r_z - c_self * t_z),
            )

        zero = jnp.zeros((8, 128), jnp.float32)
        sums = lax.fori_loop(0, chunks, chunk, (zero,) * 6, unroll=32)
        for k in range(6):
            sums_ref[k, rows, :] = sums[k]
        return carry

    lax.fori_loop(0, targets // 8, group, 0)
    ones = jnp.ones((8, 128), jnp.bfloat16)
    for k in range(6):
        value = sums_ref[k]
        high = value.astype(jnp.bfloat16)
        rest = value - high.astype(jnp.float32)
        middle = rest.astype(jnp.bfloat16)
        low = (rest - middle.astype(jnp.float32)).astype(jnp.bfloat16)
        total = None
        for part in (high, middle, low):
            term = lax.dot_general(
                ones, part, (((1,), (1,)), ((), ())), preferred_element_type=jnp.float32
            )
            total = term if total is None else total + term
        scale = 1.0 if k < 3 else 0.75
        out_ref[k : k + 1, :] = total[0:1, :] + scale * own_ref[k : k + 1, :]


def mobility_own(spread, places, forces, own_forces):
    own_rows = own_forces.shape[1]
    sources = places.shape[0] * 128
    return pl.pallas_call(
        pair_kernel,
        out_shape=jax.ShapeDtypeStruct((6, own_rows), jnp.float32),
        scratch_shapes=[pltpu.VMEM((6, own_rows, 128), jnp.float32)],
        cost_estimate=pl.CostEstimate(
            flops=90 * own_rows * sources,
            transcendentals=own_rows * sources,
            bytes_accessed=4 * (9 * sources + 3 * own_rows * 128),
        ),
    )(spread, places, forces, own_forces)

def gather_all(block, devices):
    rows, width = block.shape
    spread = jnp.broadcast_to(block[None], (devices, rows, width))
    spread = lax.all_to_all(spread, AXES, 0, 0, tiled=True)
    return spread.transpose(1, 0, 2).reshape(rows, devices * width)


def scatter_sum(full, devices):
    rows, length = full.shape
    width = length // devices
    pieces = full.reshape(rows, devices, width).transpose(1, 0, 2)
    pieces = lax.all_to_all(pieces, AXES, 0, 0, tiled=True)
    return jnp.sum(pieces, 0)


def per_device(
    positions, contact_bodies, contact_frame, gaps, impulse_now, impulse_prev, step_sizes
):
    devices = lax.axis_size("src") * lax.axis_size("tgt")
    me = lax.axis_index("src") * lax.axis_size("tgt") + lax.axis_index("tgt")
    own_rows = positions.shape[1]
    body_count = own_rows * devices
    first_rows, second_rows = contact_rows(contact_frame)
    contacts = contact_bodies.shape[1]
    end_bodies = jnp.concatenate([contact_bodies[0], contact_bodies[1]])
    end_rows = jnp.concatenate([first_rows, second_rows], axis=1)
    owner_t = (
        jnp.arange(devices, dtype=jnp.int32)[:, None] == (end_bodies // own_rows)[None, :]
    ).astype(jnp.bfloat16)
    slot_t = (
        jnp.arange(own_rows, dtype=jnp.int32)[:, None] == (end_bodies % own_rows)[None, :]
    ).astype(jnp.bfloat16)
    spread = jnp.broadcast_to(positions[:, :, None], (3, own_rows, 128))
    current = impulse_now
    shifted = impulse_now + MOMENTUM * (impulse_now - impulse_prev)
    own_velocity = jnp.zeros((6, own_rows), jnp.float32)
    for k in range(ITERS):
        end_force = end_rows * jnp.concatenate([shifted, shifted])[None, :]
        pieces = scatter_forces(owner_t, slot_t, end_force)
        pieces = lax.all_to_all(pieces, AXES, 0, 0, tiled=True)
        own_forces = jnp.sum(pieces, 0).reshape(6, own_rows)
        if k == 0:
            block = jnp.concatenate([own_forces, positions]).reshape(1, 1, 9 * own_rows)
            places = lax.all_to_all(
                jnp.broadcast_to(block, (devices, 1, 9 * own_rows)), AXES, 0, 0, tiled=True
            )
            forces = places
        else:
            block = own_forces.reshape(1, 1, 6 * own_rows)
            forces = lax.all_to_all(
                jnp.broadcast_to(block, (devices, 1, 6 * own_rows)), AXES, 0, 0, tiled=True
            )
        own_velocity = mobility_own(spread, places, forces, own_forces)
        every = jnp.broadcast_to(own_velocity.reshape(1, 6 * own_rows), (devices, 6 * own_rows))
        every = lax.all_to_all(every, AXES, 0, 0, tiled=True)
        end_velocity = gather_velocity(owner_t, slot_t, every.T)
        end_rate = jnp.sum(end_rows * end_velocity, 0)
        normal_rate = end_rate[:contacts] + end_rate[contacts:]
        updated = jnp.maximum(shifted - step_sizes[k] * (gaps + normal_rate), 0.0)
        shifted = updated + MOMENTUM * (updated - current)
        current = updated
    return (current, own_velocity)


def solution(mesh):
    placed = (
        P(None, AXES),
        P(None, AXES),
        P(None, AXES),
        P(AXES),
        P(AXES),
        P(AXES),
        P(),
    )
    return jax.shard_map(
        per_device,
        mesh=mesh,
        in_specs=placed,
        out_specs=(P(AXES), P(None, AXES)),
        check_vma=False,
    )
```

```python
import functools

import jax
import jax.numpy as jnp
from jax import lax
from jax.experimental import pallas as pl
from jax.experimental.pallas import tpu as pltpu
from jax.sharding import PartitionSpec as P

ITERS = 2
MOMENTUM = 0.4
AXES = ("src", "tgt")
SOURCE_BLOCK = 1024


def cross_product(first, second):
    return jnp.stack(
        [
            first[1] * second[2] - first[2] * second[1],
            first[2] * second[0] - first[0] * second[2],
            first[0] * second[1] - first[1] * second[0],
        ]
    )


def contact_rows(frame):
    normal = frame[0:3]
    lever_first = cross_product(frame[3:6], normal)
    lever_second = cross_product(frame[6:9], normal)
    return (jnp.concatenate([-normal, -lever_first]), jnp.concatenate([normal, lever_second]))


def pair_block(target_pos, target_ids, source_pos, source_ids, forces):
    delta_x = target_pos[0][None, :] - source_pos[0][:, None]
    delta_y = target_pos[1][None, :] - source_pos[1][:, None]
    delta_z = target_pos[2][None, :] - source_pos[2][:, None]
    coincide = target_ids[None, :] == source_ids[:, None]
    dist_sq = jnp.where(coincide, 1.0, delta_x * delta_x + delta_y * delta_y + delta_z * delta_z)
    inverse = jnp.where(coincide, 0.0, lax.rsqrt(dist_sq))
    self_term = jnp.where(coincide, 1.0, 0.0)
    unit_x = delta_x * inverse
    unit_y = delta_y * inverse
    unit_z = delta_z * inverse
    force_x, force_y, force_z = (forces[0][:, None], forces[1][:, None], forces[2][:, None])
    torque_x, torque_y, torque_z = (forces[3][:, None], forces[4][:, None], forces[5][:, None])
    inverse_sq = inverse * inverse
    c_one = 0.75 * inverse
    c_two = 0.75 * inverse_sq
    c_three = 0.375 * inverse_sq * inverse
    along_force = unit_x * force_x + unit_y * force_y + unit_z * force_z
    along_torque = unit_x * torque_x + unit_y * torque_y + unit_z * torque_z
    isotropic = c_one * (1.0 + inverse_sq * (2.0 / 3.0)) + self_term
    dyadic = c_one * (1.0 - 2.0 * inverse_sq) * along_force
    vel_x = isotropic * force_x + dyadic * unit_x + c_two * (torque_y * unit_z - torque_z * unit_y)
    vel_y = isotropic * force_y + dyadic * unit_y + c_two * (torque_z * unit_x - torque_x * unit_z)
    vel_z = isotropic * force_z + dyadic * unit_z + c_two * (torque_x * unit_y - torque_y * unit_x)
    spin_self = 0.75 * self_term - c_three
    spin_x = (
        c_two * (force_y * unit_z - force_z * unit_y)
        + c_three * 3.0 * unit_x * along_torque
        + spin_self * torque_x
    )
    spin_y = (
        c_two * (force_z * unit_x - force_x * unit_z)
        + c_three * 3.0 * unit_y * along_torque
        + spin_self * torque_y
    )
    spin_z = (
        c_two * (force_x * unit_y - force_y * unit_x)
        + c_three * 3.0 * unit_z * along_torque
        + spin_self * torque_z
    )
    return jnp.stack(
        [
            jnp.sum(vel_x, 0),
            jnp.sum(vel_y, 0),
            jnp.sum(vel_z, 0),
            jnp.sum(spin_x, 0),
            jnp.sum(spin_y, 0),
            jnp.sum(spin_z, 0),
        ]
    )


def split_two(value):
    high = lax.reduce_precision(value, exponent_bits=8, mantissa_bits=7)
    low = value - high
    return jnp.stack([high, low]).astype(jnp.bfloat16)


def scatter_kernel(owner_ref, slot_ref, parts_ref, out_ref):
    slots = slot_ref.shape[0]
    owner = owner_ref[...]
    slot = slot_ref[...]
    for k in range(6):
        total = None
        for p in range(2):
            weighted = slot * parts_ref[p, k : k + 1, :]
            term = lax.dot_general(
                owner, weighted, (((1,), (1,)), ((), ())), preferred_element_type=jnp.float32
            )
            total = term if total is None else total + term
        out_ref[:, 0, k * slots : (k + 1) * slots] = total


def gather_kernel(owner_ref, slot_ref, parts_ref, out_ref):
    slots = slot_ref.shape[0]
    owner = owner_ref[...]
    slot = slot_ref[...].astype(jnp.float32)
    for k in range(6):
        picked = None
        for p in range(2):
            part = parts_ref[p, k * slots : (k + 1) * slots, :]
            term = jnp.dot(part, owner, preferred_element_type=jnp.float32)
            picked = term if picked is None else picked + term
        out_ref[k : k + 1, :] = jnp.sum(picked * slot, axis=0, keepdims=True)


def scatter_forces(owner_t, slot_t, end_force):
    owners, ends = owner_t.shape
    slots = slot_t.shape[0]
    parts = split_two(end_force)
    return pl.pallas_call(
        scatter_kernel,
        out_shape=jax.ShapeDtypeStruct((owners, 1, 6 * slots), jnp.float32),
        cost_estimate=pl.CostEstimate(
            flops=2 * 12 * owners * slots * ends, transcendentals=0, bytes_accessed=4 * ends * 300
        ),
    )(owner_t, slot_t, parts)


def gather_velocity(owner_t, slot_t, table):
    owners, ends = owner_t.shape
    slots = slot_t.shape[0]
    return pl.pallas_call(
        gather_kernel,
        out_shape=jax.ShapeDtypeStruct((6, ends), jnp.float32),
        cost_estimate=pl.CostEstimate(
            flops=2 * 12 * owners * slots * ends, transcendentals=0, bytes_accessed=4 * ends * 300
        ),
    )(owner_t, slot_t, split_two(table))


def split_pair(value):
    high = value.astype(jnp.bfloat16)
    low = (value - high.astype(jnp.float32)).astype(jnp.bfloat16)
    return (high, low)


def contact_kernel(gather, scatter, *refs):
    owner_ref, slot_ref, rows_ref, state_ref = refs[:4]
    refs = refs[4:]
    if gather:
        table_ref, refs = refs[0], refs[1:]
    outs = refs
    slots = slot_ref.shape[0]
    contacts = state_ref.shape[1]
    owner = owner_ref[...]
    slot = slot_ref[...]
    shifted = state_ref[1:2, :]
    if gather:
        slot_wide = slot.astype(jnp.float32)
        rate = None
        for k in range(6):
            picked = None
            for part in split_pair(table_ref[k * slots : (k + 1) * slots, :]):
                term = jnp.dot(part, owner, preferred_element_type=jnp.float32)
                picked = term if picked is None else picked + term
            velocity = jnp.sum(picked * slot_wide, axis=0, keepdims=True)
            term = rows_ref[k : k + 1, :] * velocity
            rate = term if rate is None else rate + term
        normal_rate = rate[:, :contacts] + rate[:, contacts:]
        current = state_ref[0:1, :]
        gaps = state_ref[2:3, :]
        step = state_ref[3:4, :]
        updated = jnp.maximum(shifted - step * (gaps + normal_rate), 0.0)
        shifted = updated + MOMENTUM * (updated - current)
        outs[0][0:1, :] = updated
        outs[0][1:2, :] = shifted
        outs = outs[1:]
    if scatter:
        out_ref = outs[0]
        for k in range(6):
            total = None
            for side in range(2):
                ends = slice(side * contacts, (side + 1) * contacts)
                force = rows_ref[k : k + 1, ends] * shifted
                for part in split_pair(force):
                    weighted = slot[:, ends] * part
                    term = lax.dot_general(
                        owner[:, ends], weighted, (((1,), (1,)), ((), ())),
                        preferred_element_type=jnp.float32,
                    )
                    total = term if total is None else total + term
            out_ref[:, 0, k * slots : (k + 1) * slots] = total


def contact_step(owner_t, slot_t, end_rows, state, table=None, scatter=True):
    owners, ends = owner_t.shape
    slots = slot_t.shape[0]
    contacts = state.shape[1]
    gather = table is not None
    shapes = []
    if gather:
        shapes.append(jax.ShapeDtypeStruct((2, contacts), jnp.float32))
    if scatter:
        shapes.append(jax.ShapeDtypeStruct((owners, 1, 6 * slots), jnp.float32))
    args = (owner_t, slot_t, end_rows, state) + ((table,) if gather else ())
    return pl.pallas_call(
        functools.partial(contact_kernel, gather, scatter),
        out_shape=tuple(shapes),
        cost_estimate=pl.CostEstimate(
            flops=2 * 12 * owners * slots * ends * (int(gather) + int(scatter)),
            transcendentals=0,
            bytes_accessed=4 * ends * 300,
        ),
    )(*args)


def pair_kernel(target_ref, place_ref, force_ref, own_ref, out_ref, sums_ref):
    targets = target_ref.shape[1]
    chunks = place_ref.shape[0]
    first_place = place_ref.shape[2] // 128 - 3

    def group(g, carry):
        rows = pl.ds(pl.multiple_of(g * 8, 8), 8)
        target_x = target_ref[0, rows, :]
        target_y = target_ref[1, rows, :]
        target_z = target_ref[2, rows, :]

        def chunk(j, sums):
            place = place_ref[j]
            force = force_ref[j]

            def lane_row(block, row):
                return block[:, row * 128 : (row + 1) * 128]

            r_x = target_x - lane_row(place, first_place)
            r_y = target_y - lane_row(place, first_place + 1)
            r_z = target_z - lane_row(place, first_place + 2)
            f_x, f_y, f_z = (lane_row(force, 0), lane_row(force, 1), lane_row(force, 2))
            t_x, t_y, t_z = (lane_row(force, 3), lane_row(force, 4), lane_row(force, 5))
            dist_sq = r_x * r_x + r_y * r_y + r_z * r_z
            inverse = jnp.where(dist_sq > 0.0, lax.rsqrt(dist_sq), 0.0)
            inverse_sq = inverse * inverse
            inverse_cube = inverse_sq * inverse
            inverse_fifth = inverse_cube * inverse_sq
            c_cross = 0.75 * inverse_cube
            c_iso = 0.75 * inverse + 0.5 * inverse_cube
            c_dyad = c_cross - 1.5 * inverse_fifth
            c_spin = 1.125 * inverse_fifth
            c_self = 0.375 * inverse_cube
            dyad = c_dyad * (r_x * f_x + r_y * f_y + r_z * f_z)
            spin = c_spin * (r_x * t_x + r_y * t_y + r_z * t_z)
            s_x = c_cross * r_x
            s_y = c_cross * r_y
            s_z = c_cross * r_z
            return (
                sums[0] + (c_iso * f_x + dyad * r_x + (t_y * s_z - t_z * s_y)),
                sums[1] + (c_iso * f_y + dyad * r_y + (t_z * s_x - t_x * s_z)),
                sums[2] + (c_iso * f_z + dyad * r_z + (t_x * s_y - t_y * s_x)),
                sums[3] + ((f_y * s_z - f_z * s_y) + spin * r_x - c_self * t_x),
                sums[4] + ((f_z * s_x - f_x * s_z) + spin * r_y - c_self * t_y),
                sums[5] + ((f_x * s_y - f_y * s_x) + spin * r_z - c_self * t_z),
            )

        zero = jnp.zeros((8, 128), jnp.float32)
        sums = lax.fori_loop(0, chunks, chunk, (zero,) * 6, unroll=32)
        for k in range(6):
            sums_ref[k, rows, :] = sums[k]
        return carry

    lax.fori_loop(0, targets // 8, group, 0)
    ones = jnp.ones((8, 128), jnp.bfloat16)
    for k in range(6):
        value = sums_ref[k]
        high = value.astype(jnp.bfloat16)
        rest = value - high.astype(jnp.float32)
        middle = rest.astype(jnp.bfloat16)
        low = (rest - middle.astype(jnp.float32)).astype(jnp.bfloat16)
        total = None
        for part in (high, middle, low):
            term = lax.dot_general(
                ones, part, (((1,), (1,)), ((), ())), preferred_element_type=jnp.float32
            )
            total = term if total is None else total + term
        scale = 1.0 if k < 3 else 0.75
        out_ref[k : k + 1, :] = total[0:1, :] + scale * own_ref[k : k + 1, :]


def mobility_own(spread, places, forces, own_forces):
    own_rows = own_forces.shape[1]
    sources = places.shape[0] * 128
    return pl.pallas_call(
        pair_kernel,
        out_shape=jax.ShapeDtypeStruct((6, own_rows), jnp.float32),
        scratch_shapes=[pltpu.VMEM((6, own_rows, 128), jnp.float32)],
        cost_estimate=pl.CostEstimate(
            flops=90 * own_rows * sources,
            transcendentals=own_rows * sources,
            bytes_accessed=4 * (9 * sources + 3 * own_rows * 128),
        ),
    )(spread, places, forces, own_forces)

def gather_all(block, devices):
    rows, width = block.shape
    spread = jnp.broadcast_to(block[None], (devices, rows, width))
    spread = lax.all_to_all(spread, AXES, 0, 0, tiled=True)
    return spread.transpose(1, 0, 2).reshape(rows, devices * width)


def scatter_sum(full, devices):
    rows, length = full.shape
    width = length // devices
    pieces = full.reshape(rows, devices, width).transpose(1, 0, 2)
    pieces = lax.all_to_all(pieces, AXES, 0, 0, tiled=True)
    return jnp.sum(pieces, 0)


def per_device(
    positions, contact_bodies, contact_frame, gaps, impulse_now, impulse_prev, step_sizes
):
    devices = lax.axis_size("src") * lax.axis_size("tgt")
    me = lax.axis_index("src") * lax.axis_size("tgt") + lax.axis_index("tgt")
    own_rows = positions.shape[1]
    body_count = own_rows * devices
    first_rows, second_rows = contact_rows(contact_frame)
    contacts = contact_bodies.shape[1]
    end_bodies = jnp.concatenate([contact_bodies[0], contact_bodies[1]])
    end_rows = jnp.concatenate([first_rows, second_rows], axis=1)
    owner_t = (
        jnp.arange(devices, dtype=jnp.int32)[:, None] == (end_bodies // own_rows)[None, :]
    ).astype(jnp.bfloat16)
    slot_t = (
        jnp.arange(own_rows, dtype=jnp.int32)[:, None] == (end_bodies % own_rows)[None, :]
    ).astype(jnp.bfloat16)
    spread = jnp.broadcast_to(positions[:, :, None], (3, own_rows, 128))
    shifted = impulse_now + MOMENTUM * (impulse_now - impulse_prev)
    state = jnp.stack([impulse_now, shifted, gaps, jnp.broadcast_to(step_sizes[0], gaps.shape)])
    (pieces,) = contact_step(owner_t, slot_t, end_rows, state)
    own_velocity = jnp.zeros((6, own_rows), jnp.float32)
    for k in range(ITERS):
        pieces = lax.all_to_all(pieces, AXES, 0, 0, tiled=True)
        own_forces = jnp.sum(pieces, 0).reshape(6, own_rows)
        if k == 0:
            block = jnp.concatenate([own_forces, positions]).reshape(1, 1, 9 * own_rows)
            places = lax.all_to_all(
                jnp.broadcast_to(block, (devices, 1, 9 * own_rows)), AXES, 0, 0, tiled=True
            )
            forces = places
        else:
            block = own_forces.reshape(1, 1, 6 * own_rows)
            forces = lax.all_to_all(
                jnp.broadcast_to(block, (devices, 1, 6 * own_rows)), AXES, 0, 0, tiled=True
            )
        own_velocity = mobility_own(spread, places, forces, own_forces)
        every = jnp.broadcast_to(own_velocity.reshape(1, 6 * own_rows), (devices, 6 * own_rows))
        every = lax.all_to_all(every, AXES, 0, 0, tiled=True)
        state = jnp.concatenate(
            [state[:3], jnp.broadcast_to(step_sizes[k], (1,) + gaps.shape)]
        )
        last = k == ITERS - 1
        result = contact_step(owner_t, slot_t, end_rows, state, every.T, scatter=not last)
        state = jnp.concatenate([result[0], state[2:]])
        if not last:
            pieces = result[1]
    current = state[0]
    return (current, own_velocity)


def solution(mesh):
    placed = (
        P(None, AXES),
        P(None, AXES),
        P(None, AXES),
        P(AXES),
        P(AXES),
        P(AXES),
        P(),
    )
    return jax.shard_map(
        per_device,
        mesh=mesh,
        in_specs=placed,
        out_specs=(P(AXES), P(None, AXES)),
        check_vma=False,
    )
```

```python
import functools

import jax
import jax.numpy as jnp
from jax import lax
from jax.experimental import pallas as pl
from jax.experimental.pallas import tpu as pltpu
from jax.sharding import PartitionSpec as P

ITERS = 2
MOMENTUM = 0.4
AXES = ("src", "tgt")
SOURCE_BLOCK = 1024


def cross_product(first, second):
    return jnp.stack(
        [
            first[1] * second[2] - first[2] * second[1],
            first[2] * second[0] - first[0] * second[2],
            first[0] * second[1] - first[1] * second[0],
        ]
    )


def contact_rows(frame):
    normal = frame[0:3]
    lever_first = cross_product(frame[3:6], normal)
    lever_second = cross_product(frame[6:9], normal)
    return (jnp.concatenate([-normal, -lever_first]), jnp.concatenate([normal, lever_second]))


def pair_block(target_pos, target_ids, source_pos, source_ids, forces):
    delta_x = target_pos[0][None, :] - source_pos[0][:, None]
    delta_y = target_pos[1][None, :] - source_pos[1][:, None]
    delta_z = target_pos[2][None, :] - source_pos[2][:, None]
    coincide = target_ids[None, :] == source_ids[:, None]
    dist_sq = jnp.where(coincide, 1.0, delta_x * delta_x + delta_y * delta_y + delta_z * delta_z)
    inverse = jnp.where(coincide, 0.0, lax.rsqrt(dist_sq))
    self_term = jnp.where(coincide, 1.0, 0.0)
    unit_x = delta_x * inverse
    unit_y = delta_y * inverse
    unit_z = delta_z * inverse
    force_x, force_y, force_z = (forces[0][:, None], forces[1][:, None], forces[2][:, None])
    torque_x, torque_y, torque_z = (forces[3][:, None], forces[4][:, None], forces[5][:, None])
    inverse_sq = inverse * inverse
    c_one = 0.75 * inverse
    c_two = 0.75 * inverse_sq
    c_three = 0.375 * inverse_sq * inverse
    along_force = unit_x * force_x + unit_y * force_y + unit_z * force_z
    along_torque = unit_x * torque_x + unit_y * torque_y + unit_z * torque_z
    isotropic = c_one * (1.0 + inverse_sq * (2.0 / 3.0)) + self_term
    dyadic = c_one * (1.0 - 2.0 * inverse_sq) * along_force
    vel_x = isotropic * force_x + dyadic * unit_x + c_two * (torque_y * unit_z - torque_z * unit_y)
    vel_y = isotropic * force_y + dyadic * unit_y + c_two * (torque_z * unit_x - torque_x * unit_z)
    vel_z = isotropic * force_z + dyadic * unit_z + c_two * (torque_x * unit_y - torque_y * unit_x)
    spin_self = 0.75 * self_term - c_three
    spin_x = (
        c_two * (force_y * unit_z - force_z * unit_y)
        + c_three * 3.0 * unit_x * along_torque
        + spin_self * torque_x
    )
    spin_y = (
        c_two * (force_z * unit_x - force_x * unit_z)
        + c_three * 3.0 * unit_y * along_torque
        + spin_self * torque_y
    )
    spin_z = (
        c_two * (force_x * unit_y - force_y * unit_x)
        + c_three * 3.0 * unit_z * along_torque
        + spin_self * torque_z
    )
    return jnp.stack(
        [
            jnp.sum(vel_x, 0),
            jnp.sum(vel_y, 0),
            jnp.sum(vel_z, 0),
            jnp.sum(spin_x, 0),
            jnp.sum(spin_y, 0),
            jnp.sum(spin_z, 0),
        ]
    )


def split_two(value):
    high = lax.reduce_precision(value, exponent_bits=8, mantissa_bits=7)
    low = value - high
    return jnp.stack([high, low]).astype(jnp.bfloat16)


def scatter_kernel(owner_ref, slot_ref, parts_ref, out_ref):
    slots = slot_ref.shape[0]
    owner = owner_ref[...]
    slot = slot_ref[...]
    for k in range(6):
        total = None
        for p in range(2):
            weighted = slot * parts_ref[p, k : k + 1, :]
            term = lax.dot_general(
                owner, weighted, (((1,), (1,)), ((), ())), preferred_element_type=jnp.float32
            )
            total = term if total is None else total + term
        out_ref[:, 0, k * slots : (k + 1) * slots] = total


def gather_kernel(owner_ref, slot_ref, parts_ref, out_ref):
    slots = slot_ref.shape[0]
    owner = owner_ref[...]
    slot = slot_ref[...].astype(jnp.float32)
    for k in range(6):
        picked = None
        for p in range(2):
            part = parts_ref[p, k * slots : (k + 1) * slots, :]
            term = jnp.dot(part, owner, preferred_element_type=jnp.float32)
            picked = term if picked is None else picked + term
        out_ref[k : k + 1, :] = jnp.sum(picked * slot, axis=0, keepdims=True)


def scatter_forces(owner_t, slot_t, end_force):
    owners, ends = owner_t.shape
    slots = slot_t.shape[0]
    parts = split_two(end_force)
    return pl.pallas_call(
        scatter_kernel,
        out_shape=jax.ShapeDtypeStruct((owners, 1, 6 * slots), jnp.float32),
        cost_estimate=pl.CostEstimate(
            flops=2 * 12 * owners * slots * ends, transcendentals=0, bytes_accessed=4 * ends * 300
        ),
    )(owner_t, slot_t, parts)


def gather_velocity(owner_t, slot_t, table):
    owners, ends = owner_t.shape
    slots = slot_t.shape[0]
    return pl.pallas_call(
        gather_kernel,
        out_shape=jax.ShapeDtypeStruct((6, ends), jnp.float32),
        cost_estimate=pl.CostEstimate(
            flops=2 * 12 * owners * slots * ends, transcendentals=0, bytes_accessed=4 * ends * 300
        ),
    )(owner_t, slot_t, split_two(table))


def split_pair(value):
    high = value.astype(jnp.bfloat16)
    low = (value - high.astype(jnp.float32)).astype(jnp.bfloat16)
    return (high, low)


def contact_kernel(step, gather, scatter, *refs):
    bodies_ref, frame_ref, state_ref, gaps_ref, steps_ref = refs[:5]
    refs = refs[5:]
    if gather:
        table_ref, refs = refs[0], refs[1:]
    outs = refs
    contacts = frame_ref.shape[1]
    owners = outs[-1].shape[0] if scatter else table_ref.shape[1]
    slots = outs[-1].shape[2] // 6 if scatter else table_ref.shape[0] // 6
    frame = frame_ref[...]
    normal = (frame[0:1], frame[1:2], frame[2:3])

    def crossed(arm):
        return (
            arm[1] * normal[2] - arm[2] * normal[1],
            arm[2] * normal[0] - arm[0] * normal[2],
            arm[0] * normal[1] - arm[1] * normal[0],
        )

    first_lever = crossed((frame[3:4], frame[4:5], frame[5:6]))
    second_lever = crossed((frame[6:7], frame[7:8], frame[8:9]))
    rows = (
        tuple(-v for v in normal) + tuple(-v for v in first_lever),
        normal + second_lever,
    )
    owner_ids = lax.broadcasted_iota(jnp.int32, (owners, contacts), 0)
    slot_ids = lax.broadcasted_iota(jnp.int32, (slots, contacts), 0)
    owner_hot, slot_hot = [], []
    for side in range(2):
        body = bodies_ref[side : side + 1, :]
        owner_hot.append((owner_ids == body // slots).astype(jnp.bfloat16))
        slot_hot.append((slot_ids == body % slots).astype(jnp.bfloat16))
    current = state_ref[0:1, :]
    if step == 0:
        shifted = current + MOMENTUM * (current - state_ref[1:2, :])
    else:
        shifted = state_ref[1:2, :]
    if gather:
        rate = None
        for side in range(2):
            slot_wide = slot_hot[side].astype(jnp.float32)
            for k in range(6):
                picked = None
                for part in split_pair(table_ref[k * slots : (k + 1) * slots, :]):
                    term = jnp.dot(part, owner_hot[side], preferred_element_type=jnp.float32)
                    picked = term if picked is None else picked + term
                velocity = jnp.sum(picked * slot_wide, axis=0, keepdims=True)
                term = rows[side][k] * velocity
                rate = term if rate is None else rate + term
        updated = jnp.maximum(shifted - steps_ref[step] * (gaps_ref[...] + rate), 0.0)
        shifted = updated + MOMENTUM * (updated - current)
        outs[0][0:1, :] = updated
        outs[0][1:2, :] = shifted
        outs = outs[1:]
    if scatter:
        out_ref = outs[0]
        for k in range(6):
            total = None
            for side in range(2):
                for part in split_pair(rows[side][k] * shifted):
                    weighted = slot_hot[side] * part
                    term = lax.dot_general(
                        owner_hot[side], weighted, (((1,), (1,)), ((), ())),
                        preferred_element_type=jnp.float32,
                    )
                    total = term if total is None else total + term
            out_ref[:, 0, k * slots : (k + 1) * slots] = total


def contact_step(step, owners, slots, bodies, frame, state, gaps, steps, table=None, scatter=True):
    contacts = frame.shape[1]
    gather = table is not None
    shapes = []
    if gather:
        shapes.append(jax.ShapeDtypeStruct((2, contacts), jnp.float32))
    if scatter:
        shapes.append(jax.ShapeDtypeStruct((owners, 1, 6 * slots), jnp.float32))
    args = (bodies, frame, state, gaps, steps) + ((table,) if gather else ())
    vmem = pl.BlockSpec(memory_space=pltpu.VMEM)
    specs = [vmem, vmem, vmem, vmem, pl.BlockSpec(memory_space=pltpu.SMEM)] + [vmem] * int(gather)
    return pl.pallas_call(
        functools.partial(contact_kernel, step, gather, scatter),
        out_shape=tuple(shapes),
        in_specs=specs,
        out_specs=tuple(vmem for _ in shapes),
        cost_estimate=pl.CostEstimate(
            flops=2 * 12 * owners * slots * 2 * contacts * (int(gather) + int(scatter)),
            transcendentals=0,
            bytes_accessed=4 * contacts * 600,
        ),
    )(*args)

def pair_kernel(target_ref, place_ref, force_ref, own_ref, out_ref, sums_ref):
    targets = target_ref.shape[1]
    chunks = place_ref.shape[0]
    first_place = place_ref.shape[2] // 128 - 3

    def group(g, carry):
        rows = pl.ds(pl.multiple_of(g * 8, 8), 8)
        target_x = target_ref[0, rows, :]
        target_y = target_ref[1, rows, :]
        target_z = target_ref[2, rows, :]

        def chunk(j, sums):
            place = place_ref[j]
            force = force_ref[j]

            def lane_row(block, row):
                return block[:, row * 128 : (row + 1) * 128]

            r_x = target_x - lane_row(place, first_place)
            r_y = target_y - lane_row(place, first_place + 1)
            r_z = target_z - lane_row(place, first_place + 2)
            f_x, f_y, f_z = (lane_row(force, 0), lane_row(force, 1), lane_row(force, 2))
            t_x, t_y, t_z = (lane_row(force, 3), lane_row(force, 4), lane_row(force, 5))
            dist_sq = r_x * r_x + r_y * r_y + r_z * r_z
            inverse = jnp.where(dist_sq > 0.0, lax.rsqrt(dist_sq), 0.0)
            inverse_sq = inverse * inverse
            inverse_cube = inverse_sq * inverse
            inverse_fifth = inverse_cube * inverse_sq
            c_cross = 0.75 * inverse_cube
            c_iso = 0.75 * inverse + 0.5 * inverse_cube
            c_dyad = c_cross - 1.5 * inverse_fifth
            c_spin = 1.125 * inverse_fifth
            c_self = 0.375 * inverse_cube
            dyad = c_dyad * (r_x * f_x + r_y * f_y + r_z * f_z)
            spin = c_spin * (r_x * t_x + r_y * t_y + r_z * t_z)
            s_x = c_cross * r_x
            s_y = c_cross * r_y
            s_z = c_cross * r_z
            return (
                sums[0] + (c_iso * f_x + dyad * r_x + (t_y * s_z - t_z * s_y)),
                sums[1] + (c_iso * f_y + dyad * r_y + (t_z * s_x - t_x * s_z)),
                sums[2] + (c_iso * f_z + dyad * r_z + (t_x * s_y - t_y * s_x)),
                sums[3] + ((f_y * s_z - f_z * s_y) + spin * r_x - c_self * t_x),
                sums[4] + ((f_z * s_x - f_x * s_z) + spin * r_y - c_self * t_y),
                sums[5] + ((f_x * s_y - f_y * s_x) + spin * r_z - c_self * t_z),
            )

        zero = jnp.zeros((8, 128), jnp.float32)
        sums = lax.fori_loop(0, chunks, chunk, (zero,) * 6, unroll=32)
        for k in range(6):
            sums_ref[k, rows, :] = sums[k]
        return carry

    lax.fori_loop(0, targets // 8, group, 0)
    ones = jnp.ones((8, 128), jnp.bfloat16)
    for k in range(6):
        value = sums_ref[k]
        high = value.astype(jnp.bfloat16)
        rest = value - high.astype(jnp.float32)
        middle = rest.astype(jnp.bfloat16)
        low = (rest - middle.astype(jnp.float32)).astype(jnp.bfloat16)
        total = None
        for part in (high, middle, low):
            term = lax.dot_general(
                ones, part, (((1,), (1,)), ((), ())), preferred_element_type=jnp.float32
            )
            total = term if total is None else total + term
        scale = 1.0 if k < 3 else 0.75
        out_ref[k : k + 1, :] = total[0:1, :] + scale * own_ref[k : k + 1, :]


def mobility_own(spread, places, forces, own_forces):
    own_rows = own_forces.shape[1]
    sources = places.shape[0] * 128
    return pl.pallas_call(
        pair_kernel,
        out_shape=jax.ShapeDtypeStruct((6, own_rows), jnp.float32),
        scratch_shapes=[pltpu.VMEM((6, own_rows, 128), jnp.float32)],
        cost_estimate=pl.CostEstimate(
            flops=90 * own_rows * sources,
            transcendentals=own_rows * sources,
            bytes_accessed=4 * (9 * sources + 3 * own_rows * 128),
        ),
    )(spread, places, forces, own_forces)

def gather_all(block, devices):
    rows, width = block.shape
    spread = jnp.broadcast_to(block[None], (devices, rows, width))
    spread = lax.all_to_all(spread, AXES, 0, 0, tiled=True)
    return spread.transpose(1, 0, 2).reshape(rows, devices * width)


def scatter_sum(full, devices):
    rows, length = full.shape
    width = length // devices
    pieces = full.reshape(rows, devices, width).transpose(1, 0, 2)
    pieces = lax.all_to_all(pieces, AXES, 0, 0, tiled=True)
    return jnp.sum(pieces, 0)


def per_device(
    positions, contact_bodies, contact_frame, gaps, impulse_now, impulse_prev, step_sizes
):
    devices = lax.axis_size("src") * lax.axis_size("tgt")
    me = lax.axis_index("src") * lax.axis_size("tgt") + lax.axis_index("tgt")
    own_rows = positions.shape[1]
    body_count = own_rows * devices
    spread = jnp.broadcast_to(positions[:, :, None], (3, own_rows, 128))
    gaps_row = gaps.reshape(1, -1)
    state = jnp.stack([impulse_now, impulse_prev])
    (pieces,) = contact_step(0, devices, own_rows, contact_bodies, contact_frame, state, gaps_row, step_sizes)
    own_velocity = jnp.zeros((6, own_rows), jnp.float32)
    for k in range(ITERS):
        pieces = lax.all_to_all(pieces, AXES, 0, 0, tiled=True)
        own_forces = jnp.sum(pieces, 0).reshape(6, own_rows)
        if k == 0:
            block = jnp.concatenate([own_forces, positions]).reshape(1, 1, 9 * own_rows)
            places = lax.all_to_all(
                jnp.broadcast_to(block, (devices, 1, 9 * own_rows)), AXES, 0, 0, tiled=True
            )
            forces = places
        else:
            block = own_forces.reshape(1, 1, 6 * own_rows)
            forces = lax.all_to_all(
                jnp.broadcast_to(block, (devices, 1, 6 * own_rows)), AXES, 0, 0, tiled=True
            )
        own_velocity = mobility_own(spread, places, forces, own_forces)
        every = jnp.broadcast_to(own_velocity.reshape(1, 6 * own_rows), (devices, 6 * own_rows))
        every = lax.all_to_all(every, AXES, 0, 0, tiled=True)
        last = k == ITERS - 1
        result = contact_step(
            k, devices, own_rows, contact_bodies, contact_frame, state, gaps_row, step_sizes, every.T, scatter=not last
        )
        state = result[0]
        if not last:
            pieces = result[1]
    current = state[0]
    return (current, own_velocity)


def solution(mesh):
    placed = (
        P(None, AXES),
        P(None, AXES),
        P(None, AXES),
        P(AXES),
        P(AXES),
        P(AXES),
        P(),
    )
    return jax.shard_map(
        per_device,
        mesh=mesh,
        in_specs=placed,
        out_specs=(P(AXES), P(None, AXES)),
        check_vma=False,
    )
```

```python
import functools

import jax
import jax.numpy as jnp
from jax import lax
from jax.experimental import pallas as pl
from jax.experimental.pallas import tpu as pltpu
from jax.sharding import PartitionSpec as P

ITERS = 2
MOMENTUM = 0.4
AXES = ("src", "tgt")
SOURCE_BLOCK = 1024


def cross_product(first, second):
    return jnp.stack(
        [
            first[1] * second[2] - first[2] * second[1],
            first[2] * second[0] - first[0] * second[2],
            first[0] * second[1] - first[1] * second[0],
        ]
    )


def contact_rows(frame):
    normal = frame[0:3]
    lever_first = cross_product(frame[3:6], normal)
    lever_second = cross_product(frame[6:9], normal)
    return (jnp.concatenate([-normal, -lever_first]), jnp.concatenate([normal, lever_second]))


def pair_block(target_pos, target_ids, source_pos, source_ids, forces):
    delta_x = target_pos[0][None, :] - source_pos[0][:, None]
    delta_y = target_pos[1][None, :] - source_pos[1][:, None]
    delta_z = target_pos[2][None, :] - source_pos[2][:, None]
    coincide = target_ids[None, :] == source_ids[:, None]
    dist_sq = jnp.where(coincide, 1.0, delta_x * delta_x + delta_y * delta_y + delta_z * delta_z)
    inverse = jnp.where(coincide, 0.0, lax.rsqrt(dist_sq))
    self_term = jnp.where(coincide, 1.0, 0.0)
    unit_x = delta_x * inverse
    unit_y = delta_y * inverse
    unit_z = delta_z * inverse
    force_x, force_y, force_z = (forces[0][:, None], forces[1][:, None], forces[2][:, None])
    torque_x, torque_y, torque_z = (forces[3][:, None], forces[4][:, None], forces[5][:, None])
    inverse_sq = inverse * inverse
    c_one = 0.75 * inverse
    c_two = 0.75 * inverse_sq
    c_three = 0.375 * inverse_sq * inverse
    along_force = unit_x * force_x + unit_y * force_y + unit_z * force_z
    along_torque = unit_x * torque_x + unit_y * torque_y + unit_z * torque_z
    isotropic = c_one * (1.0 + inverse_sq * (2.0 / 3.0)) + self_term
    dyadic = c_one * (1.0 - 2.0 * inverse_sq) * along_force
    vel_x = isotropic * force_x + dyadic * unit_x + c_two * (torque_y * unit_z - torque_z * unit_y)
    vel_y = isotropic * force_y + dyadic * unit_y + c_two * (torque_z * unit_x - torque_x * unit_z)
    vel_z = isotropic * force_z + dyadic * unit_z + c_two * (torque_x * unit_y - torque_y * unit_x)
    spin_self = 0.75 * self_term - c_three
    spin_x = (
        c_two * (force_y * unit_z - force_z * unit_y)
        + c_three * 3.0 * unit_x * along_torque
        + spin_self * torque_x
    )
    spin_y = (
        c_two * (force_z * unit_x - force_x * unit_z)
        + c_three * 3.0 * unit_y * along_torque
        + spin_self * torque_y
    )
    spin_z = (
        c_two * (force_x * unit_y - force_y * unit_x)
        + c_three * 3.0 * unit_z * along_torque
        + spin_self * torque_z
    )
    return jnp.stack(
        [
            jnp.sum(vel_x, 0),
            jnp.sum(vel_y, 0),
            jnp.sum(vel_z, 0),
            jnp.sum(spin_x, 0),
            jnp.sum(spin_y, 0),
            jnp.sum(spin_z, 0),
        ]
    )


def split_two(value):
    high = lax.reduce_precision(value, exponent_bits=8, mantissa_bits=7)
    low = value - high
    return jnp.stack([high, low]).astype(jnp.bfloat16)


def scatter_kernel(owner_ref, slot_ref, parts_ref, out_ref):
    slots = slot_ref.shape[0]
    owner = owner_ref[...]
    slot = slot_ref[...]
    for k in range(6):
        total = None
        for p in range(2):
            weighted = slot * parts_ref[p, k : k + 1, :]
            term = lax.dot_general(
                owner, weighted, (((1,), (1,)), ((), ())), preferred_element_type=jnp.float32
            )
            total = term if total is None else total + term
        out_ref[:, 0, k * slots : (k + 1) * slots] = total


def gather_kernel(owner_ref, slot_ref, parts_ref, out_ref):
    slots = slot_ref.shape[0]
    owner = owner_ref[...]
    slot = slot_ref[...].astype(jnp.float32)
    for k in range(6):
        picked = None
        for p in range(2):
            part = parts_ref[p, k * slots : (k + 1) * slots, :]
            term = jnp.dot(part, owner, preferred_element_type=jnp.float32)
            picked = term if picked is None else picked + term
        out_ref[k : k + 1, :] = jnp.sum(picked * slot, axis=0, keepdims=True)


def scatter_forces(owner_t, slot_t, end_force):
    owners, ends = owner_t.shape
    slots = slot_t.shape[0]
    parts = split_two(end_force)
    return pl.pallas_call(
        scatter_kernel,
        out_shape=jax.ShapeDtypeStruct((owners, 1, 6 * slots), jnp.float32),
        cost_estimate=pl.CostEstimate(
            flops=2 * 12 * owners * slots * ends, transcendentals=0, bytes_accessed=4 * ends * 300
        ),
    )(owner_t, slot_t, parts)


def gather_velocity(owner_t, slot_t, table):
    owners, ends = owner_t.shape
    slots = slot_t.shape[0]
    return pl.pallas_call(
        gather_kernel,
        out_shape=jax.ShapeDtypeStruct((6, ends), jnp.float32),
        cost_estimate=pl.CostEstimate(
            flops=2 * 12 * owners * slots * ends, transcendentals=0, bytes_accessed=4 * ends * 300
        ),
    )(owner_t, slot_t, split_two(table))


def split_pair(value):
    high = value.astype(jnp.bfloat16)
    low = (value - high.astype(jnp.float32)).astype(jnp.bfloat16)
    return (high, low)


def contact_kernel(step, gather, scatter, *refs):
    bodies_ref, frame_ref, current_ref, other_ref, gaps_ref, steps_ref = refs[:6]
    refs = refs[6:]
    if gather:
        table_ref, refs = refs[0], refs[1:]
    outs = refs
    contacts = frame_ref.shape[1]
    owners = outs[-1].shape[0] if scatter else table_ref.shape[1]
    slots = outs[-1].shape[2] // 6 if scatter else table_ref.shape[0] // 6
    frame = frame_ref[...]
    normal = (frame[0:1], frame[1:2], frame[2:3])

    def crossed(arm):
        return (
            arm[1] * normal[2] - arm[2] * normal[1],
            arm[2] * normal[0] - arm[0] * normal[2],
            arm[0] * normal[1] - arm[1] * normal[0],
        )

    first_lever = crossed((frame[3:4], frame[4:5], frame[5:6]))
    second_lever = crossed((frame[6:7], frame[7:8], frame[8:9]))
    rows = (
        tuple(-v for v in normal) + tuple(-v for v in first_lever),
        normal + second_lever,
    )
    owner_ids = lax.broadcasted_iota(jnp.int32, (owners, contacts), 0)
    slot_ids = lax.broadcasted_iota(jnp.int32, (slots, contacts), 0)
    owner_hot, slot_hot = [], []
    for side in range(2):
        body = bodies_ref[side : side + 1, :]
        owner_hot.append((owner_ids == body // slots).astype(jnp.bfloat16))
        slot_hot.append((slot_ids == body % slots).astype(jnp.bfloat16))
    current = current_ref[...]
    if step == 0:
        shifted = current + MOMENTUM * (current - other_ref[...])
    else:
        shifted = other_ref[...]
    if gather:
        rate = None
        for side in range(2):
            slot_wide = slot_hot[side].astype(jnp.float32)
            for k in range(6):
                picked = None
                for part in split_pair(table_ref[k * slots : (k + 1) * slots, :]):
                    term = jnp.dot(part, owner_hot[side], preferred_element_type=jnp.float32)
                    picked = term if picked is None else picked + term
                velocity = jnp.sum(picked * slot_wide, axis=0, keepdims=True)
                term = rows[side][k] * velocity
                rate = term if rate is None else rate + term
        updated = jnp.maximum(shifted - steps_ref[step] * (gaps_ref[...] + rate), 0.0)
        shifted = updated + MOMENTUM * (updated - current)
        outs[0][...] = updated
        if scatter:
            outs[1][...] = shifted
        outs = outs[1 + int(scatter):]
    if scatter:
        out_ref = outs[0]
        for k in range(6):
            total = None
            for side in range(2):
                for part in split_pair(rows[side][k] * shifted):
                    weighted = slot_hot[side] * part
                    term = lax.dot_general(
                        owner_hot[side], weighted, (((1,), (1,)), ((), ())),
                        preferred_element_type=jnp.float32,
                    )
                    total = term if total is None else total + term
            out_ref[:, 0, k * slots : (k + 1) * slots] = total


def contact_step(step, owners, slots, bodies, frame, state, gaps, steps, table=None, scatter=True):
    contacts = frame.shape[1]
    gather = table is not None
    shapes = []
    if gather:
        shapes += [jax.ShapeDtypeStruct((1, contacts), jnp.float32)] * (1 + int(scatter))
    if scatter:
        shapes.append(jax.ShapeDtypeStruct((owners, 1, 6 * slots), jnp.float32))
    args = (bodies, frame) + tuple(state) + (gaps, steps) + ((table,) if gather else ())
    vmem = pl.BlockSpec(memory_space=pltpu.VMEM)
    specs = [vmem] * 5 + [pl.BlockSpec(memory_space=pltpu.SMEM)] + [vmem] * int(gather)
    return pl.pallas_call(
        functools.partial(contact_kernel, step, gather, scatter),
        out_shape=tuple(shapes),
        in_specs=specs,
        out_specs=tuple(vmem for _ in shapes),
        cost_estimate=pl.CostEstimate(
            flops=2 * 12 * owners * slots * 2 * contacts * (int(gather) + int(scatter)),
            transcendentals=0,
            bytes_accessed=4 * contacts * 600,
        ),
    )(*args)

def pair_kernel(target_ref, place_ref, force_ref, own_ref, out_ref, sums_ref):
    targets = target_ref.shape[1]
    chunks = place_ref.shape[0]
    first_place = place_ref.shape[2] // 128 - 3

    def group(g, carry):
        rows = pl.ds(pl.multiple_of(g * 8, 8), 8)
        target_x = target_ref[0, rows, :]
        target_y = target_ref[1, rows, :]
        target_z = target_ref[2, rows, :]

        def chunk(j, sums):
            place = place_ref[j]
            force = force_ref[j]

            def lane_row(block, row):
                return block[:, row * 128 : (row + 1) * 128]

            r_x = target_x - lane_row(place, first_place)
            r_y = target_y - lane_row(place, first_place + 1)
            r_z = target_z - lane_row(place, first_place + 2)
            f_x, f_y, f_z = (lane_row(force, 0), lane_row(force, 1), lane_row(force, 2))
            t_x, t_y, t_z = (lane_row(force, 3), lane_row(force, 4), lane_row(force, 5))
            dist_sq = r_x * r_x + r_y * r_y + r_z * r_z
            inverse = jnp.where(dist_sq > 0.0, lax.rsqrt(dist_sq), 0.0)
            inverse_sq = inverse * inverse
            inverse_cube = inverse_sq * inverse
            inverse_fifth = inverse_cube * inverse_sq
            c_cross = 0.75 * inverse_cube
            c_iso = 0.75 * inverse + 0.5 * inverse_cube
            c_dyad = c_cross - 1.5 * inverse_fifth
            c_spin = 1.125 * inverse_fifth
            c_self = 0.375 * inverse_cube
            dyad = c_dyad * (r_x * f_x + r_y * f_y + r_z * f_z)
            spin = c_spin * (r_x * t_x + r_y * t_y + r_z * t_z)
            s_x = c_cross * r_x
            s_y = c_cross * r_y
            s_z = c_cross * r_z
            return (
                sums[0] + (c_iso * f_x + dyad * r_x + (t_y * s_z - t_z * s_y)),
                sums[1] + (c_iso * f_y + dyad * r_y + (t_z * s_x - t_x * s_z)),
                sums[2] + (c_iso * f_z + dyad * r_z + (t_x * s_y - t_y * s_x)),
                sums[3] + ((f_y * s_z - f_z * s_y) + spin * r_x - c_self * t_x),
                sums[4] + ((f_z * s_x - f_x * s_z) + spin * r_y - c_self * t_y),
                sums[5] + ((f_x * s_y - f_y * s_x) + spin * r_z - c_self * t_z),
            )

        zero = jnp.zeros((8, 128), jnp.float32)
        sums = lax.fori_loop(0, chunks, chunk, (zero,) * 6, unroll=32)
        for k in range(6):
            sums_ref[k, rows, :] = sums[k]
        return carry

    lax.fori_loop(0, targets // 8, group, 0)
    ones = jnp.ones((8, 128), jnp.bfloat16)
    for k in range(6):
        value = sums_ref[k]
        high = value.astype(jnp.bfloat16)
        rest = value - high.astype(jnp.float32)
        middle = rest.astype(jnp.bfloat16)
        low = (rest - middle.astype(jnp.float32)).astype(jnp.bfloat16)
        total = None
        for part in (high, middle, low):
            term = lax.dot_general(
                ones, part, (((1,), (1,)), ((), ())), preferred_element_type=jnp.float32
            )
            total = term if total is None else total + term
        scale = 1.0 if k < 3 else 0.75
        out_ref[k : k + 1, :] = total[0:1, :] + scale * own_ref[k : k + 1, :]


def mobility_own(spread, places, forces, own_forces):
    own_rows = own_forces.shape[1]
    sources = places.shape[0] * 128
    return pl.pallas_call(
        pair_kernel,
        out_shape=jax.ShapeDtypeStruct((6, own_rows), jnp.float32),
        scratch_shapes=[pltpu.VMEM((6, own_rows, 128), jnp.float32)],
        cost_estimate=pl.CostEstimate(
            flops=90 * own_rows * sources,
            transcendentals=own_rows * sources,
            bytes_accessed=4 * (9 * sources + 3 * own_rows * 128),
        ),
    )(spread, places, forces, own_forces)

def gather_all(block, devices):
    rows, width = block.shape
    spread = jnp.broadcast_to(block[None], (devices, rows, width))
    spread = lax.all_to_all(spread, AXES, 0, 0, tiled=True)
    return spread.transpose(1, 0, 2).reshape(rows, devices * width)


def scatter_sum(full, devices):
    rows, length = full.shape
    width = length // devices
    pieces = full.reshape(rows, devices, width).transpose(1, 0, 2)
    pieces = lax.all_to_all(pieces, AXES, 0, 0, tiled=True)
    return jnp.sum(pieces, 0)


def per_device(
    positions, contact_bodies, contact_frame, gaps, impulse_now, impulse_prev, step_sizes
):
    devices = lax.axis_size("src") * lax.axis_size("tgt")
    me = lax.axis_index("src") * lax.axis_size("tgt") + lax.axis_index("tgt")
    own_rows = positions.shape[1]
    body_count = own_rows * devices
    spread = jnp.broadcast_to(positions[:, :, None], (3, own_rows, 128))
    gaps_row = gaps.reshape(1, -1)
    state = (impulse_now.reshape(1, -1), impulse_prev.reshape(1, -1))
    (pieces,) = contact_step(0, devices, own_rows, contact_bodies, contact_frame, state, gaps_row, step_sizes)
    own_velocity = jnp.zeros((6, own_rows), jnp.float32)
    for k in range(ITERS):
        pieces = lax.all_to_all(pieces, AXES, 0, 0, tiled=True)
        own_forces = jnp.sum(pieces, 0).reshape(6, own_rows)
        if k == 0:
            block = jnp.concatenate([own_forces, positions]).reshape(1, 1, 9 * own_rows)
            places = lax.all_to_all(
                jnp.broadcast_to(block, (devices, 1, 9 * own_rows)), AXES, 0, 0, tiled=True
            )
            forces = places
        else:
            block = own_forces.reshape(1, 1, 6 * own_rows)
            forces = lax.all_to_all(
                jnp.broadcast_to(block, (devices, 1, 6 * own_rows)), AXES, 0, 0, tiled=True
            )
        own_velocity = mobility_own(spread, places, forces, own_forces)
        every = jnp.broadcast_to(own_velocity.reshape(1, 6 * own_rows), (devices, 6 * own_rows))
        every = lax.all_to_all(every, AXES, 0, 0, tiled=True)
        last = k == ITERS - 1
        result = contact_step(
            k, devices, own_rows, contact_bodies, contact_frame, state, gaps_row, step_sizes, every.T, scatter=not last
        )
        state = result[:2]
        if not last:
            pieces = result[2]
    current = state[0].reshape(-1)
    return (current, own_velocity)


def solution(mesh):
    placed = (
        P(None, AXES),
        P(None, AXES),
        P(None, AXES),
        P(AXES),
        P(AXES),
        P(AXES),
        P(),
    )
    return jax.shard_map(
        per_device,
        mesh=mesh,
        in_specs=placed,
        out_specs=(P(AXES), P(None, AXES)),
        check_vma=False,
    )
```

```python
import functools

import jax
import jax.numpy as jnp
from jax import lax
from jax.experimental import pallas as pl
from jax.experimental.pallas import tpu as pltpu
from jax.sharding import PartitionSpec as P

ITERS = 2
MOMENTUM = 0.4
AXES = ("src", "tgt")
SOURCE_BLOCK = 1024


def cross_product(first, second):
    return jnp.stack(
        [
            first[1] * second[2] - first[2] * second[1],
            first[2] * second[0] - first[0] * second[2],
            first[0] * second[1] - first[1] * second[0],
        ]
    )


def contact_rows(frame):
    normal = frame[0:3]
    lever_first = cross_product(frame[3:6], normal)
    lever_second = cross_product(frame[6:9], normal)
    return (jnp.concatenate([-normal, -lever_first]), jnp.concatenate([normal, lever_second]))


def pair_block(target_pos, target_ids, source_pos, source_ids, forces):
    delta_x = target_pos[0][None, :] - source_pos[0][:, None]
    delta_y = target_pos[1][None, :] - source_pos[1][:, None]
    delta_z = target_pos[2][None, :] - source_pos[2][:, None]
    coincide = target_ids[None, :] == source_ids[:, None]
    dist_sq = jnp.where(coincide, 1.0, delta_x * delta_x + delta_y * delta_y + delta_z * delta_z)
    inverse = jnp.where(coincide, 0.0, lax.rsqrt(dist_sq))
    self_term = jnp.where(coincide, 1.0, 0.0)
    unit_x = delta_x * inverse
    unit_y = delta_y * inverse
    unit_z = delta_z * inverse
    force_x, force_y, force_z = (forces[0][:, None], forces[1][:, None], forces[2][:, None])
    torque_x, torque_y, torque_z = (forces[3][:, None], forces[4][:, None], forces[5][:, None])
    inverse_sq = inverse * inverse
    c_one = 0.75 * inverse
    c_two = 0.75 * inverse_sq
    c_three = 0.375 * inverse_sq * inverse
    along_force = unit_x * force_x + unit_y * force_y + unit_z * force_z
    along_torque = unit_x * torque_x + unit_y * torque_y + unit_z * torque_z
    isotropic = c_one * (1.0 + inverse_sq * (2.0 / 3.0)) + self_term
    dyadic = c_one * (1.0 - 2.0 * inverse_sq) * along_force
    vel_x = isotropic * force_x + dyadic * unit_x + c_two * (torque_y * unit_z - torque_z * unit_y)
    vel_y = isotropic * force_y + dyadic * unit_y + c_two * (torque_z * unit_x - torque_x * unit_z)
    vel_z = isotropic * force_z + dyadic * unit_z + c_two * (torque_x * unit_y - torque_y * unit_x)
    spin_self = 0.75 * self_term - c_three
    spin_x = (
        c_two * (force_y * unit_z - force_z * unit_y)
        + c_three * 3.0 * unit_x * along_torque
        + spin_self * torque_x
    )
    spin_y = (
        c_two * (force_z * unit_x - force_x * unit_z)
        + c_three * 3.0 * unit_y * along_torque
        + spin_self * torque_y
    )
    spin_z = (
        c_two * (force_x * unit_y - force_y * unit_x)
        + c_three * 3.0 * unit_z * along_torque
        + spin_self * torque_z
    )
    return jnp.stack(
        [
            jnp.sum(vel_x, 0),
            jnp.sum(vel_y, 0),
            jnp.sum(vel_z, 0),
            jnp.sum(spin_x, 0),
            jnp.sum(spin_y, 0),
            jnp.sum(spin_z, 0),
        ]
    )


def split_two(value):
    high = lax.reduce_precision(value, exponent_bits=8, mantissa_bits=7)
    low = value - high
    return jnp.stack([high, low]).astype(jnp.bfloat16)


def scatter_kernel(owner_ref, slot_ref, parts_ref, out_ref):
    slots = slot_ref.shape[0]
    owner = owner_ref[...]
    slot = slot_ref[...]
    for k in range(6):
        total = None
        for p in range(2):
            weighted = slot * parts_ref[p, k : k + 1, :]
            term = lax.dot_general(
                owner, weighted, (((1,), (1,)), ((), ())), preferred_element_type=jnp.float32
            )
            total = term if total is None else total + term
        out_ref[:, 0, k * slots : (k + 1) * slots] = total


def gather_kernel(owner_ref, slot_ref, parts_ref, out_ref):
    slots = slot_ref.shape[0]
    owner = owner_ref[...]
    slot = slot_ref[...].astype(jnp.float32)
    for k in range(6):
        picked = None
        for p in range(2):
            part = parts_ref[p, k * slots : (k + 1) * slots, :]
            term = jnp.dot(part, owner, preferred_element_type=jnp.float32)
            picked = term if picked is None else picked + term
        out_ref[k : k + 1, :] = jnp.sum(picked * slot, axis=0, keepdims=True)


def scatter_forces(owner_t, slot_t, end_force):
    owners, ends = owner_t.shape
    slots = slot_t.shape[0]
    parts = split_two(end_force)
    return pl.pallas_call(
        scatter_kernel,
        out_shape=jax.ShapeDtypeStruct((owners, 1, 6 * slots), jnp.float32),
        cost_estimate=pl.CostEstimate(
            flops=2 * 12 * owners * slots * ends, transcendentals=0, bytes_accessed=4 * ends * 300
        ),
    )(owner_t, slot_t, parts)


def gather_velocity(owner_t, slot_t, table):
    owners, ends = owner_t.shape
    slots = slot_t.shape[0]
    return pl.pallas_call(
        gather_kernel,
        out_shape=jax.ShapeDtypeStruct((6, ends), jnp.float32),
        cost_estimate=pl.CostEstimate(
            flops=2 * 12 * owners * slots * ends, transcendentals=0, bytes_accessed=4 * ends * 300
        ),
    )(owner_t, slot_t, split_two(table))


def split_pair(value):
    high = value.astype(jnp.bfloat16)
    low = (value - high.astype(jnp.float32)).astype(jnp.bfloat16)
    return (high, low)


def contact_kernel(step, gather, scatter, *refs):
    bodies_ref, frame_ref, current_ref, other_ref, gaps_ref, steps_ref = refs[:6]
    refs = refs[6:]
    if gather:
        table_ref, refs = refs[0], refs[1:]
    outs = refs
    contacts = frame_ref.shape[1]
    owners = outs[-1].shape[0] if scatter else table_ref.shape[1]
    slots = outs[-1].shape[2] // 6 if scatter else table_ref.shape[0] // 6
    frame = frame_ref[...]
    normal = (frame[0:1], frame[1:2], frame[2:3])

    def crossed(arm):
        return (
            arm[1] * normal[2] - arm[2] * normal[1],
            arm[2] * normal[0] - arm[0] * normal[2],
            arm[0] * normal[1] - arm[1] * normal[0],
        )

    first_lever = crossed((frame[3:4], frame[4:5], frame[5:6]))
    second_lever = crossed((frame[6:7], frame[7:8], frame[8:9]))
    rows = (
        tuple(-v for v in normal) + tuple(-v for v in first_lever),
        normal + second_lever,
    )
    owner_ids = lax.broadcasted_iota(jnp.int32, (owners, contacts), 0)
    slot_ids = lax.broadcasted_iota(jnp.int32, (slots, contacts), 0)
    owner_hot, slot_hot = [], []
    for side in range(2):
        body = bodies_ref[side : side + 1, :]
        owner_hot.append((owner_ids == body // slots).astype(jnp.bfloat16))
        slot_hot.append((slot_ids == body % slots).astype(jnp.bfloat16))
    current = current_ref[...]
    if step == 0:
        shifted = current + MOMENTUM * (current - other_ref[...])
    else:
        shifted = other_ref[...]
    if gather:
        rate = None
        for side in range(2):
            slot_wide = slot_hot[side].astype(jnp.float32)
            for k in range(6):
                picked = None
                for part in split_pair(table_ref[k * slots : (k + 1) * slots, :]):
                    term = jnp.dot(part, owner_hot[side], preferred_element_type=jnp.float32)
                    picked = term if picked is None else picked + term
                velocity = jnp.sum(picked * slot_wide, axis=0, keepdims=True)
                term = rows[side][k] * velocity
                rate = term if rate is None else rate + term
        updated = jnp.maximum(shifted - steps_ref[step] * (gaps_ref[...] + rate), 0.0)
        shifted = updated + MOMENTUM * (updated - current)
        outs[0][...] = updated
        if scatter:
            outs[1][...] = shifted
        outs = outs[1 + int(scatter):]
    if scatter:
        out_ref = outs[0]
        for k in range(6):
            total = None
            for side in range(2):
                for part in split_pair(rows[side][k] * shifted):
                    weighted = slot_hot[side] * part
                    term = lax.dot_general(
                        owner_hot[side], weighted, (((1,), (1,)), ((), ())),
                        preferred_element_type=jnp.float32,
                    )
                    total = term if total is None else total + term
            out_ref[:, 0, k * slots : (k + 1) * slots] = total


def contact_step(step, owners, slots, bodies, frame, state, gaps, steps, table=None, scatter=True):
    contacts = frame.shape[1]
    gather = table is not None
    shapes = []
    if gather:
        shapes += [jax.ShapeDtypeStruct((1, contacts), jnp.float32)] * (1 + int(scatter))
    if scatter:
        shapes.append(jax.ShapeDtypeStruct((owners, 1, 6 * slots), jnp.float32))
    args = (bodies, frame) + tuple(state) + (gaps, steps) + ((table,) if gather else ())
    vmem = pl.BlockSpec(memory_space=pltpu.VMEM)
    specs = [vmem] * 5 + [pl.BlockSpec(memory_space=pltpu.SMEM)] + [vmem] * int(gather)
    return pl.pallas_call(
        functools.partial(contact_kernel, step, gather, scatter),
        out_shape=tuple(shapes),
        in_specs=specs,
        out_specs=tuple(vmem for _ in shapes),
        cost_estimate=pl.CostEstimate(
            flops=2 * 12 * owners * slots * 2 * contacts * (int(gather) + int(scatter)),
            transcendentals=0,
            bytes_accessed=4 * contacts * 600,
        ),
    )(*args)

def pair_kernel(target_ref, place_ref, force_ref, own_ref, out_ref, sums_ref):
    targets = target_ref.shape[1]
    chunks = place_ref.shape[0]
    first_place = place_ref.shape[2] // 128 - 3

    def group(g, carry):
        rows = pl.ds(pl.multiple_of(g * 8, 8), 8)
        target_x = target_ref[0, rows, :]
        target_y = target_ref[1, rows, :]
        target_z = target_ref[2, rows, :]

        def chunk(j, sums):
            place = place_ref[j]
            force = force_ref[j]

            def lane_row(block, row):
                return block[:, row * 128 : (row + 1) * 128]

            r_x = target_x - lane_row(place, first_place)
            r_y = target_y - lane_row(place, first_place + 1)
            r_z = target_z - lane_row(place, first_place + 2)
            f_x, f_y, f_z = (lane_row(force, 0), lane_row(force, 1), lane_row(force, 2))
            t_x, t_y, t_z = (lane_row(force, 3), lane_row(force, 4), lane_row(force, 5))
            dist_sq = r_x * r_x + r_y * r_y + r_z * r_z
            inverse = lax.rsqrt(jnp.maximum(dist_sq, 1.0))
            inverse_sq = inverse * inverse
            c_cross = inverse_sq * inverse
            inverse_fifth = c_cross * inverse_sq
            c_iso = inverse + (2.0 / 3.0) * c_cross
            c_dyad = c_cross - 2.0 * inverse_fifth
            c_spin = 1.5 * inverse_fifth
            c_self = 0.5 * c_cross
            dyad = c_dyad * (r_x * f_x + r_y * f_y + r_z * f_z)
            spin = c_spin * (r_x * t_x + r_y * t_y + r_z * t_z)
            s_x = c_cross * r_x
            s_y = c_cross * r_y
            s_z = c_cross * r_z
            return (
                sums[0] + (c_iso * f_x + dyad * r_x + (t_y * s_z - t_z * s_y)),
                sums[1] + (c_iso * f_y + dyad * r_y + (t_z * s_x - t_x * s_z)),
                sums[2] + (c_iso * f_z + dyad * r_z + (t_x * s_y - t_y * s_x)),
                sums[3] + ((f_y * s_z - f_z * s_y) + spin * r_x - c_self * t_x),
                sums[4] + ((f_z * s_x - f_x * s_z) + spin * r_y - c_self * t_y),
                sums[5] + ((f_x * s_y - f_y * s_x) + spin * r_z - c_self * t_z),
            )

        zero = jnp.zeros((8, 128), jnp.float32)
        sums = lax.fori_loop(0, chunks, chunk, (zero,) * 6, unroll=32)
        for k in range(6):
            sums_ref[k, rows, :] = sums[k]
        return carry

    lax.fori_loop(0, targets // 8, group, 0)
    ones = jnp.ones((8, 128), jnp.bfloat16)
    for k in range(6):
        value = sums_ref[k]
        high = value.astype(jnp.bfloat16)
        rest = value - high.astype(jnp.float32)
        middle = rest.astype(jnp.bfloat16)
        low = (rest - middle.astype(jnp.float32)).astype(jnp.bfloat16)
        total = None
        for part in (high, middle, low):
            term = lax.dot_general(
                ones, part, (((1,), (1,)), ((), ())), preferred_element_type=jnp.float32
            )
            total = term if total is None else total + term
        scale = -0.25 if k < 3 else 1.125
        out_ref[k : k + 1, :] = total[0:1, :] + scale * own_ref[k : k + 1, :]


def mobility_own(spread, places, forces, own_forces):
    own_rows = own_forces.shape[1]
    sources = places.shape[0] * 128
    return pl.pallas_call(
        pair_kernel,
        out_shape=jax.ShapeDtypeStruct((6, own_rows), jnp.float32),
        scratch_shapes=[pltpu.VMEM((6, own_rows, 128), jnp.float32)],
        cost_estimate=pl.CostEstimate(
            flops=90 * own_rows * sources,
            transcendentals=own_rows * sources,
            bytes_accessed=4 * (9 * sources + 3 * own_rows * 128),
        ),
    )(spread, places, forces, own_forces)

def gather_all(block, devices):
    rows, width = block.shape
    spread = jnp.broadcast_to(block[None], (devices, rows, width))
    spread = lax.all_to_all(spread, AXES, 0, 0, tiled=True)
    return spread.transpose(1, 0, 2).reshape(rows, devices * width)


def scatter_sum(full, devices):
    rows, length = full.shape
    width = length // devices
    pieces = full.reshape(rows, devices, width).transpose(1, 0, 2)
    pieces = lax.all_to_all(pieces, AXES, 0, 0, tiled=True)
    return jnp.sum(pieces, 0)


def per_device(
    positions, contact_bodies, contact_frame, gaps, impulse_now, impulse_prev, step_sizes
):
    devices = lax.axis_size("src") * lax.axis_size("tgt")
    me = lax.axis_index("src") * lax.axis_size("tgt") + lax.axis_index("tgt")
    own_rows = positions.shape[1]
    body_count = own_rows * devices
    spread = jnp.broadcast_to(positions[:, :, None], (3, own_rows, 128))
    gaps_row = gaps.reshape(1, -1)
    state = (impulse_now.reshape(1, -1), impulse_prev.reshape(1, -1))
    (pieces,) = contact_step(0, devices, own_rows, contact_bodies, contact_frame, state, gaps_row, step_sizes)
    own_velocity = jnp.zeros((6, own_rows), jnp.float32)
    for k in range(ITERS):
        pieces = lax.all_to_all(pieces, AXES, 0, 0, tiled=True)
        own_forces = jnp.sum(pieces, 0).reshape(6, own_rows)
        if k == 0:
            block = jnp.concatenate([0.75 * own_forces, positions]).reshape(1, 1, 9 * own_rows)
            places = lax.all_to_all(
                jnp.broadcast_to(block, (devices, 1, 9 * own_rows)), AXES, 0, 0, tiled=True
            )
            forces = places
        else:
            block = (0.75 * own_forces).reshape(1, 1, 6 * own_rows)
            forces = lax.all_to_all(
                jnp.broadcast_to(block, (devices, 1, 6 * own_rows)), AXES, 0, 0, tiled=True
            )
        own_velocity = mobility_own(spread, places, forces, own_forces)
        every = jnp.broadcast_to(own_velocity.reshape(1, 6 * own_rows), (devices, 6 * own_rows))
        every = lax.all_to_all(every, AXES, 0, 0, tiled=True)
        last = k == ITERS - 1
        result = contact_step(
            k, devices, own_rows, contact_bodies, contact_frame, state, gaps_row, step_sizes, every.T, scatter=not last
        )
        state = result[:2]
        if not last:
            pieces = result[2]
    current = state[0].reshape(-1)
    return (current, own_velocity)


def solution(mesh):
    placed = (
        P(None, AXES),
        P(None, AXES),
        P(None, AXES),
        P(AXES),
        P(AXES),
        P(AXES),
        P(),
    )
    return jax.shard_map(
        per_device,
        mesh=mesh,
        in_specs=placed,
        out_specs=(P(AXES), P(None, AXES)),
        check_vma=False,
    )
```

```python
import functools

import jax
import jax.numpy as jnp
from jax import lax
from jax.experimental import pallas as pl
from jax.experimental.pallas import tpu as pltpu
from jax.sharding import PartitionSpec as P

ITERS = 2
MOMENTUM = 0.4
AXES = ("src", "tgt")
SOURCE_BLOCK = 1024


def cross_product(first, second):
    return jnp.stack(
        [
            first[1] * second[2] - first[2] * second[1],
            first[2] * second[0] - first[0] * second[2],
            first[0] * second[1] - first[1] * second[0],
        ]
    )


def contact_rows(frame):
    normal = frame[0:3]
    lever_first = cross_product(frame[3:6], normal)
    lever_second = cross_product(frame[6:9], normal)
    return (jnp.concatenate([-normal, -lever_first]), jnp.concatenate([normal, lever_second]))


def pair_block(target_pos, target_ids, source_pos, source_ids, forces):
    delta_x = target_pos[0][None, :] - source_pos[0][:, None]
    delta_y = target_pos[1][None, :] - source_pos[1][:, None]
    delta_z = target_pos[2][None, :] - source_pos[2][:, None]
    coincide = target_ids[None, :] == source_ids[:, None]
    dist_sq = jnp.where(coincide, 1.0, delta_x * delta_x + delta_y * delta_y + delta_z * delta_z)
    inverse = jnp.where(coincide, 0.0, lax.rsqrt(dist_sq))
    self_term = jnp.where(coincide, 1.0, 0.0)
    unit_x = delta_x * inverse
    unit_y = delta_y * inverse
    unit_z = delta_z * inverse
    force_x, force_y, force_z = (forces[0][:, None], forces[1][:, None], forces[2][:, None])
    torque_x, torque_y, torque_z = (forces[3][:, None], forces[4][:, None], forces[5][:, None])
    inverse_sq = inverse * inverse
    c_one = 0.75 * inverse
    c_two = 0.75 * inverse_sq
    c_three = 0.375 * inverse_sq * inverse
    along_force = unit_x * force_x + unit_y * force_y + unit_z * force_z
    along_torque = unit_x * torque_x + unit_y * torque_y + unit_z * torque_z
    isotropic = c_one * (1.0 + inverse_sq * (2.0 / 3.0)) + self_term
    dyadic = c_one * (1.0 - 2.0 * inverse_sq) * along_force
    vel_x = isotropic * force_x + dyadic * unit_x + c_two * (torque_y * unit_z - torque_z * unit_y)
    vel_y = isotropic * force_y + dyadic * unit_y + c_two * (torque_z * unit_x - torque_x * unit_z)
    vel_z = isotropic * force_z + dyadic * unit_z + c_two * (torque_x * unit_y - torque_y * unit_x)
    spin_self = 0.75 * self_term - c_three
    spin_x = (
        c_two * (force_y * unit_z - force_z * unit_y)
        + c_three * 3.0 * unit_x * along_torque
        + spin_self * torque_x
    )
    spin_y = (
        c_two * (force_z * unit_x - force_x * unit_z)
        + c_three * 3.0 * unit_y * along_torque
        + spin_self * torque_y
    )
    spin_z = (
        c_two * (force_x * unit_y - force_y * unit_x)
        + c_three * 3.0 * unit_z * along_torque
        + spin_self * torque_z
    )
    return jnp.stack(
        [
            jnp.sum(vel_x, 0),
            jnp.sum(vel_y, 0),
            jnp.sum(vel_z, 0),
            jnp.sum(spin_x, 0),
            jnp.sum(spin_y, 0),
            jnp.sum(spin_z, 0),
        ]
    )


def split_two(value):
    high = lax.reduce_precision(value, exponent_bits=8, mantissa_bits=7)
    low = value - high
    return jnp.stack([high, low]).astype(jnp.bfloat16)


def scatter_kernel(owner_ref, slot_ref, parts_ref, out_ref):
    slots = slot_ref.shape[0]
    owner = owner_ref[...]
    slot = slot_ref[...]
    for k in range(6):
        total = None
        for p in range(2):
            weighted = slot * parts_ref[p, k : k + 1, :]
            term = lax.dot_general(
                owner, weighted, (((1,), (1,)), ((), ())), preferred_element_type=jnp.float32
            )
            total = term if total is None else total + term
        out_ref[:, 0, k * slots : (k + 1) * slots] = total


def gather_kernel(owner_ref, slot_ref, parts_ref, out_ref):
    slots = slot_ref.shape[0]
    owner = owner_ref[...]
    slot = slot_ref[...].astype(jnp.float32)
    for k in range(6):
        picked = None
        for p in range(2):
            part = parts_ref[p, k * slots : (k + 1) * slots, :]
            term = jnp.dot(part, owner, preferred_element_type=jnp.float32)
            picked = term if picked is None else picked + term
        out_ref[k : k + 1, :] = jnp.sum(picked * slot, axis=0, keepdims=True)


def scatter_forces(owner_t, slot_t, end_force):
    owners, ends = owner_t.shape
    slots = slot_t.shape[0]
    parts = split_two(end_force)
    return pl.pallas_call(
        scatter_kernel,
        out_shape=jax.ShapeDtypeStruct((owners, 1, 6 * slots), jnp.float32),
        cost_estimate=pl.CostEstimate(
            flops=2 * 12 * owners * slots * ends, transcendentals=0, bytes_accessed=4 * ends * 300
        ),
    )(owner_t, slot_t, parts)


def gather_velocity(owner_t, slot_t, table):
    owners, ends = owner_t.shape
    slots = slot_t.shape[0]
    return pl.pallas_call(
        gather_kernel,
        out_shape=jax.ShapeDtypeStruct((6, ends), jnp.float32),
        cost_estimate=pl.CostEstimate(
            flops=2 * 12 * owners * slots * ends, transcendentals=0, bytes_accessed=4 * ends * 300
        ),
    )(owner_t, slot_t, split_two(table))


def split_pair(value):
    high = value.astype(jnp.bfloat16)
    low = (value - high.astype(jnp.float32)).astype(jnp.bfloat16)
    return (high, low)


def contact_kernel(step, gather, scatter, carry, *refs):
    bodies_ref, frame_ref, current_ref, other_ref, gaps_ref, steps_ref = refs[:6]
    refs = refs[6:]
    if gather:
        table_ref, refs = refs[0], refs[1:]
    if carry:
        places_ref, refs = refs[0], refs[1:]
    outs = refs
    contacts = frame_ref.shape[1]
    owners = outs[-1].shape[0] if scatter else table_ref.shape[1]
    slots = table_ref.shape[0] // 6 if gather else outs[-1].shape[2] // (9 if carry else 6)
    frame = frame_ref[...]
    normal = (frame[0:1], frame[1:2], frame[2:3])

    def crossed(arm):
        return (
            arm[1] * normal[2] - arm[2] * normal[1],
            arm[2] * normal[0] - arm[0] * normal[2],
            arm[0] * normal[1] - arm[1] * normal[0],
        )

    first_lever = crossed((frame[3:4], frame[4:5], frame[5:6]))
    second_lever = crossed((frame[6:7], frame[7:8], frame[8:9]))
    rows = (
        tuple(-v for v in normal) + tuple(-v for v in first_lever),
        normal + second_lever,
    )
    owner_ids = lax.broadcasted_iota(jnp.int32, (owners, contacts), 0)
    slot_ids = lax.broadcasted_iota(jnp.int32, (slots, contacts), 0)
    owner_hot, slot_hot = [], []
    for side in range(2):
        body = bodies_ref[side : side + 1, :]
        owner_hot.append((owner_ids == body // slots).astype(jnp.bfloat16))
        slot_hot.append((slot_ids == body % slots).astype(jnp.bfloat16))
    current = current_ref[...]
    if step == 0:
        shifted = current + MOMENTUM * (current - other_ref[...])
    else:
        shifted = other_ref[...]
    if gather:
        rate = None
        for side in range(2):
            slot_wide = slot_hot[side].astype(jnp.float32)
            for k in range(6):
                picked = None
                for part in split_pair(table_ref[k * slots : (k + 1) * slots, :]):
                    term = jnp.dot(part, owner_hot[side], preferred_element_type=jnp.float32)
                    picked = term if picked is None else picked + term
                velocity = jnp.sum(picked * slot_wide, axis=0, keepdims=True)
                term = rows[side][k] * velocity
                rate = term if rate is None else rate + term
        updated = jnp.maximum(shifted - steps_ref[step] * (gaps_ref[...] + rate), 0.0)
        shifted = updated + MOMENTUM * (updated - current)
        outs[0][...] = updated
        if scatter:
            outs[1][...] = shifted
        outs = outs[1 + int(scatter):]
    if scatter:
        out_ref = outs[0]
        for k in range(6):
            total = None
            for side in range(2):
                for part in split_pair(rows[side][k] * shifted):
                    weighted = slot_hot[side] * part
                    term = lax.dot_general(
                        owner_hot[side], weighted, (((1,), (1,)), ((), ())),
                        preferred_element_type=jnp.float32,
                    )
                    total = term if total is None else total + term
            out_ref[:, 0, k * slots : (k + 1) * slots] = total
        if carry:
            for c in range(3):
                row = places_ref[c : c + 1, :]
                out_ref[:, 0, (6 + c) * slots : (7 + c) * slots] = jnp.broadcast_to(row, (owners, slots))


def contact_step(step, owners, slots, bodies, frame, state, gaps, steps, table=None, scatter=True, places=None):
    contacts = frame.shape[1]
    gather = table is not None
    shapes = []
    if gather:
        shapes += [jax.ShapeDtypeStruct((1, contacts), jnp.float32)] * (1 + int(scatter))
    carry = places is not None
    if scatter:
        shapes.append(jax.ShapeDtypeStruct((owners, 1, (9 if carry else 6) * slots), jnp.float32))
    args = (bodies, frame) + tuple(state) + (gaps, steps) + ((table,) if gather else ())
    args += (places,) if carry else ()
    vmem = pl.BlockSpec(memory_space=pltpu.VMEM)
    specs = [vmem] * 5 + [pl.BlockSpec(memory_space=pltpu.SMEM)] + [vmem] * (int(gather) + int(carry))
    return pl.pallas_call(
        functools.partial(contact_kernel, step, gather, scatter, carry),
        out_shape=tuple(shapes),
        in_specs=specs,
        out_specs=tuple(vmem for _ in shapes),
        cost_estimate=pl.CostEstimate(
            flops=2 * 12 * owners * slots * 2 * contacts * (int(gather) + int(scatter)),
            transcendentals=0,
            bytes_accessed=4 * contacts * 600,
        ),
    )(*args)

def pair_kernel(target_ref, place_ref, force_ref, own_ref, out_ref, sums_ref):
    targets = target_ref.shape[1]
    chunks = place_ref.shape[0]
    first_place = place_ref.shape[2] // 128 - 3

    def group(g, carry):
        rows = pl.ds(pl.multiple_of(g * 8, 8), 8)
        target_x = target_ref[0, rows, :]
        target_y = target_ref[1, rows, :]
        target_z = target_ref[2, rows, :]

        def chunk(j, sums):
            place = place_ref[j]
            force = force_ref[j]

            def lane_row(block, row):
                return block[:, row * 128 : (row + 1) * 128]

            r_x = target_x - lane_row(place, first_place)
            r_y = target_y - lane_row(place, first_place + 1)
            r_z = target_z - lane_row(place, first_place + 2)
            f_x, f_y, f_z = (lane_row(force, 0), lane_row(force, 1), lane_row(force, 2))
            t_x, t_y, t_z = (lane_row(force, 3), lane_row(force, 4), lane_row(force, 5))
            dist_sq = r_x * r_x + r_y * r_y + r_z * r_z
            inverse = lax.rsqrt(jnp.maximum(dist_sq, 1.0))
            inverse_sq = inverse * inverse
            c_cross = inverse_sq * inverse
            inverse_fifth = c_cross * inverse_sq
            c_iso = inverse + (2.0 / 3.0) * c_cross
            c_dyad = c_cross - 2.0 * inverse_fifth
            c_spin = 1.5 * inverse_fifth
            c_self = 0.5 * c_cross
            dyad = c_dyad * (r_x * f_x + r_y * f_y + r_z * f_z)
            spin = c_spin * (r_x * t_x + r_y * t_y + r_z * t_z)
            s_x = c_cross * r_x
            s_y = c_cross * r_y
            s_z = c_cross * r_z
            return (
                sums[0] + (c_iso * f_x + dyad * r_x + (t_y * s_z - t_z * s_y)),
                sums[1] + (c_iso * f_y + dyad * r_y + (t_z * s_x - t_x * s_z)),
                sums[2] + (c_iso * f_z + dyad * r_z + (t_x * s_y - t_y * s_x)),
                sums[3] + ((f_y * s_z - f_z * s_y) + spin * r_x - c_self * t_x),
                sums[4] + ((f_z * s_x - f_x * s_z) + spin * r_y - c_self * t_y),
                sums[5] + ((f_x * s_y - f_y * s_x) + spin * r_z - c_self * t_z),
            )

        zero = jnp.zeros((8, 128), jnp.float32)
        sums = lax.fori_loop(0, chunks, chunk, (zero,) * 6, unroll=32)
        for k in range(6):
            sums_ref[k, rows, :] = sums[k]
        return carry

    lax.fori_loop(0, targets // 8, group, 0)
    ones = jnp.ones((8, 128), jnp.bfloat16)
    for k in range(6):
        value = sums_ref[k]
        high = value.astype(jnp.bfloat16)
        rest = value - high.astype(jnp.float32)
        middle = rest.astype(jnp.bfloat16)
        low = (rest - middle.astype(jnp.float32)).astype(jnp.bfloat16)
        total = None
        for part in (high, middle, low):
            term = lax.dot_general(
                ones, part, (((1,), (1,)), ((), ())), preferred_element_type=jnp.float32
            )
            total = term if total is None else total + term
        scale = -0.25 if k < 3 else 1.125
        out_ref[k : k + 1, :] = total[0:1, :] + scale * own_ref[k : k + 1, :]


def mobility_own(spread, places, forces, own_forces):
    own_rows = own_forces.shape[1]
    sources = places.shape[0] * 128
    return pl.pallas_call(
        pair_kernel,
        out_shape=jax.ShapeDtypeStruct((6, own_rows), jnp.float32),
        scratch_shapes=[pltpu.VMEM((6, own_rows, 128), jnp.float32)],
        cost_estimate=pl.CostEstimate(
            flops=90 * own_rows * sources,
            transcendentals=own_rows * sources,
            bytes_accessed=4 * (9 * sources + 3 * own_rows * 128),
        ),
    )(spread, places, forces, own_forces)

def gather_all(block, devices):
    rows, width = block.shape
    spread = jnp.broadcast_to(block[None], (devices, rows, width))
    spread = lax.all_to_all(spread, AXES, 0, 0, tiled=True)
    return spread.transpose(1, 0, 2).reshape(rows, devices * width)


def scatter_sum(full, devices):
    rows, length = full.shape
    width = length // devices
    pieces = full.reshape(rows, devices, width).transpose(1, 0, 2)
    pieces = lax.all_to_all(pieces, AXES, 0, 0, tiled=True)
    return jnp.sum(pieces, 0)


def per_device(
    positions, contact_bodies, contact_frame, gaps, impulse_now, impulse_prev, step_sizes
):
    devices = lax.axis_size("src") * lax.axis_size("tgt")
    me = lax.axis_index("src") * lax.axis_size("tgt") + lax.axis_index("tgt")
    own_rows = positions.shape[1]
    body_count = own_rows * devices
    spread = jnp.broadcast_to(positions[:, :, None], (3, own_rows, 128))
    gaps_row = gaps.reshape(1, -1)
    state = (impulse_now.reshape(1, -1), impulse_prev.reshape(1, -1))
    (pieces,) = contact_step(
        0, devices, own_rows, contact_bodies, contact_frame, state, gaps_row, step_sizes, places=positions
    )
    own_velocity = jnp.zeros((6, own_rows), jnp.float32)
    for k in range(ITERS):
        pieces = lax.all_to_all(pieces, AXES, 0, 0, tiled=True)
        if k == 0:
            places = pieces
        own_forces = jnp.sum(pieces[:, :, : 6 * own_rows], 0).reshape(6, own_rows)
        block = (0.75 * own_forces).reshape(1, 1, 6 * own_rows)
        forces = lax.all_to_all(
            jnp.broadcast_to(block, (devices, 1, 6 * own_rows)), AXES, 0, 0, tiled=True
        )
        own_velocity = mobility_own(spread, places, forces, own_forces)
        every = jnp.broadcast_to(own_velocity.reshape(1, 6 * own_rows), (devices, 6 * own_rows))
        every = lax.all_to_all(every, AXES, 0, 0, tiled=True)
        last = k == ITERS - 1
        result = contact_step(
            k, devices, own_rows, contact_bodies, contact_frame, state, gaps_row, step_sizes, every.T, scatter=not last
        )
        state = result[:2]
        if not last:
            pieces = result[2]
    current = state[0].reshape(-1)
    return (current, own_velocity)


def solution(mesh):
    placed = (
        P(None, AXES),
        P(None, AXES),
        P(None, AXES),
        P(AXES),
        P(AXES),
        P(AXES),
        P(),
    )
    return jax.shard_map(
        per_device,
        mesh=mesh,
        in_specs=placed,
        out_specs=(P(AXES), P(None, AXES)),
        check_vma=False,
    )
```

```python
import functools

import jax
import jax.numpy as jnp
from jax import lax
from jax.experimental import pallas as pl
from jax.experimental.pallas import tpu as pltpu
from jax.sharding import PartitionSpec as P

ITERS = 2
MOMENTUM = 0.4
AXES = ("src", "tgt")
SOURCE_BLOCK = 1024


def cross_product(first, second):
    return jnp.stack(
        [
            first[1] * second[2] - first[2] * second[1],
            first[2] * second[0] - first[0] * second[2],
            first[0] * second[1] - first[1] * second[0],
        ]
    )


def contact_rows(frame):
    normal = frame[0:3]
    lever_first = cross_product(frame[3:6], normal)
    lever_second = cross_product(frame[6:9], normal)
    return (jnp.concatenate([-normal, -lever_first]), jnp.concatenate([normal, lever_second]))


def pair_block(target_pos, target_ids, source_pos, source_ids, forces):
    delta_x = target_pos[0][None, :] - source_pos[0][:, None]
    delta_y = target_pos[1][None, :] - source_pos[1][:, None]
    delta_z = target_pos[2][None, :] - source_pos[2][:, None]
    coincide = target_ids[None, :] == source_ids[:, None]
    dist_sq = jnp.where(coincide, 1.0, delta_x * delta_x + delta_y * delta_y + delta_z * delta_z)
    inverse = jnp.where(coincide, 0.0, lax.rsqrt(dist_sq))
    self_term = jnp.where(coincide, 1.0, 0.0)
    unit_x = delta_x * inverse
    unit_y = delta_y * inverse
    unit_z = delta_z * inverse
    force_x, force_y, force_z = (forces[0][:, None], forces[1][:, None], forces[2][:, None])
    torque_x, torque_y, torque_z = (forces[3][:, None], forces[4][:, None], forces[5][:, None])
    inverse_sq = inverse * inverse
    c_one = 0.75 * inverse
    c_two = 0.75 * inverse_sq
    c_three = 0.375 * inverse_sq * inverse
    along_force = unit_x * force_x + unit_y * force_y + unit_z * force_z
    along_torque = unit_x * torque_x + unit_y * torque_y + unit_z * torque_z
    isotropic = c_one * (1.0 + inverse_sq * (2.0 / 3.0)) + self_term
    dyadic = c_one * (1.0 - 2.0 * inverse_sq) * along_force
    vel_x = isotropic * force_x + dyadic * unit_x + c_two * (torque_y * unit_z - torque_z * unit_y)
    vel_y = isotropic * force_y + dyadic * unit_y + c_two * (torque_z * unit_x - torque_x * unit_z)
    vel_z = isotropic * force_z + dyadic * unit_z + c_two * (torque_x * unit_y - torque_y * unit_x)
    spin_self = 0.75 * self_term - c_three
    spin_x = (
        c_two * (force_y * unit_z - force_z * unit_y)
        + c_three * 3.0 * unit_x * along_torque
        + spin_self * torque_x
    )
    spin_y = (
        c_two * (force_z * unit_x - force_x * unit_z)
        + c_three * 3.0 * unit_y * along_torque
        + spin_self * torque_y
    )
    spin_z = (
        c_two * (force_x * unit_y - force_y * unit_x)
        + c_three * 3.0 * unit_z * along_torque
        + spin_self * torque_z
    )
    return jnp.stack(
        [
            jnp.sum(vel_x, 0),
            jnp.sum(vel_y, 0),
            jnp.sum(vel_z, 0),
            jnp.sum(spin_x, 0),
            jnp.sum(spin_y, 0),
            jnp.sum(spin_z, 0),
        ]
    )


def split_two(value):
    high = lax.reduce_precision(value, exponent_bits=8, mantissa_bits=7)
    low = value - high
    return jnp.stack([high, low]).astype(jnp.bfloat16)


def scatter_kernel(owner_ref, slot_ref, parts_ref, out_ref):
    slots = slot_ref.shape[0]
    owner = owner_ref[...]
    slot = slot_ref[...]
    for k in range(6):
        total = None
        for p in range(2):
            weighted = slot * parts_ref[p, k : k + 1, :]
            term = lax.dot_general(
                owner, weighted, (((1,), (1,)), ((), ())), preferred_element_type=jnp.float32
            )
            total = term if total is None else total + term
        out_ref[:, 0, k * slots : (k + 1) * slots] = total


def gather_kernel(owner_ref, slot_ref, parts_ref, out_ref):
    slots = slot_ref.shape[0]
    owner = owner_ref[...]
    slot = slot_ref[...].astype(jnp.float32)
    for k in range(6):
        picked = None
        for p in range(2):
            part = parts_ref[p, k * slots : (k + 1) * slots, :]
            term = jnp.dot(part, owner, preferred_element_type=jnp.float32)
            picked = term if picked is None else picked + term
        out_ref[k : k + 1, :] = jnp.sum(picked * slot, axis=0, keepdims=True)


def scatter_forces(owner_t, slot_t, end_force):
    owners, ends = owner_t.shape
    slots = slot_t.shape[0]
    parts = split_two(end_force)
    return pl.pallas_call(
        scatter_kernel,
        out_shape=jax.ShapeDtypeStruct((owners, 1, 6 * slots), jnp.float32),
        cost_estimate=pl.CostEstimate(
            flops=2 * 12 * owners * slots * ends, transcendentals=0, bytes_accessed=4 * ends * 300
        ),
    )(owner_t, slot_t, parts)


def gather_velocity(owner_t, slot_t, table):
    owners, ends = owner_t.shape
    slots = slot_t.shape[0]
    return pl.pallas_call(
        gather_kernel,
        out_shape=jax.ShapeDtypeStruct((6, ends), jnp.float32),
        cost_estimate=pl.CostEstimate(
            flops=2 * 12 * owners * slots * ends, transcendentals=0, bytes_accessed=4 * ends * 300
        ),
    )(owner_t, slot_t, split_two(table))


def split_pair(value):
    high = value.astype(jnp.bfloat16)
    low = (value - high.astype(jnp.float32)).astype(jnp.bfloat16)
    return (high, low)


def contact_kernel(step, gather, scatter, *refs):
    bodies_ref, frame_ref, current_ref, other_ref, gaps_ref, steps_ref = refs[:6]
    refs = refs[6:]
    if gather:
        table_ref, refs = refs[0], refs[1:]
    outs = refs
    contacts = frame_ref.shape[1]
    owners = outs[-1].shape[0] if scatter else table_ref.shape[0]
    slots = outs[-1].shape[2] // 6 if scatter else table_ref.shape[2] // 6
    frame = frame_ref[...]
    normal = (frame[0:1], frame[1:2], frame[2:3])

    def crossed(arm):
        return (
            arm[1] * normal[2] - arm[2] * normal[1],
            arm[2] * normal[0] - arm[0] * normal[2],
            arm[0] * normal[1] - arm[1] * normal[0],
        )

    first_lever = crossed((frame[3:4], frame[4:5], frame[5:6]))
    second_lever = crossed((frame[6:7], frame[7:8], frame[8:9]))
    rows = (
        tuple(-v for v in normal) + tuple(-v for v in first_lever),
        normal + second_lever,
    )
    owner_ids = lax.broadcasted_iota(jnp.int32, (owners, contacts), 0)
    slot_ids = lax.broadcasted_iota(jnp.int32, (slots, contacts), 0)
    owner_hot, slot_hot = [], []
    for side in range(2):
        body = bodies_ref[side : side + 1, :]
        owner_hot.append((owner_ids == body // slots).astype(jnp.bfloat16))
        slot_hot.append((slot_ids == body % slots).astype(jnp.bfloat16))
    current = current_ref[...]
    if step == 0:
        shifted = current + MOMENTUM * (current - other_ref[...])
    else:
        shifted = other_ref[...]
    if gather:
        rate = None
        for side in range(2):
            slot_wide = slot_hot[side].astype(jnp.float32)
            for k in range(6):
                picked = None
                for part in split_pair(table_ref[:, 0, k * slots : (k + 1) * slots]):
                    term = lax.dot_general(
                        part, owner_hot[side], (((0,), (0,)), ((), ())),
                        preferred_element_type=jnp.float32,
                    )
                    picked = term if picked is None else picked + term
                velocity = jnp.sum(picked * slot_wide, axis=0, keepdims=True)
                term = rows[side][k] * velocity
                rate = term if rate is None else rate + term
        updated = jnp.maximum(shifted - steps_ref[step] * (gaps_ref[...] + rate), 0.0)
        shifted = updated + MOMENTUM * (updated - current)
        outs[0][...] = updated
        if scatter:
            outs[1][...] = shifted
        outs = outs[1 + int(scatter):]
    if scatter:
        out_ref = outs[0]
        for k in range(6):
            total = None
            for side in range(2):
                for part in split_pair(rows[side][k] * shifted):
                    weighted = slot_hot[side] * part
                    term = lax.dot_general(
                        owner_hot[side], weighted, (((1,), (1,)), ((), ())),
                        preferred_element_type=jnp.float32,
                    )
                    total = term if total is None else total + term
            out_ref[:, 0, k * slots : (k + 1) * slots] = total


def contact_step(step, owners, slots, bodies, frame, state, gaps, steps, table=None, scatter=True):
    contacts = frame.shape[1]
    gather = table is not None
    shapes = []
    if gather:
        shapes += [jax.ShapeDtypeStruct((1, contacts), jnp.float32)] * (1 + int(scatter))
    if scatter:
        shapes.append(jax.ShapeDtypeStruct((owners, 1, 6 * slots), jnp.float32))
    args = (bodies, frame) + tuple(state) + (gaps, steps) + ((table,) if gather else ())
    vmem = pl.BlockSpec(memory_space=pltpu.VMEM)
    specs = [vmem] * 5 + [pl.BlockSpec(memory_space=pltpu.SMEM)] + [vmem] * int(gather)
    return pl.pallas_call(
        functools.partial(contact_kernel, step, gather, scatter),
        out_shape=tuple(shapes),
        in_specs=specs,
        out_specs=tuple(vmem for _ in shapes),
        cost_estimate=pl.CostEstimate(
            flops=2 * 12 * owners * slots * 2 * contacts * (int(gather) + int(scatter)),
            transcendentals=0,
            bytes_accessed=4 * contacts * 600,
        ),
    )(*args)

def pair_kernel(target_ref, place_ref, force_ref, own_ref, out_ref, sums_ref):
    targets = target_ref.shape[1]
    chunks = place_ref.shape[0]
    first_place = place_ref.shape[2] // 128 - 3

    def group(g, carry):
        rows = pl.ds(pl.multiple_of(g * 8, 8), 8)
        target_x = target_ref[0, rows, :]
        target_y = target_ref[1, rows, :]
        target_z = target_ref[2, rows, :]

        def chunk(j, sums):
            place = place_ref[j]
            force = force_ref[j]

            def lane_row(block, row):
                return block[:, row * 128 : (row + 1) * 128]

            r_x = target_x - lane_row(place, first_place)
            r_y = target_y - lane_row(place, first_place + 1)
            r_z = target_z - lane_row(place, first_place + 2)
            f_x, f_y, f_z = (lane_row(force, 0), lane_row(force, 1), lane_row(force, 2))
            t_x, t_y, t_z = (lane_row(force, 3), lane_row(force, 4), lane_row(force, 5))
            dist_sq = r_x * r_x + r_y * r_y + r_z * r_z
            inverse = lax.rsqrt(jnp.maximum(dist_sq, 1.0))
            inverse_sq = inverse * inverse
            c_cross = inverse_sq * inverse
            inverse_fifth = c_cross * inverse_sq
            c_iso = inverse + (2.0 / 3.0) * c_cross
            c_dyad = c_cross - 2.0 * inverse_fifth
            c_spin = 1.5 * inverse_fifth
            c_self = 0.5 * c_cross
            dyad = c_dyad * (r_x * f_x + r_y * f_y + r_z * f_z)
            spin = c_spin * (r_x * t_x + r_y * t_y + r_z * t_z)
            s_x = c_cross * r_x
            s_y = c_cross * r_y
            s_z = c_cross * r_z
            return (
                sums[0] + (c_iso * f_x + dyad * r_x + (t_y * s_z - t_z * s_y)),
                sums[1] + (c_iso * f_y + dyad * r_y + (t_z * s_x - t_x * s_z)),
                sums[2] + (c_iso * f_z + dyad * r_z + (t_x * s_y - t_y * s_x)),
                sums[3] + ((f_y * s_z - f_z * s_y) + spin * r_x - c_self * t_x),
                sums[4] + ((f_z * s_x - f_x * s_z) + spin * r_y - c_self * t_y),
                sums[5] + ((f_x * s_y - f_y * s_x) + spin * r_z - c_self * t_z),
            )

        zero = jnp.zeros((8, 128), jnp.float32)
        sums = lax.fori_loop(0, chunks, chunk, (zero,) * 6, unroll=32)
        for k in range(6):
            sums_ref[k, rows, :] = sums[k]
        return carry

    lax.fori_loop(0, targets // 8, group, 0)
    ones = jnp.ones((8, 128), jnp.bfloat16)
    for k in range(6):
        value = sums_ref[k]
        high = value.astype(jnp.bfloat16)
        rest = value - high.astype(jnp.float32)
        middle = rest.astype(jnp.bfloat16)
        low = (rest - middle.astype(jnp.float32)).astype(jnp.bfloat16)
        total = None
        for part in (high, middle, low):
            term = lax.dot_general(
                ones, part, (((1,), (1,)), ((), ())), preferred_element_type=jnp.float32
            )
            total = term if total is None else total + term
        scale = -0.25 if k < 3 else 1.125
        out_ref[k : k + 1, :] = total[0:1, :] + scale * own_ref[k : k + 1, :]


def mobility_own(spread, places, forces, own_forces):
    own_rows = own_forces.shape[1]
    sources = places.shape[0] * 128
    return pl.pallas_call(
        pair_kernel,
        out_shape=jax.ShapeDtypeStruct((6, own_rows), jnp.float32),
        scratch_shapes=[pltpu.VMEM((6, own_rows, 128), jnp.float32)],
        cost_estimate=pl.CostEstimate(
            flops=90 * own_rows * sources,
            transcendentals=own_rows * sources,
            bytes_accessed=4 * (9 * sources + 3 * own_rows * 128),
        ),
    )(spread, places, forces, own_forces)

def gather_all(block, devices):
    rows, width = block.shape
    spread = jnp.broadcast_to(block[None], (devices, rows, width))
    spread = lax.all_to_all(spread, AXES, 0, 0, tiled=True)
    return spread.transpose(1, 0, 2).reshape(rows, devices * width)


def scatter_sum(full, devices):
    rows, length = full.shape
    width = length // devices
    pieces = full.reshape(rows, devices, width).transpose(1, 0, 2)
    pieces = lax.all_to_all(pieces, AXES, 0, 0, tiled=True)
    return jnp.sum(pieces, 0)


def per_device(
    positions, contact_bodies, contact_frame, gaps, impulse_now, impulse_prev, step_sizes
):
    devices = lax.axis_size("src") * lax.axis_size("tgt")
    me = lax.axis_index("src") * lax.axis_size("tgt") + lax.axis_index("tgt")
    own_rows = positions.shape[1]
    body_count = own_rows * devices
    spread = jnp.broadcast_to(positions[:, :, None], (3, own_rows, 128))
    gaps_row = gaps.reshape(1, -1)
    state = (impulse_now.reshape(1, -1), impulse_prev.reshape(1, -1))
    (pieces,) = contact_step(0, devices, own_rows, contact_bodies, contact_frame, state, gaps_row, step_sizes)
    own_velocity = jnp.zeros((6, own_rows), jnp.float32)
    for k in range(ITERS):
        pieces = lax.all_to_all(pieces, AXES, 0, 0, tiled=True)
        own_forces = jnp.sum(pieces, 0).reshape(6, own_rows)
        if k == 0:
            block = jnp.concatenate([0.75 * own_forces, positions]).reshape(1, 1, 9 * own_rows)
            places = lax.all_to_all(
                jnp.broadcast_to(block, (devices, 1, 9 * own_rows)), AXES, 0, 0, tiled=True
            )
            forces = places
        else:
            block = (0.75 * own_forces).reshape(1, 1, 6 * own_rows)
            forces = lax.all_to_all(
                jnp.broadcast_to(block, (devices, 1, 6 * own_rows)), AXES, 0, 0, tiled=True
            )
        own_velocity = mobility_own(spread, places, forces, own_forces)
        every = jnp.broadcast_to(own_velocity.reshape(1, 1, 6 * own_rows), (devices, 1, 6 * own_rows))
        every = lax.all_to_all(every, AXES, 0, 0, tiled=True)
        last = k == ITERS - 1
        result = contact_step(
            k, devices, own_rows, contact_bodies, contact_frame, state, gaps_row, step_sizes, every, scatter=not last
        )
        state = result[:2]
        if not last:
            pieces = result[2]
    current = state[0].reshape(-1)
    return (current, own_velocity)


def solution(mesh):
    placed = (
        P(None, AXES),
        P(None, AXES),
        P(None, AXES),
        P(AXES),
        P(AXES),
        P(AXES),
        P(),
    )
    return jax.shard_map(
        per_device,
        mesh=mesh,
        in_specs=placed,
        out_specs=(P(AXES), P(None, AXES)),
        check_vma=False,
    )
```

```python
import functools

import jax
import jax.numpy as jnp
from jax import lax
from jax.experimental import pallas as pl
from jax.experimental.pallas import tpu as pltpu
from jax.sharding import PartitionSpec as P

ITERS = 2
MOMENTUM = 0.4
AXES = ("src", "tgt")
SOURCE_BLOCK = 1024


def cross_product(first, second):
    return jnp.stack(
        [
            first[1] * second[2] - first[2] * second[1],
            first[2] * second[0] - first[0] * second[2],
            first[0] * second[1] - first[1] * second[0],
        ]
    )


def contact_rows(frame):
    normal = frame[0:3]
    lever_first = cross_product(frame[3:6], normal)
    lever_second = cross_product(frame[6:9], normal)
    return (jnp.concatenate([-normal, -lever_first]), jnp.concatenate([normal, lever_second]))


def pair_block(target_pos, target_ids, source_pos, source_ids, forces):
    delta_x = target_pos[0][None, :] - source_pos[0][:, None]
    delta_y = target_pos[1][None, :] - source_pos[1][:, None]
    delta_z = target_pos[2][None, :] - source_pos[2][:, None]
    coincide = target_ids[None, :] == source_ids[:, None]
    dist_sq = jnp.where(coincide, 1.0, delta_x * delta_x + delta_y * delta_y + delta_z * delta_z)
    inverse = jnp.where(coincide, 0.0, lax.rsqrt(dist_sq))
    self_term = jnp.where(coincide, 1.0, 0.0)
    unit_x = delta_x * inverse
    unit_y = delta_y * inverse
    unit_z = delta_z * inverse
    force_x, force_y, force_z = (forces[0][:, None], forces[1][:, None], forces[2][:, None])
    torque_x, torque_y, torque_z = (forces[3][:, None], forces[4][:, None], forces[5][:, None])
    inverse_sq = inverse * inverse
    c_one = 0.75 * inverse
    c_two = 0.75 * inverse_sq
    c_three = 0.375 * inverse_sq * inverse
    along_force = unit_x * force_x + unit_y * force_y + unit_z * force_z
    along_torque = unit_x * torque_x + unit_y * torque_y + unit_z * torque_z
    isotropic = c_one * (1.0 + inverse_sq * (2.0 / 3.0)) + self_term
    dyadic = c_one * (1.0 - 2.0 * inverse_sq) * along_force
    vel_x = isotropic * force_x + dyadic * unit_x + c_two * (torque_y * unit_z - torque_z * unit_y)
    vel_y = isotropic * force_y + dyadic * unit_y + c_two * (torque_z * unit_x - torque_x * unit_z)
    vel_z = isotropic * force_z + dyadic * unit_z + c_two * (torque_x * unit_y - torque_y * unit_x)
    spin_self = 0.75 * self_term - c_three
    spin_x = (
        c_two * (force_y * unit_z - force_z * unit_y)
        + c_three * 3.0 * unit_x * along_torque
        + spin_self * torque_x
    )
    spin_y = (
        c_two * (force_z * unit_x - force_x * unit_z)
        + c_three * 3.0 * unit_y * along_torque
        + spin_self * torque_y
    )
    spin_z = (
        c_two * (force_x * unit_y - force_y * unit_x)
        + c_three * 3.0 * unit_z * along_torque
        + spin_self * torque_z
    )
    return jnp.stack(
        [
            jnp.sum(vel_x, 0),
            jnp.sum(vel_y, 0),
            jnp.sum(vel_z, 0),
            jnp.sum(spin_x, 0),
            jnp.sum(spin_y, 0),
            jnp.sum(spin_z, 0),
        ]
    )


def split_two(value):
    high = lax.reduce_precision(value, exponent_bits=8, mantissa_bits=7)
    low = value - high
    return jnp.stack([high, low]).astype(jnp.bfloat16)


def scatter_kernel(owner_ref, slot_ref, parts_ref, out_ref):
    slots = slot_ref.shape[0]
    owner = owner_ref[...]
    slot = slot_ref[...]
    for k in range(6):
        total = None
        for p in range(2):
            weighted = slot * parts_ref[p, k : k + 1, :]
            term = lax.dot_general(
                owner, weighted, (((1,), (1,)), ((), ())), preferred_element_type=jnp.float32
            )
            total = term if total is None else total + term
        out_ref[:, 0, k * slots : (k + 1) * slots] = total


def gather_kernel(owner_ref, slot_ref, parts_ref, out_ref):
    slots = slot_ref.shape[0]
    owner = owner_ref[...]
    slot = slot_ref[...].astype(jnp.float32)
    for k in range(6):
        picked = None
        for p in range(2):
            part = parts_ref[p, k * slots : (k + 1) * slots, :]
            term = jnp.dot(part, owner, preferred_element_type=jnp.float32)
            picked = term if picked is None else picked + term
        out_ref[k : k + 1, :] = jnp.sum(picked * slot, axis=0, keepdims=True)


def scatter_forces(owner_t, slot_t, end_force):
    owners, ends = owner_t.shape
    slots = slot_t.shape[0]
    parts = split_two(end_force)
    return pl.pallas_call(
        scatter_kernel,
        out_shape=jax.ShapeDtypeStruct((owners, 1, 6 * slots), jnp.float32),
        cost_estimate=pl.CostEstimate(
            flops=2 * 12 * owners * slots * ends, transcendentals=0, bytes_accessed=4 * ends * 300
        ),
    )(owner_t, slot_t, parts)


def gather_velocity(owner_t, slot_t, table):
    owners, ends = owner_t.shape
    slots = slot_t.shape[0]
    return pl.pallas_call(
        gather_kernel,
        out_shape=jax.ShapeDtypeStruct((6, ends), jnp.float32),
        cost_estimate=pl.CostEstimate(
            flops=2 * 12 * owners * slots * ends, transcendentals=0, bytes_accessed=4 * ends * 300
        ),
    )(owner_t, slot_t, split_two(table))


def split_pair(value):
    high = value.astype(jnp.bfloat16)
    low = (value - high.astype(jnp.float32)).astype(jnp.bfloat16)
    return (high, low)


def contact_kernel(step, gather, scatter, *refs):
    bodies_ref, frame_ref, current_ref, other_ref, gaps_ref, steps_ref = refs[:6]
    refs = refs[6:]
    if gather:
        table_ref, refs = refs[0], refs[1:]
    outs = refs
    contacts = frame_ref.shape[1]
    owners = outs[-1].shape[0] if scatter else table_ref.shape[1]
    slots = outs[-1].shape[2] // 6 if scatter else table_ref.shape[0] // 6
    frame = frame_ref[...]
    normal = (frame[0:1], frame[1:2], frame[2:3])

    def crossed(arm):
        return (
            arm[1] * normal[2] - arm[2] * normal[1],
            arm[2] * normal[0] - arm[0] * normal[2],
            arm[0] * normal[1] - arm[1] * normal[0],
        )

    first_lever = crossed((frame[3:4], frame[4:5], frame[5:6]))
    second_lever = crossed((frame[6:7], frame[7:8], frame[8:9]))
    rows = (
        tuple(-v for v in normal) + tuple(-v for v in first_lever),
        normal + second_lever,
    )
    owner_ids = lax.broadcasted_iota(jnp.int32, (owners, 2 * contacts), 0)
    slot_ids = lax.broadcasted_iota(jnp.int32, (slots, 2 * contacts), 0)
    body = jnp.concatenate([bodies_ref[0:1, :], bodies_ref[1:2, :]], axis=1)
    owner_hot = (owner_ids == body // slots).astype(jnp.bfloat16)
    slot_hot = (slot_ids == body % slots).astype(jnp.bfloat16)
    end_rows = [jnp.concatenate([rows[0][k], rows[1][k]], axis=1) for k in range(6)]
    current = current_ref[...]
    if step == 0:
        shifted = current + MOMENTUM * (current - other_ref[...])
    else:
        shifted = other_ref[...]
    if gather:
        slot_wide = slot_hot.astype(jnp.float32)
        rate = None
        for k in range(6):
            picked = None
            for part in split_pair(table_ref[k * slots : (k + 1) * slots, :]):
                term = jnp.dot(part, owner_hot, preferred_element_type=jnp.float32)
                picked = term if picked is None else picked + term
            velocity = jnp.sum(picked * slot_wide, axis=0, keepdims=True)
            term = end_rows[k] * velocity
            rate = term if rate is None else rate + term
        rate = rate[:, :contacts] + rate[:, contacts:]
        updated = jnp.maximum(shifted - steps_ref[step] * (gaps_ref[...] + rate), 0.0)
        shifted = updated + MOMENTUM * (updated - current)
        outs[0][...] = updated
        if scatter:
            outs[1][...] = shifted
        outs = outs[1 + int(scatter):]
    if scatter:
        out_ref = outs[0]
        both = jnp.concatenate([shifted, shifted], axis=1)
        for k in range(6):
            total = None
            for part in split_pair(end_rows[k] * both):
                weighted = slot_hot * part
                term = lax.dot_general(
                    owner_hot, weighted, (((1,), (1,)), ((), ())),
                    preferred_element_type=jnp.float32,
                )
                total = term if total is None else total + term
            out_ref[:, 0, k * slots : (k + 1) * slots] = total


def contact_step(step, owners, slots, bodies, frame, state, gaps, steps, table=None, scatter=True):
    contacts = frame.shape[1]
    gather = table is not None
    shapes = []
    if gather:
        shapes += [jax.ShapeDtypeStruct((1, contacts), jnp.float32)] * (1 + int(scatter))
    if scatter:
        shapes.append(jax.ShapeDtypeStruct((owners, 1, 6 * slots), jnp.float32))
    args = (bodies, frame) + tuple(state) + (gaps, steps) + ((table,) if gather else ())
    vmem = pl.BlockSpec(memory_space=pltpu.VMEM)
    specs = [vmem] * 5 + [pl.BlockSpec(memory_space=pltpu.SMEM)] + [vmem] * int(gather)
    return pl.pallas_call(
        functools.partial(contact_kernel, step, gather, scatter),
        out_shape=tuple(shapes),
        in_specs=specs,
        out_specs=tuple(vmem for _ in shapes),
        cost_estimate=pl.CostEstimate(
            flops=2 * 12 * owners * slots * 2 * contacts * (int(gather) + int(scatter)),
            transcendentals=0,
            bytes_accessed=4 * contacts * 600,
        ),
    )(*args)

def pair_kernel(target_ref, place_ref, force_ref, own_ref, out_ref, sums_ref):
    targets = target_ref.shape[1]
    chunks = place_ref.shape[0]
    first_place = place_ref.shape[2] // 128 - 3

    def group(g, carry):
        rows = pl.ds(pl.multiple_of(g * 8, 8), 8)
        target_x = target_ref[0, rows, :]
        target_y = target_ref[1, rows, :]
        target_z = target_ref[2, rows, :]

        def chunk(j, sums):
            place = place_ref[j]
            force = force_ref[j]

            def lane_row(block, row):
                return block[:, row * 128 : (row + 1) * 128]

            r_x = target_x - lane_row(place, first_place)
            r_y = target_y - lane_row(place, first_place + 1)
            r_z = target_z - lane_row(place, first_place + 2)
            f_x, f_y, f_z = (lane_row(force, 0), lane_row(force, 1), lane_row(force, 2))
            t_x, t_y, t_z = (lane_row(force, 3), lane_row(force, 4), lane_row(force, 5))
            dist_sq = r_x * r_x + r_y * r_y + r_z * r_z
            inverse = lax.rsqrt(jnp.maximum(dist_sq, 1.0))
            inverse_sq = inverse * inverse
            c_cross = inverse_sq * inverse
            inverse_fifth = c_cross * inverse_sq
            c_iso = inverse + (2.0 / 3.0) * c_cross
            c_dyad = c_cross - 2.0 * inverse_fifth
            c_spin = 1.5 * inverse_fifth
            c_self = 0.5 * c_cross
            dyad = c_dyad * (r_x * f_x + r_y * f_y + r_z * f_z)
            spin = c_spin * (r_x * t_x + r_y * t_y + r_z * t_z)
            s_x = c_cross * r_x
            s_y = c_cross * r_y
            s_z = c_cross * r_z
            return (
                sums[0] + (c_iso * f_x + dyad * r_x + (t_y * s_z - t_z * s_y)),
                sums[1] + (c_iso * f_y + dyad * r_y + (t_z * s_x - t_x * s_z)),
                sums[2] + (c_iso * f_z + dyad * r_z + (t_x * s_y - t_y * s_x)),
                sums[3] + ((f_y * s_z - f_z * s_y) + spin * r_x - c_self * t_x),
                sums[4] + ((f_z * s_x - f_x * s_z) + spin * r_y - c_self * t_y),
                sums[5] + ((f_x * s_y - f_y * s_x) + spin * r_z - c_self * t_z),
            )

        zero = jnp.zeros((8, 128), jnp.float32)
        sums = lax.fori_loop(0, chunks, chunk, (zero,) * 6, unroll=32)
        for k in range(6):
            sums_ref[k, rows, :] = sums[k]
        return carry

    lax.fori_loop(0, targets // 8, group, 0)
    ones = jnp.ones((8, 128), jnp.bfloat16)
    for k in range(6):
        value = sums_ref[k]
        high = value.astype(jnp.bfloat16)
        rest = value - high.astype(jnp.float32)
        middle = rest.astype(jnp.bfloat16)
        low = (rest - middle.astype(jnp.float32)).astype(jnp.bfloat16)
        total = None
        for part in (high, middle, low):
            term = lax.dot_general(
                ones, part, (((1,), (1,)), ((), ())), preferred_element_type=jnp.float32
            )
            total = term if total is None else total + term
        scale = -0.25 if k < 3 else 1.125
        out_ref[k : k + 1, :] = total[0:1, :] + scale * own_ref[k : k + 1, :]


def mobility_own(spread, places, forces, own_forces):
    own_rows = own_forces.shape[1]
    sources = places.shape[0] * 128
    return pl.pallas_call(
        pair_kernel,
        out_shape=jax.ShapeDtypeStruct((6, own_rows), jnp.float32),
        scratch_shapes=[pltpu.VMEM((6, own_rows, 128), jnp.float32)],
        cost_estimate=pl.CostEstimate(
            flops=90 * own_rows * sources,
            transcendentals=own_rows * sources,
            bytes_accessed=4 * (9 * sources + 3 * own_rows * 128),
        ),
    )(spread, places, forces, own_forces)

def gather_all(block, devices):
    rows, width = block.shape
    spread = jnp.broadcast_to(block[None], (devices, rows, width))
    spread = lax.all_to_all(spread, AXES, 0, 0, tiled=True)
    return spread.transpose(1, 0, 2).reshape(rows, devices * width)


def scatter_sum(full, devices):
    rows, length = full.shape
    width = length // devices
    pieces = full.reshape(rows, devices, width).transpose(1, 0, 2)
    pieces = lax.all_to_all(pieces, AXES, 0, 0, tiled=True)
    return jnp.sum(pieces, 0)


def per_device(
    positions, contact_bodies, contact_frame, gaps, impulse_now, impulse_prev, step_sizes
):
    devices = lax.axis_size("src") * lax.axis_size("tgt")
    me = lax.axis_index("src") * lax.axis_size("tgt") + lax.axis_index("tgt")
    own_rows = positions.shape[1]
    body_count = own_rows * devices
    spread = jnp.broadcast_to(positions[:, :, None], (3, own_rows, 128))
    gaps_row = gaps.reshape(1, -1)
    state = (impulse_now.reshape(1, -1), impulse_prev.reshape(1, -1))
    (pieces,) = contact_step(0, devices, own_rows, contact_bodies, contact_frame, state, gaps_row, step_sizes)
    own_velocity = jnp.zeros((6, own_rows), jnp.float32)
    for k in range(ITERS):
        pieces = lax.all_to_all(pieces, AXES, 0, 0, tiled=True)
        own_forces = jnp.sum(pieces, 0).reshape(6, own_rows)
        if k == 0:
            block = jnp.concatenate([0.75 * own_forces, positions]).reshape(1, 1, 9 * own_rows)
            places = lax.all_to_all(
                jnp.broadcast_to(block, (devices, 1, 9 * own_rows)), AXES, 0, 0, tiled=True
            )
            forces = places
        else:
            block = (0.75 * own_forces).reshape(1, 1, 6 * own_rows)
            forces = lax.all_to_all(
                jnp.broadcast_to(block, (devices, 1, 6 * own_rows)), AXES, 0, 0, tiled=True
            )
        own_velocity = mobility_own(spread, places, forces, own_forces)
        every = jnp.broadcast_to(own_velocity.reshape(1, 6 * own_rows), (devices, 6 * own_rows))
        every = lax.all_to_all(every, AXES, 0, 0, tiled=True)
        last = k == ITERS - 1
        result = contact_step(
            k, devices, own_rows, contact_bodies, contact_frame, state, gaps_row, step_sizes, every.T, scatter=not last
        )
        state = result[:2]
        if not last:
            pieces = result[2]
    current = state[0].reshape(-1)
    return (current, own_velocity)


def solution(mesh):
    placed = (
        P(None, AXES),
        P(None, AXES),
        P(None, AXES),
        P(AXES),
        P(AXES),
        P(AXES),
        P(),
    )
    return jax.shard_map(
        per_device,
        mesh=mesh,
        in_specs=placed,
        out_specs=(P(AXES), P(None, AXES)),
        check_vma=False,
    )
```

```python
import functools

import jax
import jax.numpy as jnp
from jax import lax
from jax.experimental import pallas as pl
from jax.experimental.pallas import tpu as pltpu
from jax.sharding import PartitionSpec as P

ITERS = 2
MOMENTUM = 0.4
AXES = ("src", "tgt")
SOURCE_BLOCK = 1024


def cross_product(first, second):
    return jnp.stack(
        [
            first[1] * second[2] - first[2] * second[1],
            first[2] * second[0] - first[0] * second[2],
            first[0] * second[1] - first[1] * second[0],
        ]
    )


def contact_rows(frame):
    normal = frame[0:3]
    lever_first = cross_product(frame[3:6], normal)
    lever_second = cross_product(frame[6:9], normal)
    return (jnp.concatenate([-normal, -lever_first]), jnp.concatenate([normal, lever_second]))


def pair_block(target_pos, target_ids, source_pos, source_ids, forces):
    delta_x = target_pos[0][None, :] - source_pos[0][:, None]
    delta_y = target_pos[1][None, :] - source_pos[1][:, None]
    delta_z = target_pos[2][None, :] - source_pos[2][:, None]
    coincide = target_ids[None, :] == source_ids[:, None]
    dist_sq = jnp.where(coincide, 1.0, delta_x * delta_x + delta_y * delta_y + delta_z * delta_z)
    inverse = jnp.where(coincide, 0.0, lax.rsqrt(dist_sq))
    self_term = jnp.where(coincide, 1.0, 0.0)
    unit_x = delta_x * inverse
    unit_y = delta_y * inverse
    unit_z = delta_z * inverse
    force_x, force_y, force_z = (forces[0][:, None], forces[1][:, None], forces[2][:, None])
    torque_x, torque_y, torque_z = (forces[3][:, None], forces[4][:, None], forces[5][:, None])
    inverse_sq = inverse * inverse
    c_one = 0.75 * inverse
    c_two = 0.75 * inverse_sq
    c_three = 0.375 * inverse_sq * inverse
    along_force = unit_x * force_x + unit_y * force_y + unit_z * force_z
    along_torque = unit_x * torque_x + unit_y * torque_y + unit_z * torque_z
    isotropic = c_one * (1.0 + inverse_sq * (2.0 / 3.0)) + self_term
    dyadic = c_one * (1.0 - 2.0 * inverse_sq) * along_force
    vel_x = isotropic * force_x + dyadic * unit_x + c_two * (torque_y * unit_z - torque_z * unit_y)
    vel_y = isotropic * force_y + dyadic * unit_y + c_two * (torque_z * unit_x - torque_x * unit_z)
    vel_z = isotropic * force_z + dyadic * unit_z + c_two * (torque_x * unit_y - torque_y * unit_x)
    spin_self = 0.75 * self_term - c_three
    spin_x = (
        c_two * (force_y * unit_z - force_z * unit_y)
        + c_three * 3.0 * unit_x * along_torque
        + spin_self * torque_x
    )
    spin_y = (
        c_two * (force_z * unit_x - force_x * unit_z)
        + c_three * 3.0 * unit_y * along_torque
        + spin_self * torque_y
    )
    spin_z = (
        c_two * (force_x * unit_y - force_y * unit_x)
        + c_three * 3.0 * unit_z * along_torque
        + spin_self * torque_z
    )
    return jnp.stack(
        [
            jnp.sum(vel_x, 0),
            jnp.sum(vel_y, 0),
            jnp.sum(vel_z, 0),
            jnp.sum(spin_x, 0),
            jnp.sum(spin_y, 0),
            jnp.sum(spin_z, 0),
        ]
    )


def split_two(value):
    high = lax.reduce_precision(value, exponent_bits=8, mantissa_bits=7)
    low = value - high
    return jnp.stack([high, low]).astype(jnp.bfloat16)


def scatter_kernel(owner_ref, slot_ref, parts_ref, out_ref):
    slots = slot_ref.shape[0]
    owner = owner_ref[...]
    slot = slot_ref[...]
    for k in range(6):
        total = None
        for p in range(2):
            weighted = slot * parts_ref[p, k : k + 1, :]
            term = lax.dot_general(
                owner, weighted, (((1,), (1,)), ((), ())), preferred_element_type=jnp.float32
            )
            total = term if total is None else total + term
        out_ref[:, 0, k * slots : (k + 1) * slots] = total


def gather_kernel(owner_ref, slot_ref, parts_ref, out_ref):
    slots = slot_ref.shape[0]
    owner = owner_ref[...]
    slot = slot_ref[...].astype(jnp.float32)
    for k in range(6):
        picked = None
        for p in range(2):
            part = parts_ref[p, k * slots : (k + 1) * slots, :]
            term = jnp.dot(part, owner, preferred_element_type=jnp.float32)
            picked = term if picked is None else picked + term
        out_ref[k : k + 1, :] = jnp.sum(picked * slot, axis=0, keepdims=True)


def scatter_forces(owner_t, slot_t, end_force):
    owners, ends = owner_t.shape
    slots = slot_t.shape[0]
    parts = split_two(end_force)
    return pl.pallas_call(
        scatter_kernel,
        out_shape=jax.ShapeDtypeStruct((owners, 1, 6 * slots), jnp.float32),
        cost_estimate=pl.CostEstimate(
            flops=2 * 12 * owners * slots * ends, transcendentals=0, bytes_accessed=4 * ends * 300
        ),
    )(owner_t, slot_t, parts)


def gather_velocity(owner_t, slot_t, table):
    owners, ends = owner_t.shape
    slots = slot_t.shape[0]
    return pl.pallas_call(
        gather_kernel,
        out_shape=jax.ShapeDtypeStruct((6, ends), jnp.float32),
        cost_estimate=pl.CostEstimate(
            flops=2 * 12 * owners * slots * ends, transcendentals=0, bytes_accessed=4 * ends * 300
        ),
    )(owner_t, slot_t, split_two(table))


def split_pair(value):
    high = value.astype(jnp.bfloat16)
    low = (value - high.astype(jnp.float32)).astype(jnp.bfloat16)
    return (high, low)


def contact_kernel(step, gather, scatter, *refs):
    bodies_ref, frame_ref, current_ref, other_ref, gaps_ref, steps_ref = refs[:6]
    refs = refs[6:]
    if gather:
        table_ref, refs = refs[0], refs[1:]
    outs = refs
    contacts = frame_ref.shape[1]
    owners = outs[-1].shape[0] if scatter else table_ref.shape[1]
    slots = outs[-1].shape[2] // 6 if scatter else table_ref.shape[0] // 6
    frame = frame_ref[...]
    normal = (frame[0:1], frame[1:2], frame[2:3])

    def crossed(arm):
        return (
            arm[1] * normal[2] - arm[2] * normal[1],
            arm[2] * normal[0] - arm[0] * normal[2],
            arm[0] * normal[1] - arm[1] * normal[0],
        )

    first_lever = crossed((frame[3:4], frame[4:5], frame[5:6]))
    second_lever = crossed((frame[6:7], frame[7:8], frame[8:9]))
    rows = (
        tuple(-v for v in normal) + tuple(-v for v in first_lever),
        normal + second_lever,
    )
    owner_ids = lax.broadcasted_iota(jnp.int32, (owners, contacts), 0)
    slot_ids = lax.broadcasted_iota(jnp.int32, (slots, contacts), 0)
    owner_hot, slot_hot = [], []
    for side in range(2):
        body = bodies_ref[side : side + 1, :]
        owner_hot.append((owner_ids == body // slots).astype(jnp.bfloat16))
        slot_hot.append((slot_ids == body % slots).astype(jnp.bfloat16))
    current = current_ref[...]
    if step == 0:
        shifted = current + MOMENTUM * (current - other_ref[...])
    else:
        shifted = other_ref[...]
    if gather:
        rate = None
        for side in range(2):
            slot_wide = slot_hot[side].astype(jnp.float32)
            for k in range(6):
                picked = None
                for part in split_pair(table_ref[k * slots : (k + 1) * slots, :]):
                    term = jnp.dot(part, owner_hot[side], preferred_element_type=jnp.float32)
                    picked = term if picked is None else picked + term
                velocity = jnp.sum(picked * slot_wide, axis=0, keepdims=True)
                term = rows[side][k] * velocity
                rate = term if rate is None else rate + term
        updated = jnp.maximum(shifted - steps_ref[step] * (gaps_ref[...] + rate), 0.0)
        shifted = updated + MOMENTUM * (updated - current)
        outs[0][...] = updated
        if scatter:
            outs[1][...] = shifted
        outs = outs[1 + int(scatter):]
    if scatter:
        out_ref = outs[0]
        for k in range(6):
            total = None
            for side in range(2):
                for part in split_pair(rows[side][k] * shifted):
                    weighted = slot_hot[side] * part
                    term = lax.dot_general(
                        owner_hot[side], weighted, (((1,), (1,)), ((), ())),
                        preferred_element_type=jnp.float32,
                    )
                    total = term if total is None else total + term
            out_ref[:, 0, k * slots : (k + 1) * slots] = total


def contact_step(step, owners, slots, bodies, frame, state, gaps, steps, table=None, scatter=True):
    contacts = frame.shape[1]
    gather = table is not None
    shapes = []
    if gather:
        shapes += [jax.ShapeDtypeStruct((1, contacts), jnp.float32)] * (1 + int(scatter))
    if scatter:
        shapes.append(jax.ShapeDtypeStruct((owners, 1, 6 * slots), jnp.float32))
    args = (bodies, frame) + tuple(state) + (gaps, steps) + ((table,) if gather else ())
    vmem = pl.BlockSpec(memory_space=pltpu.VMEM)
    specs = [vmem] * 5 + [pl.BlockSpec(memory_space=pltpu.SMEM)] + [vmem] * int(gather)
    return pl.pallas_call(
        functools.partial(contact_kernel, step, gather, scatter),
        out_shape=tuple(shapes),
        in_specs=specs,
        out_specs=tuple(vmem for _ in shapes),
        cost_estimate=pl.CostEstimate(
            flops=2 * 12 * owners * slots * 2 * contacts * (int(gather) + int(scatter)),
            transcendentals=0,
            bytes_accessed=4 * contacts * 600,
        ),
    )(*args)

def pair_kernel(target_ref, place_ref, force_ref, own_ref, out_ref, every_ref, sums_ref):
    targets = target_ref.shape[1]
    chunks = place_ref.shape[0]
    first_place = place_ref.shape[2] // 128 - 3

    def group(g, carry):
        rows = pl.ds(pl.multiple_of(g * 8, 8), 8)
        target_x = target_ref[0, rows, :]
        target_y = target_ref[1, rows, :]
        target_z = target_ref[2, rows, :]

        def chunk(j, sums):
            place = place_ref[j]
            force = force_ref[j]

            def lane_row(block, row):
                return block[:, row * 128 : (row + 1) * 128]

            r_x = target_x - lane_row(place, first_place)
            r_y = target_y - lane_row(place, first_place + 1)
            r_z = target_z - lane_row(place, first_place + 2)
            f_x, f_y, f_z = (lane_row(force, 0), lane_row(force, 1), lane_row(force, 2))
            t_x, t_y, t_z = (lane_row(force, 3), lane_row(force, 4), lane_row(force, 5))
            dist_sq = r_x * r_x + r_y * r_y + r_z * r_z
            inverse = lax.rsqrt(jnp.maximum(dist_sq, 1.0))
            inverse_sq = inverse * inverse
            c_cross = inverse_sq * inverse
            inverse_fifth = c_cross * inverse_sq
            c_iso = inverse + (2.0 / 3.0) * c_cross
            c_dyad = c_cross - 2.0 * inverse_fifth
            c_spin = 1.5 * inverse_fifth
            c_self = 0.5 * c_cross
            dyad = c_dyad * (r_x * f_x + r_y * f_y + r_z * f_z)
            spin = c_spin * (r_x * t_x + r_y * t_y + r_z * t_z)
            s_x = c_cross * r_x
            s_y = c_cross * r_y
            s_z = c_cross * r_z
            return (
                sums[0] + (c_iso * f_x + dyad * r_x + (t_y * s_z - t_z * s_y)),
                sums[1] + (c_iso * f_y + dyad * r_y + (t_z * s_x - t_x * s_z)),
                sums[2] + (c_iso * f_z + dyad * r_z + (t_x * s_y - t_y * s_x)),
                sums[3] + ((f_y * s_z - f_z * s_y) + spin * r_x - c_self * t_x),
                sums[4] + ((f_z * s_x - f_x * s_z) + spin * r_y - c_self * t_y),
                sums[5] + ((f_x * s_y - f_y * s_x) + spin * r_z - c_self * t_z),
            )

        zero = jnp.zeros((8, 128), jnp.float32)
        sums = lax.fori_loop(0, chunks, chunk, (zero,) * 6, unroll=32)
        for k in range(6):
            sums_ref[k, rows, :] = sums[k]
        return carry

    lax.fori_loop(0, targets // 8, group, 0)
    ones = jnp.ones((8, 128), jnp.bfloat16)
    for k in range(6):
        value = sums_ref[k]
        high = value.astype(jnp.bfloat16)
        rest = value - high.astype(jnp.float32)
        middle = rest.astype(jnp.bfloat16)
        low = (rest - middle.astype(jnp.float32)).astype(jnp.bfloat16)
        total = None
        for part in (high, middle, low):
            term = lax.dot_general(
                ones, part, (((1,), (1,)), ((), ())), preferred_element_type=jnp.float32
            )
            total = term if total is None else total + term
        scale = -0.25 if k < 3 else 1.125
        row = total[0:1, :] + scale * own_ref[k : k + 1, :]
        out_ref[k : k + 1, :] = row
        every_ref[:, 0, k * targets : (k + 1) * targets] = jnp.broadcast_to(
            row, (every_ref.shape[0], targets)
        )


def mobility_own(spread, places, forces, own_forces):
    own_rows = own_forces.shape[1]
    sources = places.shape[0] * 128
    return pl.pallas_call(
        pair_kernel,
        out_shape=(
            jax.ShapeDtypeStruct((6, own_rows), jnp.float32),
            jax.ShapeDtypeStruct((places.shape[0], 1, 6 * own_rows), jnp.float32),
        ),
        scratch_shapes=[pltpu.VMEM((6, own_rows, 128), jnp.float32)],
        cost_estimate=pl.CostEstimate(
            flops=90 * own_rows * sources,
            transcendentals=own_rows * sources,
            bytes_accessed=4 * (9 * sources + 3 * own_rows * 128),
        ),
    )(spread, places, forces, own_forces)

def gather_all(block, devices):
    rows, width = block.shape
    spread = jnp.broadcast_to(block[None], (devices, rows, width))
    spread = lax.all_to_all(spread, AXES, 0, 0, tiled=True)
    return spread.transpose(1, 0, 2).reshape(rows, devices * width)


def scatter_sum(full, devices):
    rows, length = full.shape
    width = length // devices
    pieces = full.reshape(rows, devices, width).transpose(1, 0, 2)
    pieces = lax.all_to_all(pieces, AXES, 0, 0, tiled=True)
    return jnp.sum(pieces, 0)


def per_device(
    positions, contact_bodies, contact_frame, gaps, impulse_now, impulse_prev, step_sizes
):
    devices = lax.axis_size("src") * lax.axis_size("tgt")
    me = lax.axis_index("src") * lax.axis_size("tgt") + lax.axis_index("tgt")
    own_rows = positions.shape[1]
    body_count = own_rows * devices
    spread = jnp.broadcast_to(positions[:, :, None], (3, own_rows, 128))
    gaps_row = gaps.reshape(1, -1)
    state = (impulse_now.reshape(1, -1), impulse_prev.reshape(1, -1))
    (pieces,) = contact_step(0, devices, own_rows, contact_bodies, contact_frame, state, gaps_row, step_sizes)
    own_velocity = jnp.zeros((6, own_rows), jnp.float32)
    for k in range(ITERS):
        pieces = lax.all_to_all(pieces, AXES, 0, 0, tiled=True)
        own_forces = jnp.sum(pieces, 0).reshape(6, own_rows)
        if k == 0:
            block = jnp.concatenate([0.75 * own_forces, positions]).reshape(1, 1, 9 * own_rows)
            places = lax.all_to_all(
                jnp.broadcast_to(block, (devices, 1, 9 * own_rows)), AXES, 0, 0, tiled=True
            )
            forces = places
        else:
            block = (0.75 * own_forces).reshape(1, 1, 6 * own_rows)
            forces = lax.all_to_all(
                jnp.broadcast_to(block, (devices, 1, 6 * own_rows)), AXES, 0, 0, tiled=True
            )
        own_velocity, every = mobility_own(spread, places, forces, own_forces)
        every = lax.all_to_all(every, AXES, 0, 0, tiled=True).reshape(devices, 6 * own_rows)
        last = k == ITERS - 1
        result = contact_step(
            k, devices, own_rows, contact_bodies, contact_frame, state, gaps_row, step_sizes, every.T, scatter=not last
        )
        state = result[:2]
        if not last:
            pieces = result[2]
    current = state[0].reshape(-1)
    return (current, own_velocity)


def solution(mesh):
    placed = (
        P(None, AXES),
        P(None, AXES),
        P(None, AXES),
        P(AXES),
        P(AXES),
        P(AXES),
        P(),
    )
    return jax.shard_map(
        per_device,
        mesh=mesh,
        in_specs=placed,
        out_specs=(P(AXES), P(None, AXES)),
        check_vma=False,
    )
```

```python
import functools

import jax
import jax.numpy as jnp
from jax import lax
from jax.experimental import pallas as pl
from jax.experimental.pallas import tpu as pltpu
from jax.sharding import PartitionSpec as P

ITERS = 2
MOMENTUM = 0.4
AXES = ("src", "tgt")
SOURCE_BLOCK = 1024


def cross_product(first, second):
    return jnp.stack(
        [
            first[1] * second[2] - first[2] * second[1],
            first[2] * second[0] - first[0] * second[2],
            first[0] * second[1] - first[1] * second[0],
        ]
    )


def contact_rows(frame):
    normal = frame[0:3]
    lever_first = cross_product(frame[3:6], normal)
    lever_second = cross_product(frame[6:9], normal)
    return (jnp.concatenate([-normal, -lever_first]), jnp.concatenate([normal, lever_second]))


def pair_block(target_pos, target_ids, source_pos, source_ids, forces):
    delta_x = target_pos[0][None, :] - source_pos[0][:, None]
    delta_y = target_pos[1][None, :] - source_pos[1][:, None]
    delta_z = target_pos[2][None, :] - source_pos[2][:, None]
    coincide = target_ids[None, :] == source_ids[:, None]
    dist_sq = jnp.where(coincide, 1.0, delta_x * delta_x + delta_y * delta_y + delta_z * delta_z)
    inverse = jnp.where(coincide, 0.0, lax.rsqrt(dist_sq))
    self_term = jnp.where(coincide, 1.0, 0.0)
    unit_x = delta_x * inverse
    unit_y = delta_y * inverse
    unit_z = delta_z * inverse
    force_x, force_y, force_z = (forces[0][:, None], forces[1][:, None], forces[2][:, None])
    torque_x, torque_y, torque_z = (forces[3][:, None], forces[4][:, None], forces[5][:, None])
    inverse_sq = inverse * inverse
    c_one = 0.75 * inverse
    c_two = 0.75 * inverse_sq
    c_three = 0.375 * inverse_sq * inverse
    along_force = unit_x * force_x + unit_y * force_y + unit_z * force_z
    along_torque = unit_x * torque_x + unit_y * torque_y + unit_z * torque_z
    isotropic = c_one * (1.0 + inverse_sq * (2.0 / 3.0)) + self_term
    dyadic = c_one * (1.0 - 2.0 * inverse_sq) * along_force
    vel_x = isotropic * force_x + dyadic * unit_x + c_two * (torque_y * unit_z - torque_z * unit_y)
    vel_y = isotropic * force_y + dyadic * unit_y + c_two * (torque_z * unit_x - torque_x * unit_z)
    vel_z = isotropic * force_z + dyadic * unit_z + c_two * (torque_x * unit_y - torque_y * unit_x)
    spin_self = 0.75 * self_term - c_three
    spin_x = (
        c_two * (force_y * unit_z - force_z * unit_y)
        + c_three * 3.0 * unit_x * along_torque
        + spin_self * torque_x
    )
    spin_y = (
        c_two * (force_z * unit_x - force_x * unit_z)
        + c_three * 3.0 * unit_y * along_torque
        + spin_self * torque_y
    )
    spin_z = (
        c_two * (force_x * unit_y - force_y * unit_x)
        + c_three * 3.0 * unit_z * along_torque
        + spin_self * torque_z
    )
    return jnp.stack(
        [
            jnp.sum(vel_x, 0),
            jnp.sum(vel_y, 0),
            jnp.sum(vel_z, 0),
            jnp.sum(spin_x, 0),
            jnp.sum(spin_y, 0),
            jnp.sum(spin_z, 0),
        ]
    )


def split_two(value):
    high = lax.reduce_precision(value, exponent_bits=8, mantissa_bits=7)
    low = value - high
    return jnp.stack([high, low]).astype(jnp.bfloat16)


def scatter_kernel(owner_ref, slot_ref, parts_ref, out_ref):
    slots = slot_ref.shape[0]
    owner = owner_ref[...]
    slot = slot_ref[...]
    for k in range(6):
        total = None
        for p in range(2):
            weighted = slot * parts_ref[p, k : k + 1, :]
            term = lax.dot_general(
                owner, weighted, (((1,), (1,)), ((), ())), preferred_element_type=jnp.float32
            )
            total = term if total is None else total + term
        out_ref[:, 0, k * slots : (k + 1) * slots] = total


def gather_kernel(owner_ref, slot_ref, parts_ref, out_ref):
    slots = slot_ref.shape[0]
    owner = owner_ref[...]
    slot = slot_ref[...].astype(jnp.float32)
    for k in range(6):
        picked = None
        for p in range(2):
            part = parts_ref[p, k * slots : (k + 1) * slots, :]
            term = jnp.dot(part, owner, preferred_element_type=jnp.float32)
            picked = term if picked is None else picked + term
        out_ref[k : k + 1, :] = jnp.sum(picked * slot, axis=0, keepdims=True)


def scatter_forces(owner_t, slot_t, end_force):
    owners, ends = owner_t.shape
    slots = slot_t.shape[0]
    parts = split_two(end_force)
    return pl.pallas_call(
        scatter_kernel,
        out_shape=jax.ShapeDtypeStruct((owners, 1, 6 * slots), jnp.float32),
        cost_estimate=pl.CostEstimate(
            flops=2 * 12 * owners * slots * ends, transcendentals=0, bytes_accessed=4 * ends * 300
        ),
    )(owner_t, slot_t, parts)


def gather_velocity(owner_t, slot_t, table):
    owners, ends = owner_t.shape
    slots = slot_t.shape[0]
    return pl.pallas_call(
        gather_kernel,
        out_shape=jax.ShapeDtypeStruct((6, ends), jnp.float32),
        cost_estimate=pl.CostEstimate(
            flops=2 * 12 * owners * slots * ends, transcendentals=0, bytes_accessed=4 * ends * 300
        ),
    )(owner_t, slot_t, split_two(table))


def split_pair(value):
    high = value.astype(jnp.bfloat16)
    low = (value - high.astype(jnp.float32)).astype(jnp.bfloat16)
    return (high, low)


def contact_kernel(step, gather, scatter, *refs):
    bodies_ref, frame_ref, current_ref, other_ref, gaps_ref, steps_ref = refs[:6]
    refs = refs[6:]
    if gather:
        table_ref, refs = refs[0], refs[1:]
    outs = refs
    contacts = frame_ref.shape[1]
    owners = outs[-1].shape[0] if scatter else table_ref.shape[1]
    slots = outs[-1].shape[2] // 6 if scatter else table_ref.shape[0] // 6
    frame = frame_ref[...]
    normal = (frame[0:1], frame[1:2], frame[2:3])

    def crossed(arm):
        return (
            arm[1] * normal[2] - arm[2] * normal[1],
            arm[2] * normal[0] - arm[0] * normal[2],
            arm[0] * normal[1] - arm[1] * normal[0],
        )

    first_lever = crossed((frame[3:4], frame[4:5], frame[5:6]))
    second_lever = crossed((frame[6:7], frame[7:8], frame[8:9]))
    rows = (
        tuple(-v for v in normal) + tuple(-v for v in first_lever),
        normal + second_lever,
    )
    owner_ids = lax.broadcasted_iota(jnp.int32, (owners, contacts), 0)
    slot_ids = lax.broadcasted_iota(jnp.int32, (slots, contacts), 0)
    owner_hot, slot_hot = [], []
    for side in range(2):
        body = bodies_ref[side : side + 1, :]
        owner_hot.append((owner_ids == body // slots).astype(jnp.bfloat16))
        slot_hot.append((slot_ids == body % slots).astype(jnp.bfloat16))
    current = current_ref[...]
    if step == 0:
        shifted = current + MOMENTUM * (current - other_ref[...])
    else:
        shifted = other_ref[...]
    if gather:
        rate = None
        for side in range(2):
            slot_wide = slot_hot[side].astype(jnp.float32)
            for k in range(6):
                picked = None
                for part in split_pair(table_ref[k * slots : (k + 1) * slots, :]):
                    term = jnp.dot(part, owner_hot[side], preferred_element_type=jnp.float32)
                    picked = term if picked is None else picked + term
                velocity = jnp.sum(picked * slot_wide, axis=0, keepdims=True)
                term = rows[side][k] * velocity
                rate = term if rate is None else rate + term
        updated = jnp.maximum(shifted - steps_ref[step] * (gaps_ref[...] + rate), 0.0)
        shifted = updated + MOMENTUM * (updated - current)
        outs[0][...] = updated
        if scatter:
            outs[1][...] = shifted
        outs = outs[1 + int(scatter):]
    if scatter:
        out_ref = outs[0]
        for k in range(6):
            total = None
            for side in range(2):
                for part in split_pair(rows[side][k] * shifted):
                    weighted = slot_hot[side] * part
                    term = lax.dot_general(
                        owner_hot[side], weighted, (((1,), (1,)), ((), ())),
                        preferred_element_type=jnp.float32,
                    )
                    total = term if total is None else total + term
            out_ref[:, 0, k * slots : (k + 1) * slots] = total


def contact_step(step, owners, slots, bodies, frame, state, gaps, steps, table=None, scatter=True):
    contacts = frame.shape[1]
    gather = table is not None
    shapes = []
    if gather:
        shapes += [jax.ShapeDtypeStruct((1, contacts), jnp.float32)] * (1 + int(scatter))
    if scatter:
        shapes.append(jax.ShapeDtypeStruct((owners, 1, 6 * slots), jnp.float32))
    args = (bodies, frame) + tuple(state) + (gaps, steps) + ((table,) if gather else ())
    vmem = pl.BlockSpec(memory_space=pltpu.VMEM)
    specs = [vmem] * 5 + [pl.BlockSpec(memory_space=pltpu.SMEM)] + [vmem] * int(gather)
    return pl.pallas_call(
        functools.partial(contact_kernel, step, gather, scatter),
        out_shape=tuple(shapes),
        in_specs=specs,
        out_specs=tuple(vmem for _ in shapes),
        cost_estimate=pl.CostEstimate(
            flops=2 * 12 * owners * slots * 2 * contacts * (int(gather) + int(scatter)),
            transcendentals=0,
            bytes_accessed=4 * contacts * 600,
        ),
    )(*args)

def pair_kernel(target_ref, place_ref, force_ref, own_ref, out_ref, sums_ref):
    targets = target_ref.shape[1]
    chunks = place_ref.shape[0]
    first_place = place_ref.shape[2] // 128 - 3

    def group(g, carry):
        rows = pl.ds(pl.multiple_of(g * 8, 8), 8)
        target_x = target_ref[0, rows, :]
        target_y = target_ref[1, rows, :]
        target_z = target_ref[2, rows, :]

        def chunk(j, sums):
            place = place_ref[j]
            force = force_ref[j]

            def lane_row(block, row):
                return block[:, row * 128 : (row + 1) * 128]

            r_x = target_x - lane_row(place, first_place)
            r_y = target_y - lane_row(place, first_place + 1)
            r_z = target_z - lane_row(place, first_place + 2)
            f_x, f_y, f_z = (lane_row(force, 0), lane_row(force, 1), lane_row(force, 2))
            t_x, t_y, t_z = (lane_row(force, 3), lane_row(force, 4), lane_row(force, 5))
            dist_sq = r_x * r_x + r_y * r_y + r_z * r_z
            inverse = lax.rsqrt(jnp.maximum(dist_sq, 1.0))
            inverse_sq = inverse * inverse
            c_cross = inverse_sq * inverse
            inverse_fifth = c_cross * inverse_sq
            c_iso = inverse + (2.0 / 3.0) * c_cross
            c_dyad = c_cross - 2.0 * inverse_fifth
            c_spin = 1.5 * inverse_fifth
            c_self = 0.5 * c_cross
            dyad = c_dyad * (r_x * f_x + r_y * f_y + r_z * f_z)
            spin = c_spin * (r_x * t_x + r_y * t_y + r_z * t_z)
            s_x = c_cross * r_x
            s_y = c_cross * r_y
            s_z = c_cross * r_z
            return (
                sums[0] + (c_iso * f_x + dyad * r_x + (t_y * s_z - t_z * s_y)),
                sums[1] + (c_iso * f_y + dyad * r_y + (t_z * s_x - t_x * s_z)),
                sums[2] + (c_iso * f_z + dyad * r_z + (t_x * s_y - t_y * s_x)),
                sums[3] + ((f_y * s_z - f_z * s_y) + spin * r_x - c_self * t_x),
                sums[4] + ((f_z * s_x - f_x * s_z) + spin * r_y - c_self * t_y),
                sums[5] + ((f_x * s_y - f_y * s_x) + spin * r_z - c_self * t_z),
            )

        zero = jnp.zeros((8, 128), jnp.float32)
        sums = lax.fori_loop(0, chunks, chunk, (zero,) * 6, unroll=64)
        for k in range(6):
            sums_ref[k, rows, :] = sums[k]
        return carry

    lax.fori_loop(0, targets // 8, group, 0)
    ones = jnp.ones((8, 128), jnp.bfloat16)
    for k in range(6):
        value = sums_ref[k]
        high = value.astype(jnp.bfloat16)
        rest = value - high.astype(jnp.float32)
        middle = rest.astype(jnp.bfloat16)
        low = (rest - middle.astype(jnp.float32)).astype(jnp.bfloat16)
        total = None
        for part in (high, middle, low):
            term = lax.dot_general(
                ones, part, (((1,), (1,)), ((), ())), preferred_element_type=jnp.float32
            )
            total = term if total is None else total + term
        scale = -0.25 if k < 3 else 1.125
        out_ref[k : k + 1, :] = total[0:1, :] + scale * own_ref[k : k + 1, :]


def mobility_own(spread, places, forces, own_forces):
    own_rows = own_forces.shape[1]
    sources = places.shape[0] * 128
    return pl.pallas_call(
        pair_kernel,
        out_shape=jax.ShapeDtypeStruct((6, own_rows), jnp.float32),
        scratch_shapes=[pltpu.VMEM((6, own_rows, 128), jnp.float32)],
        cost_estimate=pl.CostEstimate(
            flops=90 * own_rows * sources,
            transcendentals=own_rows * sources,
            bytes_accessed=4 * (9 * sources + 3 * own_rows * 128),
        ),
    )(spread, places, forces, own_forces)

def gather_all(block, devices):
    rows, width = block.shape
    spread = jnp.broadcast_to(block[None], (devices, rows, width))
    spread = lax.all_to_all(spread, AXES, 0, 0, tiled=True)
    return spread.transpose(1, 0, 2).reshape(rows, devices * width)


def scatter_sum(full, devices):
    rows, length = full.shape
    width = length // devices
    pieces = full.reshape(rows, devices, width).transpose(1, 0, 2)
    pieces = lax.all_to_all(pieces, AXES, 0, 0, tiled=True)
    return jnp.sum(pieces, 0)


def per_device(
    positions, contact_bodies, contact_frame, gaps, impulse_now, impulse_prev, step_sizes
):
    devices = lax.axis_size("src") * lax.axis_size("tgt")
    me = lax.axis_index("src") * lax.axis_size("tgt") + lax.axis_index("tgt")
    own_rows = positions.shape[1]
    body_count = own_rows * devices
    spread = jnp.broadcast_to(positions[:, :, None], (3, own_rows, 128))
    gaps_row = gaps.reshape(1, -1)
    state = (impulse_now.reshape(1, -1), impulse_prev.reshape(1, -1))
    (pieces,) = contact_step(0, devices, own_rows, contact_bodies, contact_frame, state, gaps_row, step_sizes)
    own_velocity = jnp.zeros((6, own_rows), jnp.float32)
    for k in range(ITERS):
        pieces = lax.all_to_all(pieces, AXES, 0, 0, tiled=True)
        own_forces = jnp.sum(pieces, 0).reshape(6, own_rows)
        if k == 0:
            block = jnp.concatenate([0.75 * own_forces, positions]).reshape(1, 1, 9 * own_rows)
            places = lax.all_to_all(
                jnp.broadcast_to(block, (devices, 1, 9 * own_rows)), AXES, 0, 0, tiled=True
            )
            forces = places
        else:
            block = (0.75 * own_forces).reshape(1, 1, 6 * own_rows)
            forces = lax.all_to_all(
                jnp.broadcast_to(block, (devices, 1, 6 * own_rows)), AXES, 0, 0, tiled=True
            )
        own_velocity = mobility_own(spread, places, forces, own_forces)
        every = jnp.broadcast_to(own_velocity.reshape(1, 6 * own_rows), (devices, 6 * own_rows))
        every = lax.all_to_all(every, AXES, 0, 0, tiled=True)
        last = k == ITERS - 1
        result = contact_step(
            k, devices, own_rows, contact_bodies, contact_frame, state, gaps_row, step_sizes, every.T, scatter=not last
        )
        state = result[:2]
        if not last:
            pieces = result[2]
    current = state[0].reshape(-1)
    return (current, own_velocity)


def solution(mesh):
    placed = (
        P(None, AXES),
        P(None, AXES),
        P(None, AXES),
        P(AXES),
        P(AXES),
        P(AXES),
        P(),
    )
    return jax.shard_map(
        per_device,
        mesh=mesh,
        in_specs=placed,
        out_specs=(P(AXES), P(None, AXES)),
        check_vma=False,
    )
```

```python
import functools

import jax
import jax.numpy as jnp
from jax import lax
from jax.experimental import pallas as pl
from jax.experimental.pallas import tpu as pltpu
from jax.sharding import PartitionSpec as P

ITERS = 2
MOMENTUM = 0.4
AXES = ("src", "tgt")
SOURCE_BLOCK = 1024


def cross_product(first, second):
    return jnp.stack(
        [
            first[1] * second[2] - first[2] * second[1],
            first[2] * second[0] - first[0] * second[2],
            first[0] * second[1] - first[1] * second[0],
        ]
    )


def contact_rows(frame):
    normal = frame[0:3]
    lever_first = cross_product(frame[3:6], normal)
    lever_second = cross_product(frame[6:9], normal)
    return (jnp.concatenate([-normal, -lever_first]), jnp.concatenate([normal, lever_second]))


def pair_block(target_pos, target_ids, source_pos, source_ids, forces):
    delta_x = target_pos[0][None, :] - source_pos[0][:, None]
    delta_y = target_pos[1][None, :] - source_pos[1][:, None]
    delta_z = target_pos[2][None, :] - source_pos[2][:, None]
    coincide = target_ids[None, :] == source_ids[:, None]
    dist_sq = jnp.where(coincide, 1.0, delta_x * delta_x + delta_y * delta_y + delta_z * delta_z)
    inverse = jnp.where(coincide, 0.0, lax.rsqrt(dist_sq))
    self_term = jnp.where(coincide, 1.0, 0.0)
    unit_x = delta_x * inverse
    unit_y = delta_y * inverse
    unit_z = delta_z * inverse
    force_x, force_y, force_z = (forces[0][:, None], forces[1][:, None], forces[2][:, None])
    torque_x, torque_y, torque_z = (forces[3][:, None], forces[4][:, None], forces[5][:, None])
    inverse_sq = inverse * inverse
    c_one = 0.75 * inverse
    c_two = 0.75 * inverse_sq
    c_three = 0.375 * inverse_sq * inverse
    along_force = unit_x * force_x + unit_y * force_y + unit_z * force_z
    along_torque = unit_x * torque_x + unit_y * torque_y + unit_z * torque_z
    isotropic = c_one * (1.0 + inverse_sq * (2.0 / 3.0)) + self_term
    dyadic = c_one * (1.0 - 2.0 * inverse_sq) * along_force
    vel_x = isotropic * force_x + dyadic * unit_x + c_two * (torque_y * unit_z - torque_z * unit_y)
    vel_y = isotropic * force_y + dyadic * unit_y + c_two * (torque_z * unit_x - torque_x * unit_z)
    vel_z = isotropic * force_z + dyadic * unit_z + c_two * (torque_x * unit_y - torque_y * unit_x)
    spin_self = 0.75 * self_term - c_three
    spin_x = (
        c_two * (force_y * unit_z - force_z * unit_y)
        + c_three * 3.0 * unit_x * along_torque
        + spin_self * torque_x
    )
    spin_y = (
        c_two * (force_z * unit_x - force_x * unit_z)
        + c_three * 3.0 * unit_y * along_torque
        + spin_self * torque_y
    )
    spin_z = (
        c_two * (force_x * unit_y - force_y * unit_x)
        + c_three * 3.0 * unit_z * along_torque
        + spin_self * torque_z
    )
    return jnp.stack(
        [
            jnp.sum(vel_x, 0),
            jnp.sum(vel_y, 0),
            jnp.sum(vel_z, 0),
            jnp.sum(spin_x, 0),
            jnp.sum(spin_y, 0),
            jnp.sum(spin_z, 0),
        ]
    )


def split_two(value):
    high = lax.reduce_precision(value, exponent_bits=8, mantissa_bits=7)
    low = value - high
    return jnp.stack([high, low]).astype(jnp.bfloat16)


def scatter_kernel(owner_ref, slot_ref, parts_ref, out_ref):
    slots = slot_ref.shape[0]
    owner = owner_ref[...]
    slot = slot_ref[...]
    for k in range(6):
        total = None
        for p in range(2):
            weighted = slot * parts_ref[p, k : k + 1, :]
            term = lax.dot_general(
                owner, weighted, (((1,), (1,)), ((), ())), preferred_element_type=jnp.float32
            )
            total = term if total is None else total + term
        out_ref[:, 0, k * slots : (k + 1) * slots] = total


def gather_kernel(owner_ref, slot_ref, parts_ref, out_ref):
    slots = slot_ref.shape[0]
    owner = owner_ref[...]
    slot = slot_ref[...].astype(jnp.float32)
    for k in range(6):
        picked = None
        for p in range(2):
            part = parts_ref[p, k * slots : (k + 1) * slots, :]
            term = jnp.dot(part, owner, preferred_element_type=jnp.float32)
            picked = term if picked is None else picked + term
        out_ref[k : k + 1, :] = jnp.sum(picked * slot, axis=0, keepdims=True)


def scatter_forces(owner_t, slot_t, end_force):
    owners, ends = owner_t.shape
    slots = slot_t.shape[0]
    parts = split_two(end_force)
    return pl.pallas_call(
        scatter_kernel,
        out_shape=jax.ShapeDtypeStruct((owners, 1, 6 * slots), jnp.float32),
        cost_estimate=pl.CostEstimate(
            flops=2 * 12 * owners * slots * ends, transcendentals=0, bytes_accessed=4 * ends * 300
        ),
    )(owner_t, slot_t, parts)


def gather_velocity(owner_t, slot_t, table):
    owners, ends = owner_t.shape
    slots = slot_t.shape[0]
    return pl.pallas_call(
        gather_kernel,
        out_shape=jax.ShapeDtypeStruct((6, ends), jnp.float32),
        cost_estimate=pl.CostEstimate(
            flops=2 * 12 * owners * slots * ends, transcendentals=0, bytes_accessed=4 * ends * 300
        ),
    )(owner_t, slot_t, split_two(table))


def split_pair(value):
    high = value.astype(jnp.bfloat16)
    low = (value - high.astype(jnp.float32)).astype(jnp.bfloat16)
    return (high, low)


def contact_kernel(step, gather, scatter, *refs):
    bodies_ref, frame_ref, current_ref, other_ref, gaps_ref, steps_ref = refs[:6]
    refs = refs[6:]
    if gather:
        table_ref, refs = refs[0], refs[1:]
    outs = refs
    contacts = frame_ref.shape[1]
    owners = outs[-1].shape[0] if scatter else table_ref.shape[1]
    slots = outs[-1].shape[2] // 6 if scatter else table_ref.shape[0] // 6
    frame = frame_ref[...]
    normal = (frame[0:1], frame[1:2], frame[2:3])

    def crossed(arm):
        return (
            arm[1] * normal[2] - arm[2] * normal[1],
            arm[2] * normal[0] - arm[0] * normal[2],
            arm[0] * normal[1] - arm[1] * normal[0],
        )

    first_lever = crossed((frame[3:4], frame[4:5], frame[5:6]))
    second_lever = crossed((frame[6:7], frame[7:8], frame[8:9]))
    rows = (
        tuple(-v for v in normal) + tuple(-v for v in first_lever),
        normal + second_lever,
    )
    owner_ids = lax.broadcasted_iota(jnp.int32, (owners, contacts), 0)
    slot_ids = lax.broadcasted_iota(jnp.int32, (slots, contacts), 0)
    owner_hot, slot_hot = [], []
    for side in range(2):
        body = bodies_ref[side : side + 1, :]
        owner_hot.append((owner_ids == body // slots).astype(jnp.bfloat16))
        slot_hot.append((slot_ids == body % slots).astype(jnp.bfloat16))
    current = current_ref[...]
    if step == 0:
        shifted = current + MOMENTUM * (current - other_ref[...])
    else:
        shifted = other_ref[...]
    if gather:
        rate = None
        for side in range(2):
            slot_wide = slot_hot[side].astype(jnp.float32)
            for k in range(6):
                picked = None
                for part in split_pair(table_ref[k * slots : (k + 1) * slots, :]):
                    term = jnp.dot(part, owner_hot[side], preferred_element_type=jnp.float32)
                    picked = term if picked is None else picked + term
                velocity = jnp.sum(picked * slot_wide, axis=0, keepdims=True)
                term = rows[side][k] * velocity
                rate = term if rate is None else rate + term
        updated = jnp.maximum(shifted - steps_ref[step] * (gaps_ref[...] + rate), 0.0)
        shifted = updated + MOMENTUM * (updated - current)
        outs[0][...] = updated
        if scatter:
            outs[1][...] = shifted
        outs = outs[1 + int(scatter):]
    if scatter:
        out_ref = outs[0]
        for k in range(6):
            total = None
            for side in range(2):
                for part in split_pair(rows[side][k] * shifted):
                    weighted = slot_hot[side] * part
                    term = lax.dot_general(
                        owner_hot[side], weighted, (((1,), (1,)), ((), ())),
                        preferred_element_type=jnp.float32,
                    )
                    total = term if total is None else total + term
            out_ref[:, 0, k * slots : (k + 1) * slots] = total


def contact_step(step, owners, slots, bodies, frame, state, gaps, steps, table=None, scatter=True):
    contacts = frame.shape[1]
    gather = table is not None
    shapes = []
    if gather:
        shapes += [jax.ShapeDtypeStruct((1, contacts), jnp.float32)] * (1 + int(scatter))
    if scatter:
        shapes.append(jax.ShapeDtypeStruct((owners, 1, 6 * slots), jnp.float32))
    args = (bodies, frame) + tuple(state) + (gaps, steps) + ((table,) if gather else ())
    vmem = pl.BlockSpec(memory_space=pltpu.VMEM)
    specs = [vmem] * 5 + [pl.BlockSpec(memory_space=pltpu.SMEM)] + [vmem] * int(gather)
    return pl.pallas_call(
        functools.partial(contact_kernel, step, gather, scatter),
        out_shape=tuple(shapes),
        in_specs=specs,
        out_specs=tuple(vmem for _ in shapes),
        cost_estimate=pl.CostEstimate(
            flops=2 * 12 * owners * slots * 2 * contacts * (int(gather) + int(scatter)),
            transcendentals=0,
            bytes_accessed=4 * contacts * 600,
        ),
    )(*args)

def pair_kernel(position_ref, place_ref, force_ref, own_ref, out_ref, sums_ref, target_ref):
    targets = target_ref.shape[1]
    chunks = place_ref.shape[0]
    for c in range(3):
        row = position_ref[c : c + 1, :]
        target_ref[c] = jnp.broadcast_to(row, (128, targets)).T
    first_place = place_ref.shape[2] // 128 - 3

    def group(g, carry):
        rows = pl.ds(pl.multiple_of(g * 8, 8), 8)
        target_x = target_ref[0, rows, :]
        target_y = target_ref[1, rows, :]
        target_z = target_ref[2, rows, :]

        def chunk(j, sums):
            place = place_ref[j]
            force = force_ref[j]

            def lane_row(block, row):
                return block[:, row * 128 : (row + 1) * 128]

            r_x = target_x - lane_row(place, first_place)
            r_y = target_y - lane_row(place, first_place + 1)
            r_z = target_z - lane_row(place, first_place + 2)
            f_x, f_y, f_z = (lane_row(force, 0), lane_row(force, 1), lane_row(force, 2))
            t_x, t_y, t_z = (lane_row(force, 3), lane_row(force, 4), lane_row(force, 5))
            dist_sq = r_x * r_x + r_y * r_y + r_z * r_z
            inverse = lax.rsqrt(jnp.maximum(dist_sq, 1.0))
            inverse_sq = inverse * inverse
            c_cross = inverse_sq * inverse
            inverse_fifth = c_cross * inverse_sq
            c_iso = inverse + (2.0 / 3.0) * c_cross
            c_dyad = c_cross - 2.0 * inverse_fifth
            c_spin = 1.5 * inverse_fifth
            c_self = 0.5 * c_cross
            dyad = c_dyad * (r_x * f_x + r_y * f_y + r_z * f_z)
            spin = c_spin * (r_x * t_x + r_y * t_y + r_z * t_z)
            s_x = c_cross * r_x
            s_y = c_cross * r_y
            s_z = c_cross * r_z
            return (
                sums[0] + (c_iso * f_x + dyad * r_x + (t_y * s_z - t_z * s_y)),
                sums[1] + (c_iso * f_y + dyad * r_y + (t_z * s_x - t_x * s_z)),
                sums[2] + (c_iso * f_z + dyad * r_z + (t_x * s_y - t_y * s_x)),
                sums[3] + ((f_y * s_z - f_z * s_y) + spin * r_x - c_self * t_x),
                sums[4] + ((f_z * s_x - f_x * s_z) + spin * r_y - c_self * t_y),
                sums[5] + ((f_x * s_y - f_y * s_x) + spin * r_z - c_self * t_z),
            )

        zero = jnp.zeros((8, 128), jnp.float32)
        sums = lax.fori_loop(0, chunks, chunk, (zero,) * 6, unroll=32)
        for k in range(6):
            sums_ref[k, rows, :] = sums[k]
        return carry

    lax.fori_loop(0, targets // 8, group, 0)
    ones = jnp.ones((8, 128), jnp.bfloat16)
    for k in range(6):
        value = sums_ref[k]
        high = value.astype(jnp.bfloat16)
        rest = value - high.astype(jnp.float32)
        middle = rest.astype(jnp.bfloat16)
        low = (rest - middle.astype(jnp.float32)).astype(jnp.bfloat16)
        total = None
        for part in (high, middle, low):
            term = lax.dot_general(
                ones, part, (((1,), (1,)), ((), ())), preferred_element_type=jnp.float32
            )
            total = term if total is None else total + term
        scale = -0.25 if k < 3 else 1.125
        out_ref[k : k + 1, :] = total[0:1, :] + scale * own_ref[k : k + 1, :]


def mobility_own(positions, places, forces, own_forces):
    own_rows = own_forces.shape[1]
    sources = places.shape[0] * 128
    return pl.pallas_call(
        pair_kernel,
        out_shape=jax.ShapeDtypeStruct((6, own_rows), jnp.float32),
        scratch_shapes=[
            pltpu.VMEM((6, own_rows, 128), jnp.float32),
            pltpu.VMEM((3, own_rows, 128), jnp.float32),
        ],
        cost_estimate=pl.CostEstimate(
            flops=90 * own_rows * sources,
            transcendentals=own_rows * sources,
            bytes_accessed=4 * (9 * sources + 3 * own_rows * 128),
        ),
    )(positions, places, forces, own_forces)

def gather_all(block, devices):
    rows, width = block.shape
    spread = jnp.broadcast_to(block[None], (devices, rows, width))
    spread = lax.all_to_all(spread, AXES, 0, 0, tiled=True)
    return spread.transpose(1, 0, 2).reshape(rows, devices * width)


def scatter_sum(full, devices):
    rows, length = full.shape
    width = length // devices
    pieces = full.reshape(rows, devices, width).transpose(1, 0, 2)
    pieces = lax.all_to_all(pieces, AXES, 0, 0, tiled=True)
    return jnp.sum(pieces, 0)


def per_device(
    positions, contact_bodies, contact_frame, gaps, impulse_now, impulse_prev, step_sizes
):
    devices = lax.axis_size("src") * lax.axis_size("tgt")
    me = lax.axis_index("src") * lax.axis_size("tgt") + lax.axis_index("tgt")
    own_rows = positions.shape[1]
    body_count = own_rows * devices
    gaps_row = gaps.reshape(1, -1)
    state = (impulse_now.reshape(1, -1), impulse_prev.reshape(1, -1))
    (pieces,) = contact_step(0, devices, own_rows, contact_bodies, contact_frame, state, gaps_row, step_sizes)
    own_velocity = jnp.zeros((6, own_rows), jnp.float32)
    for k in range(ITERS):
        pieces = lax.all_to_all(pieces, AXES, 0, 0, tiled=True)
        own_forces = jnp.sum(pieces, 0).reshape(6, own_rows)
        if k == 0:
            block = jnp.concatenate([0.75 * own_forces, positions]).reshape(1, 1, 9 * own_rows)
            places = lax.all_to_all(
                jnp.broadcast_to(block, (devices, 1, 9 * own_rows)), AXES, 0, 0, tiled=True
            )
            forces = places
        else:
            block = (0.75 * own_forces).reshape(1, 1, 6 * own_rows)
            forces = lax.all_to_all(
                jnp.broadcast_to(block, (devices, 1, 6 * own_rows)), AXES, 0, 0, tiled=True
            )
        own_velocity = mobility_own(positions, places, forces, own_forces)
        every = jnp.broadcast_to(own_velocity.reshape(1, 6 * own_rows), (devices, 6 * own_rows))
        every = lax.all_to_all(every, AXES, 0, 0, tiled=True)
        last = k == ITERS - 1
        result = contact_step(
            k, devices, own_rows, contact_bodies, contact_frame, state, gaps_row, step_sizes, every.T, scatter=not last
        )
        state = result[:2]
        if not last:
            pieces = result[2]
    current = state[0].reshape(-1)
    return (current, own_velocity)


def solution(mesh):
    placed = (
        P(None, AXES),
        P(None, AXES),
        P(None, AXES),
        P(AXES),
        P(AXES),
        P(AXES),
        P(),
    )
    return jax.shard_map(
        per_device,
        mesh=mesh,
        in_specs=placed,
        out_specs=(P(AXES), P(None, AXES)),
        check_vma=False,
    )
```

```python
import functools

import jax
import jax.numpy as jnp
from jax import lax
from jax.experimental import pallas as pl
from jax.experimental.pallas import tpu as pltpu
from jax.sharding import PartitionSpec as P

ITERS = 2
MOMENTUM = 0.4
AXES = ("src", "tgt")
SOURCE_BLOCK = 1024


def cross_product(first, second):
    return jnp.stack(
        [
            first[1] * second[2] - first[2] * second[1],
            first[2] * second[0] - first[0] * second[2],
            first[0] * second[1] - first[1] * second[0],
        ]
    )


def contact_rows(frame):
    normal = frame[0:3]
    lever_first = cross_product(frame[3:6], normal)
    lever_second = cross_product(frame[6:9], normal)
    return (jnp.concatenate([-normal, -lever_first]), jnp.concatenate([normal, lever_second]))


def pair_block(target_pos, target_ids, source_pos, source_ids, forces):
    delta_x = target_pos[0][None, :] - source_pos[0][:, None]
    delta_y = target_pos[1][None, :] - source_pos[1][:, None]
    delta_z = target_pos[2][None, :] - source_pos[2][:, None]
    coincide = target_ids[None, :] == source_ids[:, None]
    dist_sq = jnp.where(coincide, 1.0, delta_x * delta_x + delta_y * delta_y + delta_z * delta_z)
    inverse = jnp.where(coincide, 0.0, lax.rsqrt(dist_sq))
    self_term = jnp.where(coincide, 1.0, 0.0)
    unit_x = delta_x * inverse
    unit_y = delta_y * inverse
    unit_z = delta_z * inverse
    force_x, force_y, force_z = (forces[0][:, None], forces[1][:, None], forces[2][:, None])
    torque_x, torque_y, torque_z = (forces[3][:, None], forces[4][:, None], forces[5][:, None])
    inverse_sq = inverse * inverse
    c_one = 0.75 * inverse
    c_two = 0.75 * inverse_sq
    c_three = 0.375 * inverse_sq * inverse
    along_force = unit_x * force_x + unit_y * force_y + unit_z * force_z
    along_torque = unit_x * torque_x + unit_y * torque_y + unit_z * torque_z
    isotropic = c_one * (1.0 + inverse_sq * (2.0 / 3.0)) + self_term
    dyadic = c_one * (1.0 - 2.0 * inverse_sq) * along_force
    vel_x = isotropic * force_x + dyadic * unit_x + c_two * (torque_y * unit_z - torque_z * unit_y)
    vel_y = isotropic * force_y + dyadic * unit_y + c_two * (torque_z * unit_x - torque_x * unit_z)
    vel_z = isotropic * force_z + dyadic * unit_z + c_two * (torque_x * unit_y - torque_y * unit_x)
    spin_self = 0.75 * self_term - c_three
    spin_x = (
        c_two * (force_y * unit_z - force_z * unit_y)
        + c_three * 3.0 * unit_x * along_torque
        + spin_self * torque_x
    )
    spin_y = (
        c_two * (force_z * unit_x - force_x * unit_z)
        + c_three * 3.0 * unit_y * along_torque
        + spin_self * torque_y
    )
    spin_z = (
        c_two * (force_x * unit_y - force_y * unit_x)
        + c_three * 3.0 * unit_z * along_torque
        + spin_self * torque_z
    )
    return jnp.stack(
        [
            jnp.sum(vel_x, 0),
            jnp.sum(vel_y, 0),
            jnp.sum(vel_z, 0),
            jnp.sum(spin_x, 0),
            jnp.sum(spin_y, 0),
            jnp.sum(spin_z, 0),
        ]
    )


def split_two(value):
    high = lax.reduce_precision(value, exponent_bits=8, mantissa_bits=7)
    low = value - high
    return jnp.stack([high, low]).astype(jnp.bfloat16)


def scatter_kernel(owner_ref, slot_ref, parts_ref, out_ref):
    slots = slot_ref.shape[0]
    owner = owner_ref[...]
    slot = slot_ref[...]
    for k in range(6):
        total = None
        for p in range(2):
            weighted = slot * parts_ref[p, k : k + 1, :]
            term = lax.dot_general(
                owner, weighted, (((1,), (1,)), ((), ())), preferred_element_type=jnp.float32
            )
            total = term if total is None else total + term
        out_ref[:, 0, k * slots : (k + 1) * slots] = total


def gather_kernel(owner_ref, slot_ref, parts_ref, out_ref):
    slots = slot_ref.shape[0]
    owner = owner_ref[...]
    slot = slot_ref[...].astype(jnp.float32)
    for k in range(6):
        picked = None
        for p in range(2):
            part = parts_ref[p, k * slots : (k + 1) * slots, :]
            term = jnp.dot(part, owner, preferred_element_type=jnp.float32)
            picked = term if picked is None else picked + term
        out_ref[k : k + 1, :] = jnp.sum(picked * slot, axis=0, keepdims=True)


def scatter_forces(owner_t, slot_t, end_force):
    owners, ends = owner_t.shape
    slots = slot_t.shape[0]
    parts = split_two(end_force)
    return pl.pallas_call(
        scatter_kernel,
        out_shape=jax.ShapeDtypeStruct((owners, 1, 6 * slots), jnp.float32),
        cost_estimate=pl.CostEstimate(
            flops=2 * 12 * owners * slots * ends, transcendentals=0, bytes_accessed=4 * ends * 300
        ),
    )(owner_t, slot_t, parts)


def gather_velocity(owner_t, slot_t, table):
    owners, ends = owner_t.shape
    slots = slot_t.shape[0]
    return pl.pallas_call(
        gather_kernel,
        out_shape=jax.ShapeDtypeStruct((6, ends), jnp.float32),
        cost_estimate=pl.CostEstimate(
            flops=2 * 12 * owners * slots * ends, transcendentals=0, bytes_accessed=4 * ends * 300
        ),
    )(owner_t, slot_t, split_two(table))


def split_pair(value):
    high = value.astype(jnp.bfloat16)
    low = (value - high.astype(jnp.float32)).astype(jnp.bfloat16)
    return (high, low)


def contact_kernel(step, gather, scatter, *refs):
    bodies_ref, frame_ref, current_ref, other_ref, gaps_ref, steps_ref = refs[:6]
    refs = refs[6:]
    if gather:
        table_ref, refs = refs[0], refs[1:]
    outs = refs
    contacts = frame_ref.shape[1]
    owners = outs[-1].shape[0] if scatter else table_ref.shape[1]
    slots = outs[-1].shape[2] // 6 if scatter else table_ref.shape[0] // 6
    frame = frame_ref[...]
    normal = (frame[0:1], frame[1:2], frame[2:3])

    def crossed(arm):
        return (
            arm[1] * normal[2] - arm[2] * normal[1],
            arm[2] * normal[0] - arm[0] * normal[2],
            arm[0] * normal[1] - arm[1] * normal[0],
        )

    first_lever = crossed((frame[3:4], frame[4:5], frame[5:6]))
    second_lever = crossed((frame[6:7], frame[7:8], frame[8:9]))
    rows = (
        tuple(-v for v in normal) + tuple(-v for v in first_lever),
        normal + second_lever,
    )
    owner_ids = lax.broadcasted_iota(jnp.int32, (owners, contacts), 0)
    slot_ids = lax.broadcasted_iota(jnp.int32, (slots, contacts), 0)
    owner_hot, slot_hot = [], []
    for side in range(2):
        body = bodies_ref[side : side + 1, :]
        owner_hot.append((owner_ids == body // slots).astype(jnp.bfloat16))
        slot_hot.append((slot_ids == body % slots).astype(jnp.bfloat16))
    current = current_ref[...]
    if step == 0:
        shifted = current + MOMENTUM * (current - other_ref[...])
    else:
        shifted = other_ref[...]
    if gather:
        rate = None
        for side in range(2):
            slot_wide = slot_hot[side].astype(jnp.float32)
            for k in range(6):
                picked = None
                for part in split_pair(table_ref[k * slots : (k + 1) * slots, :]):
                    term = jnp.dot(part, owner_hot[side], preferred_element_type=jnp.float32)
                    picked = term if picked is None else picked + term
                velocity = jnp.sum(picked * slot_wide, axis=0, keepdims=True)
                term = rows[side][k] * velocity
                rate = term if rate is None else rate + term
        updated = jnp.maximum(shifted - steps_ref[step] * (gaps_ref[...] + rate), 0.0)
        shifted = updated + MOMENTUM * (updated - current)
        outs[0][...] = updated
        if scatter:
            outs[1][...] = shifted
        outs = outs[1 + int(scatter):]
    if scatter:
        out_ref = outs[0]
        for k in range(6):
            total = None
            for side in range(2):
                for part in split_pair(rows[side][k] * shifted):
                    weighted = slot_hot[side] * part
                    term = lax.dot_general(
                        owner_hot[side], weighted, (((1,), (1,)), ((), ())),
                        preferred_element_type=jnp.float32,
                    )
                    total = term if total is None else total + term
            out_ref[:, 0, k * slots : (k + 1) * slots] = total


def contact_step(step, owners, slots, bodies, frame, state, gaps, steps, table=None, scatter=True):
    contacts = frame.shape[1]
    gather = table is not None
    shapes = []
    if gather:
        shapes += [jax.ShapeDtypeStruct((1, contacts), jnp.float32)] * (1 + int(scatter))
    if scatter:
        shapes.append(jax.ShapeDtypeStruct((owners, 1, 6 * slots), jnp.float32))
    args = (bodies, frame) + tuple(state) + (gaps, steps) + ((table,) if gather else ())
    vmem = pl.BlockSpec(memory_space=pltpu.VMEM)
    specs = [vmem] * 5 + [pl.BlockSpec(memory_space=pltpu.SMEM)] + [vmem] * int(gather)
    return pl.pallas_call(
        functools.partial(contact_kernel, step, gather, scatter),
        out_shape=tuple(shapes),
        in_specs=specs,
        out_specs=tuple(vmem for _ in shapes),
        cost_estimate=pl.CostEstimate(
            flops=2 * 12 * owners * slots * 2 * contacts * (int(gather) + int(scatter)),
            transcendentals=0,
            bytes_accessed=4 * contacts * 600,
        ),
    )(*args)

def pair_kernel(position_ref, place_ref, force_ref, own_ref, out_ref, sums_ref, target_ref):
    targets = target_ref.shape[1]
    chunks = place_ref.shape[0]
    for c in range(3):
        row = position_ref[c : c + 1, :]
        target_ref[c] = jnp.broadcast_to(row, (128, targets)).T
    first_place = place_ref.shape[2] // 128 - 3

    def group(g, carry):
        rows = pl.ds(pl.multiple_of(g * 8, 8), 8)
        target_x = target_ref[0, rows, :]
        target_y = target_ref[1, rows, :]
        target_z = target_ref[2, rows, :]

        def chunk(j, sums):
            place = place_ref[j]
            force = force_ref[j]

            def lane_row(block, row):
                return block[:, row * 128 : (row + 1) * 128]

            r_x = target_x - lane_row(place, first_place)
            r_y = target_y - lane_row(place, first_place + 1)
            r_z = target_z - lane_row(place, first_place + 2)
            f_x, f_y, f_z = (lane_row(force, 0), lane_row(force, 1), lane_row(force, 2))
            t_x, t_y, t_z = (lane_row(force, 3), lane_row(force, 4), lane_row(force, 5))
            dist_sq = r_x * r_x + r_y * r_y + r_z * r_z
            inverse = lax.rsqrt(jnp.maximum(dist_sq, 1.0))
            inverse_sq = inverse * inverse
            c_cross = inverse_sq * inverse
            inverse_fifth = c_cross * inverse_sq
            c_iso = inverse + (2.0 / 3.0) * c_cross
            c_dyad = c_cross - 2.0 * inverse_fifth
            c_spin = 1.5 * inverse_fifth
            c_self = 0.5 * c_cross
            dyad = c_dyad * (r_x * f_x + r_y * f_y + r_z * f_z)
            spin = c_spin * (r_x * t_x + r_y * t_y + r_z * t_z)
            s_x = c_cross * r_x
            s_y = c_cross * r_y
            s_z = c_cross * r_z
            return (
                sums[0] + (c_iso * f_x + dyad * r_x + (t_y * s_z - t_z * s_y)),
                sums[1] + (c_iso * f_y + dyad * r_y + (t_z * s_x - t_x * s_z)),
                sums[2] + (c_iso * f_z + dyad * r_z + (t_x * s_y - t_y * s_x)),
                sums[3] + ((f_y * s_z - f_z * s_y) + spin * r_x - c_self * t_x),
                sums[4] + ((f_z * s_x - f_x * s_z) + spin * r_y - c_self * t_y),
                sums[5] + ((f_x * s_y - f_y * s_x) + spin * r_z - c_self * t_z),
            )

        zero = jnp.zeros((8, 128), jnp.float32)
        sums = lax.fori_loop(0, chunks, chunk, (zero,) * 6, unroll=64)
        for k in range(6):
            sums_ref[k, rows, :] = sums[k]
        return carry

    lax.fori_loop(0, targets // 8, group, 0)
    ones = jnp.ones((8, 128), jnp.bfloat16)
    for k in range(6):
        value = sums_ref[k]
        high = value.astype(jnp.bfloat16)
        rest = value - high.astype(jnp.float32)
        middle = rest.astype(jnp.bfloat16)
        low = (rest - middle.astype(jnp.float32)).astype(jnp.bfloat16)
        total = None
        for part in (high, middle, low):
            term = lax.dot_general(
                ones, part, (((1,), (1,)), ((), ())), preferred_element_type=jnp.float32
            )
            total = term if total is None else total + term
        scale = -0.25 if k < 3 else 1.125
        out_ref[k : k + 1, :] = total[0:1, :] + scale * own_ref[k : k + 1, :]


def mobility_own(positions, places, forces, own_forces):
    own_rows = own_forces.shape[1]
    sources = places.shape[0] * 128
    return pl.pallas_call(
        pair_kernel,
        out_shape=jax.ShapeDtypeStruct((6, own_rows), jnp.float32),
        scratch_shapes=[
            pltpu.VMEM((6, own_rows, 128), jnp.float32),
            pltpu.VMEM((3, own_rows, 128), jnp.float32),
        ],
        cost_estimate=pl.CostEstimate(
            flops=90 * own_rows * sources,
            transcendentals=own_rows * sources,
            bytes_accessed=4 * (9 * sources + 3 * own_rows * 128),
        ),
    )(positions, places, forces, own_forces)

def gather_all(block, devices):
    rows, width = block.shape
    spread = jnp.broadcast_to(block[None], (devices, rows, width))
    spread = lax.all_to_all(spread, AXES, 0, 0, tiled=True)
    return spread.transpose(1, 0, 2).reshape(rows, devices * width)


def scatter_sum(full, devices):
    rows, length = full.shape
    width = length // devices
    pieces = full.reshape(rows, devices, width).transpose(1, 0, 2)
    pieces = lax.all_to_all(pieces, AXES, 0, 0, tiled=True)
    return jnp.sum(pieces, 0)


def per_device(
    positions, contact_bodies, contact_frame, gaps, impulse_now, impulse_prev, step_sizes
):
    devices = lax.axis_size("src") * lax.axis_size("tgt")
    me = lax.axis_index("src") * lax.axis_size("tgt") + lax.axis_index("tgt")
    own_rows = positions.shape[1]
    body_count = own_rows * devices
    gaps_row = gaps.reshape(1, -1)
    state = (impulse_now.reshape(1, -1), impulse_prev.reshape(1, -1))
    (pieces,) = contact_step(0, devices, own_rows, contact_bodies, contact_frame, state, gaps_row, step_sizes)
    own_velocity = jnp.zeros((6, own_rows), jnp.float32)
    for k in range(ITERS):
        pieces = lax.all_to_all(pieces, AXES, 0, 0, tiled=True)
        own_forces = jnp.sum(pieces, 0).reshape(6, own_rows)
        if k == 0:
            block = jnp.concatenate([0.75 * own_forces, positions]).reshape(1, 1, 9 * own_rows)
            places = lax.all_to_all(
                jnp.broadcast_to(block, (devices, 1, 9 * own_rows)), AXES, 0, 0, tiled=True
            )
            forces = places
        else:
            block = (0.75 * own_forces).reshape(1, 1, 6 * own_rows)
            forces = lax.all_to_all(
                jnp.broadcast_to(block, (devices, 1, 6 * own_rows)), AXES, 0, 0, tiled=True
            )
        own_velocity = mobility_own(positions, places, forces, own_forces)
        every = jnp.broadcast_to(own_velocity.reshape(1, 6 * own_rows), (devices, 6 * own_rows))
        every = lax.all_to_all(every, AXES, 0, 0, tiled=True)
        last = k == ITERS - 1
        result = contact_step(
            k, devices, own_rows, contact_bodies, contact_frame, state, gaps_row, step_sizes, every.T, scatter=not last
        )
        state = result[:2]
        if not last:
            pieces = result[2]
    current = state[0].reshape(-1)
    return (current, own_velocity)


def solution(mesh):
    placed = (
        P(None, AXES),
        P(None, AXES),
        P(None, AXES),
        P(AXES),
        P(AXES),
        P(AXES),
        P(),
    )
    return jax.shard_map(
        per_device,
        mesh=mesh,
        in_specs=placed,
        out_specs=(P(AXES), P(None, AXES)),
        check_vma=False,
    )
```

```python
import functools

import jax
import jax.numpy as jnp
from jax import lax
from jax.experimental import pallas as pl
from jax.experimental.pallas import tpu as pltpu
from jax.sharding import PartitionSpec as P

ITERS = 2
MOMENTUM = 0.4
AXES = ("src", "tgt")
SOURCE_BLOCK = 1024


def cross_product(first, second):
    return jnp.stack(
        [
            first[1] * second[2] - first[2] * second[1],
            first[2] * second[0] - first[0] * second[2],
            first[0] * second[1] - first[1] * second[0],
        ]
    )


def contact_rows(frame):
    normal = frame[0:3]
    lever_first = cross_product(frame[3:6], normal)
    lever_second = cross_product(frame[6:9], normal)
    return (jnp.concatenate([-normal, -lever_first]), jnp.concatenate([normal, lever_second]))


def pair_block(target_pos, target_ids, source_pos, source_ids, forces):
    delta_x = target_pos[0][None, :] - source_pos[0][:, None]
    delta_y = target_pos[1][None, :] - source_pos[1][:, None]
    delta_z = target_pos[2][None, :] - source_pos[2][:, None]
    coincide = target_ids[None, :] == source_ids[:, None]
    dist_sq = jnp.where(coincide, 1.0, delta_x * delta_x + delta_y * delta_y + delta_z * delta_z)
    inverse = jnp.where(coincide, 0.0, lax.rsqrt(dist_sq))
    self_term = jnp.where(coincide, 1.0, 0.0)
    unit_x = delta_x * inverse
    unit_y = delta_y * inverse
    unit_z = delta_z * inverse
    force_x, force_y, force_z = (forces[0][:, None], forces[1][:, None], forces[2][:, None])
    torque_x, torque_y, torque_z = (forces[3][:, None], forces[4][:, None], forces[5][:, None])
    inverse_sq = inverse * inverse
    c_one = 0.75 * inverse
    c_two = 0.75 * inverse_sq
    c_three = 0.375 * inverse_sq * inverse
    along_force = unit_x * force_x + unit_y * force_y + unit_z * force_z
    along_torque = unit_x * torque_x + unit_y * torque_y + unit_z * torque_z
    isotropic = c_one * (1.0 + inverse_sq * (2.0 / 3.0)) + self_term
    dyadic = c_one * (1.0 - 2.0 * inverse_sq) * along_force
    vel_x = isotropic * force_x + dyadic * unit_x + c_two * (torque_y * unit_z - torque_z * unit_y)
    vel_y = isotropic * force_y + dyadic * unit_y + c_two * (torque_z * unit_x - torque_x * unit_z)
    vel_z = isotropic * force_z + dyadic * unit_z + c_two * (torque_x * unit_y - torque_y * unit_x)
    spin_self = 0.75 * self_term - c_three
    spin_x = (
        c_two * (force_y * unit_z - force_z * unit_y)
        + c_three * 3.0 * unit_x * along_torque
        + spin_self * torque_x
    )
    spin_y = (
        c_two * (force_z * unit_x - force_x * unit_z)
        + c_three * 3.0 * unit_y * along_torque
        + spin_self * torque_y
    )
    spin_z = (
        c_two * (force_x * unit_y - force_y * unit_x)
        + c_three * 3.0 * unit_z * along_torque
        + spin_self * torque_z
    )
    return jnp.stack(
        [
            jnp.sum(vel_x, 0),
            jnp.sum(vel_y, 0),
            jnp.sum(vel_z, 0),
            jnp.sum(spin_x, 0),
            jnp.sum(spin_y, 0),
            jnp.sum(spin_z, 0),
        ]
    )


def split_two(value):
    high = lax.reduce_precision(value, exponent_bits=8, mantissa_bits=7)
    low = value - high
    return jnp.stack([high, low]).astype(jnp.bfloat16)


def scatter_kernel(owner_ref, slot_ref, parts_ref, out_ref):
    slots = slot_ref.shape[0]
    owner = owner_ref[...]
    slot = slot_ref[...]
    for k in range(6):
        total = None
        for p in range(2):
            weighted = slot * parts_ref[p, k : k + 1, :]
            term = lax.dot_general(
                owner, weighted, (((1,), (1,)), ((), ())), preferred_element_type=jnp.float32
            )
            total = term if total is None else total + term
        out_ref[:, 0, k * slots : (k + 1) * slots] = total


def gather_kernel(owner_ref, slot_ref, parts_ref, out_ref):
    slots = slot_ref.shape[0]
    owner = owner_ref[...]
    slot = slot_ref[...].astype(jnp.float32)
    for k in range(6):
        picked = None
        for p in range(2):
            part = parts_ref[p, k * slots : (k + 1) * slots, :]
            term = jnp.dot(part, owner, preferred_element_type=jnp.float32)
            picked = term if picked is None else picked + term
        out_ref[k : k + 1, :] = jnp.sum(picked * slot, axis=0, keepdims=True)


def scatter_forces(owner_t, slot_t, end_force):
    owners, ends = owner_t.shape
    slots = slot_t.shape[0]
    parts = split_two(end_force)
    return pl.pallas_call(
        scatter_kernel,
        out_shape=jax.ShapeDtypeStruct((owners, 1, 6 * slots), jnp.float32),
        cost_estimate=pl.CostEstimate(
            flops=2 * 12 * owners * slots * ends, transcendentals=0, bytes_accessed=4 * ends * 300
        ),
    )(owner_t, slot_t, parts)


def gather_velocity(owner_t, slot_t, table):
    owners, ends = owner_t.shape
    slots = slot_t.shape[0]
    return pl.pallas_call(
        gather_kernel,
        out_shape=jax.ShapeDtypeStruct((6, ends), jnp.float32),
        cost_estimate=pl.CostEstimate(
            flops=2 * 12 * owners * slots * ends, transcendentals=0, bytes_accessed=4 * ends * 300
        ),
    )(owner_t, slot_t, split_two(table))


def split_pair(value):
    high = value.astype(jnp.bfloat16)
    low = (value - high.astype(jnp.float32)).astype(jnp.bfloat16)
    return (high, low)


def contact_kernel(step, gather, scatter, *refs):
    bodies_ref, frame_ref, current_ref, other_ref, gaps_ref, steps_ref = refs[:6]
    refs = refs[6:]
    if gather:
        table_ref, refs = refs[0], refs[1:]
    outs = refs
    contacts = frame_ref.shape[1]
    owners = outs[-1].shape[0] if scatter else table_ref.shape[1]
    slots = outs[-1].shape[2] // 6 if scatter else table_ref.shape[0] // 6
    frame = frame_ref[...]
    normal = (frame[0:1], frame[1:2], frame[2:3])

    def crossed(arm):
        return (
            arm[1] * normal[2] - arm[2] * normal[1],
            arm[2] * normal[0] - arm[0] * normal[2],
            arm[0] * normal[1] - arm[1] * normal[0],
        )

    first_lever = crossed((frame[3:4], frame[4:5], frame[5:6]))
    second_lever = crossed((frame[6:7], frame[7:8], frame[8:9]))
    rows = (
        tuple(-v for v in normal) + tuple(-v for v in first_lever),
        normal + second_lever,
    )
    owner_ids = lax.broadcasted_iota(jnp.int32, (owners, contacts), 0)
    slot_ids = lax.broadcasted_iota(jnp.int32, (slots, contacts), 0)
    owner_hot, slot_hot = [], []
    for side in range(2):
        body = bodies_ref[side : side + 1, :]
        owner_hot.append((owner_ids == body // slots).astype(jnp.bfloat16))
        slot_hot.append((slot_ids == body % slots).astype(jnp.bfloat16))
    current = current_ref[...]
    if step == 0:
        shifted = current + MOMENTUM * (current - other_ref[...])
    else:
        shifted = other_ref[...]
    if gather:
        rate = None
        for side in range(2):
            slot_wide = slot_hot[side].astype(jnp.float32)
            for k in range(6):
                picked = None
                for part in split_pair(table_ref[k * slots : (k + 1) * slots, :]):
                    term = jnp.dot(part, owner_hot[side], preferred_element_type=jnp.float32)
                    picked = term if picked is None else picked + term
                velocity = jnp.sum(picked * slot_wide, axis=0, keepdims=True)
                term = rows[side][k] * velocity
                rate = term if rate is None else rate + term
        updated = jnp.maximum(shifted - steps_ref[step] * (gaps_ref[...] + rate), 0.0)
        shifted = updated + MOMENTUM * (updated - current)
        outs[0][...] = updated
        if scatter:
            outs[1][...] = shifted
        outs = outs[1 + int(scatter):]
    if scatter:
        out_ref = outs[0]
        for k in range(6):
            total = None
            for side in range(2):
                for part in split_pair(rows[side][k] * shifted):
                    weighted = slot_hot[side] * part
                    term = lax.dot_general(
                        owner_hot[side], weighted, (((1,), (1,)), ((), ())),
                        preferred_element_type=jnp.float32,
                    )
                    total = term if total is None else total + term
            out_ref[:, 0, k * slots : (k + 1) * slots] = total


def contact_step(step, owners, slots, bodies, frame, state, gaps, steps, table=None, scatter=True):
    contacts = frame.shape[1]
    gather = table is not None
    shapes = []
    if gather:
        shapes += [jax.ShapeDtypeStruct((1, contacts), jnp.float32)] * (1 + int(scatter))
    if scatter:
        shapes.append(jax.ShapeDtypeStruct((owners, 1, 6 * slots), jnp.float32))
    args = (bodies, frame) + tuple(state) + (gaps, steps) + ((table,) if gather else ())
    vmem = pl.BlockSpec(memory_space=pltpu.VMEM)
    specs = [vmem] * 5 + [pl.BlockSpec(memory_space=pltpu.SMEM)] + [vmem] * int(gather)
    return pl.pallas_call(
        functools.partial(contact_kernel, step, gather, scatter),
        out_shape=tuple(shapes),
        in_specs=specs,
        out_specs=tuple(vmem for _ in shapes),
        cost_estimate=pl.CostEstimate(
            flops=2 * 12 * owners * slots * 2 * contacts * (int(gather) + int(scatter)),
            transcendentals=0,
            bytes_accessed=4 * contacts * 600,
        ),
    )(*args)

def pair_kernel(position_ref, place_ref, force_ref, own_ref, out_ref, sums_ref, target_ref):
    targets = target_ref.shape[1]
    chunks = place_ref.shape[0]
    for c in range(3):
        row = position_ref[c : c + 1, :]
        target_ref[c] = jnp.broadcast_to(row, (128, targets)).T
    first_place = place_ref.shape[2] // 128 - 3

    def group(g, carry):
        rows = pl.ds(pl.multiple_of(g * 8, 8), 8)
        target_x = target_ref[0, rows, :]
        target_y = target_ref[1, rows, :]
        target_z = target_ref[2, rows, :]

        def chunk(j, sums):
            place = place_ref[j]
            force = force_ref[j]

            def lane_row(block, row):
                return block[:, row * 128 : (row + 1) * 128]

            r_x = target_x - lane_row(place, first_place)
            r_y = target_y - lane_row(place, first_place + 1)
            r_z = target_z - lane_row(place, first_place + 2)
            f_x, f_y, f_z = (lane_row(force, 0), lane_row(force, 1), lane_row(force, 2))
            t_x, t_y, t_z = (lane_row(force, 3), lane_row(force, 4), lane_row(force, 5))
            dist_sq = r_x * r_x + r_y * r_y + r_z * r_z
            inverse = lax.rsqrt(jnp.maximum(dist_sq, 1.0))
            inverse_sq = inverse * inverse
            c_cross = inverse_sq * inverse
            inverse_fifth = c_cross * inverse_sq
            c_iso = inverse + (2.0 / 3.0) * c_cross
            c_dyad = c_cross - 2.0 * inverse_fifth
            c_spin = 1.5 * inverse_fifth
            c_self = 0.5 * c_cross
            dyad = c_dyad * (r_x * f_x + r_y * f_y + r_z * f_z)
            spin = c_spin * (r_x * t_x + r_y * t_y + r_z * t_z)
            s_x = c_cross * r_x
            s_y = c_cross * r_y
            s_z = c_cross * r_z
            return (
                sums[0] + (c_iso * f_x + dyad * r_x + (t_y * s_z - t_z * s_y)),
                sums[1] + (c_iso * f_y + dyad * r_y + (t_z * s_x - t_x * s_z)),
                sums[2] + (c_iso * f_z + dyad * r_z + (t_x * s_y - t_y * s_x)),
                sums[3] + ((f_y * s_z - f_z * s_y) + spin * r_x - c_self * t_x),
                sums[4] + ((f_z * s_x - f_x * s_z) + spin * r_y - c_self * t_y),
                sums[5] + ((f_x * s_y - f_y * s_x) + spin * r_z - c_self * t_z),
            )

        zero = jnp.zeros((8, 128), jnp.float32)
        sums = lax.fori_loop(0, chunks, chunk, (zero,) * 6, unroll=True)
        for k in range(6):
            sums_ref[k, rows, :] = sums[k]
        return carry

    lax.fori_loop(0, targets // 8, group, 0)
    ones = jnp.ones((8, 128), jnp.bfloat16)
    for k in range(6):
        value = sums_ref[k]
        high = value.astype(jnp.bfloat16)
        rest = value - high.astype(jnp.float32)
        middle = rest.astype(jnp.bfloat16)
        low = (rest - middle.astype(jnp.float32)).astype(jnp.bfloat16)
        total = None
        for part in (high, middle, low):
            term = lax.dot_general(
                ones, part, (((1,), (1,)), ((), ())), preferred_element_type=jnp.float32
            )
            total = term if total is None else total + term
        scale = -0.25 if k < 3 else 1.125
        out_ref[k : k + 1, :] = total[0:1, :] + scale * own_ref[k : k + 1, :]


def mobility_own(positions, places, forces, own_forces):
    own_rows = own_forces.shape[1]
    sources = places.shape[0] * 128
    return pl.pallas_call(
        pair_kernel,
        out_shape=jax.ShapeDtypeStruct((6, own_rows), jnp.float32),
        scratch_shapes=[
            pltpu.VMEM((6, own_rows, 128), jnp.float32),
            pltpu.VMEM((3, own_rows, 128), jnp.float32),
        ],
        cost_estimate=pl.CostEstimate(
            flops=90 * own_rows * sources,
            transcendentals=own_rows * sources,
            bytes_accessed=4 * (9 * sources + 3 * own_rows * 128),
        ),
    )(positions, places, forces, own_forces)

def gather_all(block, devices):
    rows, width = block.shape
    spread = jnp.broadcast_to(block[None], (devices, rows, width))
    spread = lax.all_to_all(spread, AXES, 0, 0, tiled=True)
    return spread.transpose(1, 0, 2).reshape(rows, devices * width)


def scatter_sum(full, devices):
    rows, length = full.shape
    width = length // devices
    pieces = full.reshape(rows, devices, width).transpose(1, 0, 2)
    pieces = lax.all_to_all(pieces, AXES, 0, 0, tiled=True)
    return jnp.sum(pieces, 0)


def per_device(
    positions, contact_bodies, contact_frame, gaps, impulse_now, impulse_prev, step_sizes
):
    devices = lax.axis_size("src") * lax.axis_size("tgt")
    me = lax.axis_index("src") * lax.axis_size("tgt") + lax.axis_index("tgt")
    own_rows = positions.shape[1]
    body_count = own_rows * devices
    gaps_row = gaps.reshape(1, -1)
    state = (impulse_now.reshape(1, -1), impulse_prev.reshape(1, -1))
    (pieces,) = contact_step(0, devices, own_rows, contact_bodies, contact_frame, state, gaps_row, step_sizes)
    own_velocity = jnp.zeros((6, own_rows), jnp.float32)
    for k in range(ITERS):
        pieces = lax.all_to_all(pieces, AXES, 0, 0, tiled=True)
        own_forces = jnp.sum(pieces, 0).reshape(6, own_rows)
        if k == 0:
            block = jnp.concatenate([0.75 * own_forces, positions]).reshape(1, 1, 9 * own_rows)
            places = lax.all_to_all(
                jnp.broadcast_to(block, (devices, 1, 9 * own_rows)), AXES, 0, 0, tiled=True
            )
            forces = places
        else:
            block = (0.75 * own_forces).reshape(1, 1, 6 * own_rows)
            forces = lax.all_to_all(
                jnp.broadcast_to(block, (devices, 1, 6 * own_rows)), AXES, 0, 0, tiled=True
            )
        own_velocity = mobility_own(positions, places, forces, own_forces)
        every = jnp.broadcast_to(own_velocity.reshape(1, 6 * own_rows), (devices, 6 * own_rows))
        every = lax.all_to_all(every, AXES, 0, 0, tiled=True)
        last = k == ITERS - 1
        result = contact_step(
            k, devices, own_rows, contact_bodies, contact_frame, state, gaps_row, step_sizes, every.T, scatter=not last
        )
        state = result[:2]
        if not last:
            pieces = result[2]
    current = state[0].reshape(-1)
    return (current, own_velocity)


def solution(mesh):
    placed = (
        P(None, AXES),
        P(None, AXES),
        P(None, AXES),
        P(AXES),
        P(AXES),
        P(AXES),
        P(),
    )
    return jax.shard_map(
        per_device,
        mesh=mesh,
        in_specs=placed,
        out_specs=(P(AXES), P(None, AXES)),
        check_vma=False,
    )
```

```python
import functools

import jax
import jax.numpy as jnp
from jax import lax
from jax.experimental import pallas as pl
from jax.experimental.pallas import tpu as pltpu
from jax.sharding import PartitionSpec as P

ITERS = 2
MOMENTUM = 0.4
AXES = ("src", "tgt")
SOURCE_BLOCK = 1024


def cross_product(first, second):
    return jnp.stack(
        [
            first[1] * second[2] - first[2] * second[1],
            first[2] * second[0] - first[0] * second[2],
            first[0] * second[1] - first[1] * second[0],
        ]
    )


def contact_rows(frame):
    normal = frame[0:3]
    lever_first = cross_product(frame[3:6], normal)
    lever_second = cross_product(frame[6:9], normal)
    return (jnp.concatenate([-normal, -lever_first]), jnp.concatenate([normal, lever_second]))


def pair_block(target_pos, target_ids, source_pos, source_ids, forces):
    delta_x = target_pos[0][None, :] - source_pos[0][:, None]
    delta_y = target_pos[1][None, :] - source_pos[1][:, None]
    delta_z = target_pos[2][None, :] - source_pos[2][:, None]
    coincide = target_ids[None, :] == source_ids[:, None]
    dist_sq = jnp.where(coincide, 1.0, delta_x * delta_x + delta_y * delta_y + delta_z * delta_z)
    inverse = jnp.where(coincide, 0.0, lax.rsqrt(dist_sq))
    self_term = jnp.where(coincide, 1.0, 0.0)
    unit_x = delta_x * inverse
    unit_y = delta_y * inverse
    unit_z = delta_z * inverse
    force_x, force_y, force_z = (forces[0][:, None], forces[1][:, None], forces[2][:, None])
    torque_x, torque_y, torque_z = (forces[3][:, None], forces[4][:, None], forces[5][:, None])
    inverse_sq = inverse * inverse
    c_one = 0.75 * inverse
    c_two = 0.75 * inverse_sq
    c_three = 0.375 * inverse_sq * inverse
    along_force = unit_x * force_x + unit_y * force_y + unit_z * force_z
    along_torque = unit_x * torque_x + unit_y * torque_y + unit_z * torque_z
    isotropic = c_one * (1.0 + inverse_sq * (2.0 / 3.0)) + self_term
    dyadic = c_one * (1.0 - 2.0 * inverse_sq) * along_force
    vel_x = isotropic * force_x + dyadic * unit_x + c_two * (torque_y * unit_z - torque_z * unit_y)
    vel_y = isotropic * force_y + dyadic * unit_y + c_two * (torque_z * unit_x - torque_x * unit_z)
    vel_z = isotropic * force_z + dyadic * unit_z + c_two * (torque_x * unit_y - torque_y * unit_x)
    spin_self = 0.75 * self_term - c_three
    spin_x = (
        c_two * (force_y * unit_z - force_z * unit_y)
        + c_three * 3.0 * unit_x * along_torque
        + spin_self * torque_x
    )
    spin_y = (
        c_two * (force_z * unit_x - force_x * unit_z)
        + c_three * 3.0 * unit_y * along_torque
        + spin_self * torque_y
    )
    spin_z = (
        c_two * (force_x * unit_y - force_y * unit_x)
        + c_three * 3.0 * unit_z * along_torque
        + spin_self * torque_z
    )
    return jnp.stack(
        [
            jnp.sum(vel_x, 0),
            jnp.sum(vel_y, 0),
            jnp.sum(vel_z, 0),
            jnp.sum(spin_x, 0),
            jnp.sum(spin_y, 0),
            jnp.sum(spin_z, 0),
        ]
    )


def split_two(value):
    high = lax.reduce_precision(value, exponent_bits=8, mantissa_bits=7)
    low = value - high
    return jnp.stack([high, low]).astype(jnp.bfloat16)


def scatter_kernel(owner_ref, slot_ref, parts_ref, out_ref):
    slots = slot_ref.shape[0]
    owner = owner_ref[...]
    slot = slot_ref[...]
    for k in range(6):
        total = None
        for p in range(2):
            weighted = slot * parts_ref[p, k : k + 1, :]
            term = lax.dot_general(
                owner, weighted, (((1,), (1,)), ((), ())), preferred_element_type=jnp.float32
            )
            total = term if total is None else total + term
        out_ref[:, 0, k * slots : (k + 1) * slots] = total


def gather_kernel(owner_ref, slot_ref, parts_ref, out_ref):
    slots = slot_ref.shape[0]
    owner = owner_ref[...]
    slot = slot_ref[...].astype(jnp.float32)
    for k in range(6):
        picked = None
        for p in range(2):
            part = parts_ref[p, k * slots : (k + 1) * slots, :]
            term = jnp.dot(part, owner, preferred_element_type=jnp.float32)
            picked = term if picked is None else picked + term
        out_ref[k : k + 1, :] = jnp.sum(picked * slot, axis=0, keepdims=True)


def scatter_forces(owner_t, slot_t, end_force):
    owners, ends = owner_t.shape
    slots = slot_t.shape[0]
    parts = split_two(end_force)
    return pl.pallas_call(
        scatter_kernel,
        out_shape=jax.ShapeDtypeStruct((owners, 1, 6 * slots), jnp.float32),
        cost_estimate=pl.CostEstimate(
            flops=2 * 12 * owners * slots * ends, transcendentals=0, bytes_accessed=4 * ends * 300
        ),
    )(owner_t, slot_t, parts)


def gather_velocity(owner_t, slot_t, table):
    owners, ends = owner_t.shape
    slots = slot_t.shape[0]
    return pl.pallas_call(
        gather_kernel,
        out_shape=jax.ShapeDtypeStruct((6, ends), jnp.float32),
        cost_estimate=pl.CostEstimate(
            flops=2 * 12 * owners * slots * ends, transcendentals=0, bytes_accessed=4 * ends * 300
        ),
    )(owner_t, slot_t, split_two(table))


def split_pair(value):
    high = value.astype(jnp.bfloat16)
    low = (value - high.astype(jnp.float32)).astype(jnp.bfloat16)
    return (high, low)


def contact_kernel(step, gather, scatter, *refs):
    bodies_ref, frame_ref, current_ref, other_ref, gaps_ref, steps_ref = refs[:6]
    refs = refs[6:]
    if gather:
        table_ref, refs = refs[0], refs[1:]
    outs = refs
    contacts = frame_ref.shape[1]
    owners = outs[-1].shape[0] if scatter else table_ref.shape[1]
    slots = outs[-1].shape[2] // 6 if scatter else table_ref.shape[0] // 6
    frame = frame_ref[...]
    normal = (frame[0:1], frame[1:2], frame[2:3])

    def crossed(arm):
        return (
            arm[1] * normal[2] - arm[2] * normal[1],
            arm[2] * normal[0] - arm[0] * normal[2],
            arm[0] * normal[1] - arm[1] * normal[0],
        )

    first_lever = crossed((frame[3:4], frame[4:5], frame[5:6]))
    second_lever = crossed((frame[6:7], frame[7:8], frame[8:9]))
    rows = (
        tuple(-v for v in normal) + tuple(-v for v in first_lever),
        normal + second_lever,
    )
    owner_ids = lax.broadcasted_iota(jnp.int32, (owners, contacts), 0)
    slot_ids = lax.broadcasted_iota(jnp.int32, (slots, contacts), 0)
    owner_hot, slot_hot = [], []
    for side in range(2):
        body = bodies_ref[side : side + 1, :]
        owner_hot.append((owner_ids == body // slots).astype(jnp.bfloat16))
        slot_hot.append((slot_ids == body % slots).astype(jnp.bfloat16))
    current = current_ref[...]
    if step == 0:
        shifted = current + MOMENTUM * (current - other_ref[...])
    else:
        shifted = other_ref[...]
    if gather:
        rate = None
        for side in range(2):
            slot_wide = slot_hot[side].astype(jnp.float32)
            for k in range(6):
                picked = None
                for part in split_pair(table_ref[k * slots : (k + 1) * slots, :]):
                    term = jnp.dot(part, owner_hot[side], preferred_element_type=jnp.float32)
                    picked = term if picked is None else picked + term
                velocity = jnp.sum(picked * slot_wide, axis=0, keepdims=True)
                term = rows[side][k] * velocity
                rate = term if rate is None else rate + term
        updated = jnp.maximum(shifted - steps_ref[step] * (gaps_ref[...] + rate), 0.0)
        shifted = updated + MOMENTUM * (updated - current)
        outs[0][...] = updated
        if scatter:
            outs[1][...] = shifted
        outs = outs[1 + int(scatter):]
    if scatter:
        out_ref = outs[0]
        for k in range(6):
            total = None
            for side in range(2):
                for part in split_pair(rows[side][k] * shifted):
                    weighted = slot_hot[side] * part
                    term = lax.dot_general(
                        owner_hot[side], weighted, (((1,), (1,)), ((), ())),
                        preferred_element_type=jnp.float32,
                    )
                    total = term if total is None else total + term
            out_ref[:, 0, k * slots : (k + 1) * slots] = total


def contact_step(step, owners, slots, bodies, frame, state, gaps, steps, table=None, scatter=True):
    contacts = frame.shape[1]
    gather = table is not None
    shapes = []
    if gather:
        shapes += [jax.ShapeDtypeStruct((1, contacts), jnp.float32)] * (1 + int(scatter))
    if scatter:
        shapes.append(jax.ShapeDtypeStruct((owners, 1, 6 * slots), jnp.float32))
    args = (bodies, frame) + tuple(state) + (gaps, steps) + ((table,) if gather else ())
    vmem = pl.BlockSpec(memory_space=pltpu.VMEM)
    specs = [vmem] * 5 + [pl.BlockSpec(memory_space=pltpu.SMEM)] + [vmem] * int(gather)
    return pl.pallas_call(
        functools.partial(contact_kernel, step, gather, scatter),
        out_shape=tuple(shapes),
        in_specs=specs,
        out_specs=tuple(vmem for _ in shapes),
        cost_estimate=pl.CostEstimate(
            flops=2 * 12 * owners * slots * 2 * contacts * (int(gather) + int(scatter)),
            transcendentals=0,
            bytes_accessed=4 * contacts * 600,
        ),
    )(*args)

def pair_kernel(position_ref, place_ref, force_ref, own_ref, out_ref, sums_ref, target_ref):
    targets = target_ref.shape[1]
    chunks = place_ref.shape[0]
    for c in range(3):
        row = position_ref[c : c + 1, :]
        target_ref[c] = jnp.broadcast_to(row, (128, targets)).T
    first_place = place_ref.shape[2] // 128 - 3

    def group(g, carry):
        rows = pl.ds(pl.multiple_of(g * 8, 8), 8)
        target_x = target_ref[0, rows, :]
        target_y = target_ref[1, rows, :]
        target_z = target_ref[2, rows, :]

        def chunk(j, sums):
            place = place_ref[j]
            force = force_ref[j]

            def lane_row(block, row):
                return block[:, row * 128 : (row + 1) * 128]

            r_x = target_x - lane_row(place, first_place)
            r_y = target_y - lane_row(place, first_place + 1)
            r_z = target_z - lane_row(place, first_place + 2)
            f_x, f_y, f_z = (lane_row(force, 0), lane_row(force, 1), lane_row(force, 2))
            t_x, t_y, t_z = (lane_row(force, 3), lane_row(force, 4), lane_row(force, 5))
            dist_sq = r_x * r_x + r_y * r_y + r_z * r_z
            inverse = lax.rsqrt(jnp.maximum(dist_sq, 1.0))
            inverse_sq = inverse * inverse
            c_cross = inverse_sq * inverse
            inverse_fifth = c_cross * inverse_sq
            c_iso = inverse + (2.0 / 3.0) * c_cross
            c_dyad = c_cross - 2.0 * inverse_fifth
            c_spin = 1.5 * inverse_fifth
            c_self = 0.5 * c_cross
            dyad = c_dyad * (r_x * f_x + r_y * f_y + r_z * f_z)
            spin = c_spin * (r_x * t_x + r_y * t_y + r_z * t_z)
            s_x = c_cross * r_x
            s_y = c_cross * r_y
            s_z = c_cross * r_z
            return (
                sums[0] + (c_iso * f_x + dyad * r_x + (t_y * s_z - t_z * s_y)),
                sums[1] + (c_iso * f_y + dyad * r_y + (t_z * s_x - t_x * s_z)),
                sums[2] + (c_iso * f_z + dyad * r_z + (t_x * s_y - t_y * s_x)),
                sums[3] + ((f_y * s_z - f_z * s_y) + spin * r_x - c_self * t_x),
                sums[4] + ((f_z * s_x - f_x * s_z) + spin * r_y - c_self * t_y),
                sums[5] + ((f_x * s_y - f_y * s_x) + spin * r_z - c_self * t_z),
            )

        zero = jnp.zeros((8, 128), jnp.float32)
        sums = lax.fori_loop(0, chunks, chunk, (zero,) * 6, unroll=64)
        for k in range(6):
            sums_ref[k, rows, :] = sums[k]
        return carry

    lax.fori_loop(0, targets // 8, group, 0, unroll=2)
    ones = jnp.ones((8, 128), jnp.bfloat16)
    for k in range(6):
        value = sums_ref[k]
        high = value.astype(jnp.bfloat16)
        rest = value - high.astype(jnp.float32)
        middle = rest.astype(jnp.bfloat16)
        low = (rest - middle.astype(jnp.float32)).astype(jnp.bfloat16)
        total = None
        for part in (high, middle, low):
            term = lax.dot_general(
                ones, part, (((1,), (1,)), ((), ())), preferred_element_type=jnp.float32
            )
            total = term if total is None else total + term
        scale = -0.25 if k < 3 else 1.125
        out_ref[k : k + 1, :] = total[0:1, :] + scale * own_ref[k : k + 1, :]


def mobility_own(positions, places, forces, own_forces):
    own_rows = own_forces.shape[1]
    sources = places.shape[0] * 128
    return pl.pallas_call(
        pair_kernel,
        out_shape=jax.ShapeDtypeStruct((6, own_rows), jnp.float32),
        scratch_shapes=[
            pltpu.VMEM((6, own_rows, 128), jnp.float32),
            pltpu.VMEM((3, own_rows, 128), jnp.float32),
        ],
        cost_estimate=pl.CostEstimate(
            flops=90 * own_rows * sources,
            transcendentals=own_rows * sources,
            bytes_accessed=4 * (9 * sources + 3 * own_rows * 128),
        ),
    )(positions, places, forces, own_forces)

def gather_all(block, devices):
    rows, width = block.shape
    spread = jnp.broadcast_to(block[None], (devices, rows, width))
    spread = lax.all_to_all(spread, AXES, 0, 0, tiled=True)
    return spread.transpose(1, 0, 2).reshape(rows, devices * width)


def scatter_sum(full, devices):
    rows, length = full.shape
    width = length // devices
    pieces = full.reshape(rows, devices, width).transpose(1, 0, 2)
    pieces = lax.all_to_all(pieces, AXES, 0, 0, tiled=True)
    return jnp.sum(pieces, 0)


def per_device(
    positions, contact_bodies, contact_frame, gaps, impulse_now, impulse_prev, step_sizes
):
    devices = lax.axis_size("src") * lax.axis_size("tgt")
    me = lax.axis_index("src") * lax.axis_size("tgt") + lax.axis_index("tgt")
    own_rows = positions.shape[1]
    body_count = own_rows * devices
    gaps_row = gaps.reshape(1, -1)
    state = (impulse_now.reshape(1, -1), impulse_prev.reshape(1, -1))
    (pieces,) = contact_step(0, devices, own_rows, contact_bodies, contact_frame, state, gaps_row, step_sizes)
    own_velocity = jnp.zeros((6, own_rows), jnp.float32)
    for k in range(ITERS):
        pieces = lax.all_to_all(pieces, AXES, 0, 0, tiled=True)
        own_forces = jnp.sum(pieces, 0).reshape(6, own_rows)
        if k == 0:
            block = jnp.concatenate([0.75 * own_forces, positions]).reshape(1, 1, 9 * own_rows)
            places = lax.all_to_all(
                jnp.broadcast_to(block, (devices, 1, 9 * own_rows)), AXES, 0, 0, tiled=True
            )
            forces = places
        else:
            block = (0.75 * own_forces).reshape(1, 1, 6 * own_rows)
            forces = lax.all_to_all(
                jnp.broadcast_to(block, (devices, 1, 6 * own_rows)), AXES, 0, 0, tiled=True
            )
        own_velocity = mobility_own(positions, places, forces, own_forces)
        every = jnp.broadcast_to(own_velocity.reshape(1, 6 * own_rows), (devices, 6 * own_rows))
        every = lax.all_to_all(every, AXES, 0, 0, tiled=True)
        last = k == ITERS - 1
        result = contact_step(
            k, devices, own_rows, contact_bodies, contact_frame, state, gaps_row, step_sizes, every.T, scatter=not last
        )
        state = result[:2]
        if not last:
            pieces = result[2]
    current = state[0].reshape(-1)
    return (current, own_velocity)


def solution(mesh):
    placed = (
        P(None, AXES),
        P(None, AXES),
        P(None, AXES),
        P(AXES),
        P(AXES),
        P(AXES),
        P(),
    )
    return jax.shard_map(
        per_device,
        mesh=mesh,
        in_specs=placed,
        out_specs=(P(AXES), P(None, AXES)),
        check_vma=False,
    )
```

```python
import functools

import jax
import jax.numpy as jnp
from jax import lax
from jax.experimental import pallas as pl
from jax.experimental.pallas import tpu as pltpu
from jax.sharding import PartitionSpec as P

ITERS = 2
MOMENTUM = 0.4
AXES = ("src", "tgt")
SOURCE_BLOCK = 1024


def cross_product(first, second):
    return jnp.stack(
        [
            first[1] * second[2] - first[2] * second[1],
            first[2] * second[0] - first[0] * second[2],
            first[0] * second[1] - first[1] * second[0],
        ]
    )


def contact_rows(frame):
    normal = frame[0:3]
    lever_first = cross_product(frame[3:6], normal)
    lever_second = cross_product(frame[6:9], normal)
    return (jnp.concatenate([-normal, -lever_first]), jnp.concatenate([normal, lever_second]))


def pair_block(target_pos, target_ids, source_pos, source_ids, forces):
    delta_x = target_pos[0][None, :] - source_pos[0][:, None]
    delta_y = target_pos[1][None, :] - source_pos[1][:, None]
    delta_z = target_pos[2][None, :] - source_pos[2][:, None]
    coincide = target_ids[None, :] == source_ids[:, None]
    dist_sq = jnp.where(coincide, 1.0, delta_x * delta_x + delta_y * delta_y + delta_z * delta_z)
    inverse = jnp.where(coincide, 0.0, lax.rsqrt(dist_sq))
    self_term = jnp.where(coincide, 1.0, 0.0)
    unit_x = delta_x * inverse
    unit_y = delta_y * inverse
    unit_z = delta_z * inverse
    force_x, force_y, force_z = (forces[0][:, None], forces[1][:, None], forces[2][:, None])
    torque_x, torque_y, torque_z = (forces[3][:, None], forces[4][:, None], forces[5][:, None])
    inverse_sq = inverse * inverse
    c_one = 0.75 * inverse
    c_two = 0.75 * inverse_sq
    c_three = 0.375 * inverse_sq * inverse
    along_force = unit_x * force_x + unit_y * force_y + unit_z * force_z
    along_torque = unit_x * torque_x + unit_y * torque_y + unit_z * torque_z
    isotropic = c_one * (1.0 + inverse_sq * (2.0 / 3.0)) + self_term
    dyadic = c_one * (1.0 - 2.0 * inverse_sq) * along_force
    vel_x = isotropic * force_x + dyadic * unit_x + c_two * (torque_y * unit_z - torque_z * unit_y)
    vel_y = isotropic * force_y + dyadic * unit_y + c_two * (torque_z * unit_x - torque_x * unit_z)
    vel_z = isotropic * force_z + dyadic * unit_z + c_two * (torque_x * unit_y - torque_y * unit_x)
    spin_self = 0.75 * self_term - c_three
    spin_x = (
        c_two * (force_y * unit_z - force_z * unit_y)
        + c_three * 3.0 * unit_x * along_torque
        + spin_self * torque_x
    )
    spin_y = (
        c_two * (force_z * unit_x - force_x * unit_z)
        + c_three * 3.0 * unit_y * along_torque
        + spin_self * torque_y
    )
    spin_z = (
        c_two * (force_x * unit_y - force_y * unit_x)
        + c_three * 3.0 * unit_z * along_torque
        + spin_self * torque_z
    )
    return jnp.stack(
        [
            jnp.sum(vel_x, 0),
            jnp.sum(vel_y, 0),
            jnp.sum(vel_z, 0),
            jnp.sum(spin_x, 0),
            jnp.sum(spin_y, 0),
            jnp.sum(spin_z, 0),
        ]
    )


def split_two(value):
    high = lax.reduce_precision(value, exponent_bits=8, mantissa_bits=7)
    low = value - high
    return jnp.stack([high, low]).astype(jnp.bfloat16)


def scatter_kernel(owner_ref, slot_ref, parts_ref, out_ref):
    slots = slot_ref.shape[0]
    owner = owner_ref[...]
    slot = slot_ref[...]
    for k in range(6):
        total = None
        for p in range(2):
            weighted = slot * parts_ref[p, k : k + 1, :]
            term = lax.dot_general(
                owner, weighted, (((1,), (1,)), ((), ())), preferred_element_type=jnp.float32
            )
            total = term if total is None else total + term
        out_ref[:, 0, k * slots : (k + 1) * slots] = total


def gather_kernel(owner_ref, slot_ref, parts_ref, out_ref):
    slots = slot_ref.shape[0]
    owner = owner_ref[...]
    slot = slot_ref[...].astype(jnp.float32)
    for k in range(6):
        picked = None
        for p in range(2):
            part = parts_ref[p, k * slots : (k + 1) * slots, :]
            term = jnp.dot(part, owner, preferred_element_type=jnp.float32)
            picked = term if picked is None else picked + term
        out_ref[k : k + 1, :] = jnp.sum(picked * slot, axis=0, keepdims=True)


def scatter_forces(owner_t, slot_t, end_force):
    owners, ends = owner_t.shape
    slots = slot_t.shape[0]
    parts = split_two(end_force)
    return pl.pallas_call(
        scatter_kernel,
        out_shape=jax.ShapeDtypeStruct((owners, 1, 6 * slots), jnp.float32),
        cost_estimate=pl.CostEstimate(
            flops=2 * 12 * owners * slots * ends, transcendentals=0, bytes_accessed=4 * ends * 300
        ),
    )(owner_t, slot_t, parts)


def gather_velocity(owner_t, slot_t, table):
    owners, ends = owner_t.shape
    slots = slot_t.shape[0]
    return pl.pallas_call(
        gather_kernel,
        out_shape=jax.ShapeDtypeStruct((6, ends), jnp.float32),
        cost_estimate=pl.CostEstimate(
            flops=2 * 12 * owners * slots * ends, transcendentals=0, bytes_accessed=4 * ends * 300
        ),
    )(owner_t, slot_t, split_two(table))


def split_pair(value):
    high = value.astype(jnp.bfloat16)
    low = (value - high.astype(jnp.float32)).astype(jnp.bfloat16)
    return (high, low)


def contact_kernel(step, gather, scatter, *refs):
    bodies_ref, frame_ref, current_ref, other_ref, gaps_ref, steps_ref = refs[:6]
    refs = refs[6:]
    if gather:
        table_ref, refs = refs[0], refs[1:]
    outs = refs
    contacts = frame_ref.shape[1]
    owners = outs[-1].shape[0] if scatter else table_ref.shape[2]
    slots = outs[-1].shape[2] // 6 if scatter else table_ref.shape[1] // 6
    frame = frame_ref[...]
    normal = (frame[0:1], frame[1:2], frame[2:3])

    def crossed(arm):
        return (
            arm[1] * normal[2] - arm[2] * normal[1],
            arm[2] * normal[0] - arm[0] * normal[2],
            arm[0] * normal[1] - arm[1] * normal[0],
        )

    first_lever = crossed((frame[3:4], frame[4:5], frame[5:6]))
    second_lever = crossed((frame[6:7], frame[7:8], frame[8:9]))
    rows = (
        tuple(-v for v in normal) + tuple(-v for v in first_lever),
        normal + second_lever,
    )
    owner_ids = lax.broadcasted_iota(jnp.int32, (owners, contacts), 0)
    slot_ids = lax.broadcasted_iota(jnp.int32, (slots, contacts), 0)
    owner_hot, slot_hot = [], []
    for side in range(2):
        body = bodies_ref[side : side + 1, :]
        owner_hot.append((owner_ids == body // slots).astype(jnp.bfloat16))
        slot_hot.append((slot_ids == body % slots).astype(jnp.bfloat16))
    current = current_ref[...]
    if step == 0:
        shifted = current + MOMENTUM * (current - other_ref[...])
    else:
        shifted = other_ref[...]
    if gather:
        rate = None
        for side in range(2):
            slot_wide = slot_hot[side].astype(jnp.float32)
            for k in range(6):
                picked = None
                for part in (table_ref[0, k * slots : (k + 1) * slots, :], table_ref[1, k * slots : (k + 1) * slots, :]):
                    term = jnp.dot(part, owner_hot[side], preferred_element_type=jnp.float32)
                    picked = term if picked is None else picked + term
                velocity = jnp.sum(picked * slot_wide, axis=0, keepdims=True)
                term = rows[side][k] * velocity
                rate = term if rate is None else rate + term
        updated = jnp.maximum(shifted - steps_ref[step] * (gaps_ref[...] + rate), 0.0)
        shifted = updated + MOMENTUM * (updated - current)
        outs[0][...] = updated
        if scatter:
            outs[1][...] = shifted
        outs = outs[1 + int(scatter):]
    if scatter:
        out_ref = outs[0]
        for k in range(6):
            total = None
            for side in range(2):
                for part in split_pair(rows[side][k] * shifted):
                    weighted = slot_hot[side] * part
                    term = lax.dot_general(
                        owner_hot[side], weighted, (((1,), (1,)), ((), ())),
                        preferred_element_type=jnp.float32,
                    )
                    total = term if total is None else total + term
            out_ref[:, 0, k * slots : (k + 1) * slots] = total


def contact_step(step, owners, slots, bodies, frame, state, gaps, steps, table=None, scatter=True):
    contacts = frame.shape[1]
    gather = table is not None
    shapes = []
    if gather:
        shapes += [jax.ShapeDtypeStruct((1, contacts), jnp.float32)] * (1 + int(scatter))
    if scatter:
        shapes.append(jax.ShapeDtypeStruct((owners, 1, 6 * slots), jnp.float32))
    args = (bodies, frame) + tuple(state) + (gaps, steps) + ((table,) if gather else ())
    vmem = pl.BlockSpec(memory_space=pltpu.VMEM)
    specs = [vmem] * 5 + [pl.BlockSpec(memory_space=pltpu.SMEM)] + [vmem] * int(gather)
    return pl.pallas_call(
        functools.partial(contact_kernel, step, gather, scatter),
        out_shape=tuple(shapes),
        in_specs=specs,
        out_specs=tuple(vmem for _ in shapes),
        cost_estimate=pl.CostEstimate(
            flops=2 * 12 * owners * slots * 2 * contacts * (int(gather) + int(scatter)),
            transcendentals=0,
            bytes_accessed=4 * contacts * 600,
        ),
    )(*args)

def pair_kernel(position_ref, place_ref, force_ref, own_ref, out_ref, sums_ref, target_ref):
    targets = target_ref.shape[1]
    chunks = place_ref.shape[0]
    for c in range(3):
        row = position_ref[c : c + 1, :]
        target_ref[c] = jnp.broadcast_to(row, (128, targets)).T
    first_place = place_ref.shape[2] // 128 - 3

    def group(g, carry):
        rows = pl.ds(pl.multiple_of(g * 8, 8), 8)
        target_x = target_ref[0, rows, :]
        target_y = target_ref[1, rows, :]
        target_z = target_ref[2, rows, :]

        def chunk(j, sums):
            place = place_ref[j]
            force = force_ref[j]

            def lane_row(block, row):
                return block[:, row * 128 : (row + 1) * 128]

            r_x = target_x - lane_row(place, first_place)
            r_y = target_y - lane_row(place, first_place + 1)
            r_z = target_z - lane_row(place, first_place + 2)
            f_x, f_y, f_z = (lane_row(force, 0), lane_row(force, 1), lane_row(force, 2))
            t_x, t_y, t_z = (lane_row(force, 3), lane_row(force, 4), lane_row(force, 5))
            dist_sq = r_x * r_x + r_y * r_y + r_z * r_z
            inverse = lax.rsqrt(jnp.maximum(dist_sq, 1.0))
            inverse_sq = inverse * inverse
            c_cross = inverse_sq * inverse
            inverse_fifth = c_cross * inverse_sq
            c_iso = inverse + (2.0 / 3.0) * c_cross
            c_dyad = c_cross - 2.0 * inverse_fifth
            c_spin = 1.5 * inverse_fifth
            c_self = 0.5 * c_cross
            dyad = c_dyad * (r_x * f_x + r_y * f_y + r_z * f_z)
            spin = c_spin * (r_x * t_x + r_y * t_y + r_z * t_z)
            s_x = c_cross * r_x
            s_y = c_cross * r_y
            s_z = c_cross * r_z
            return (
                sums[0] + (c_iso * f_x + dyad * r_x + (t_y * s_z - t_z * s_y)),
                sums[1] + (c_iso * f_y + dyad * r_y + (t_z * s_x - t_x * s_z)),
                sums[2] + (c_iso * f_z + dyad * r_z + (t_x * s_y - t_y * s_x)),
                sums[3] + ((f_y * s_z - f_z * s_y) + spin * r_x - c_self * t_x),
                sums[4] + ((f_z * s_x - f_x * s_z) + spin * r_y - c_self * t_y),
                sums[5] + ((f_x * s_y - f_y * s_x) + spin * r_z - c_self * t_z),
            )

        zero = jnp.zeros((8, 128), jnp.float32)
        sums = lax.fori_loop(0, chunks, chunk, (zero,) * 6, unroll=64)
        for k in range(6):
            sums_ref[k, rows, :] = sums[k]
        return carry

    lax.fori_loop(0, targets // 8, group, 0)
    ones = jnp.ones((8, 128), jnp.bfloat16)
    for k in range(6):
        value = sums_ref[k]
        high = value.astype(jnp.bfloat16)
        rest = value - high.astype(jnp.float32)
        middle = rest.astype(jnp.bfloat16)
        low = (rest - middle.astype(jnp.float32)).astype(jnp.bfloat16)
        total = None
        for part in (high, middle, low):
            term = lax.dot_general(
                ones, part, (((1,), (1,)), ((), ())), preferred_element_type=jnp.float32
            )
            total = term if total is None else total + term
        scale = -0.25 if k < 3 else 1.125
        out_ref[k : k + 1, :] = total[0:1, :] + scale * own_ref[k : k + 1, :]


def mobility_own(positions, places, forces, own_forces):
    own_rows = own_forces.shape[1]
    sources = places.shape[0] * 128
    return pl.pallas_call(
        pair_kernel,
        out_shape=jax.ShapeDtypeStruct((6, own_rows), jnp.float32),
        scratch_shapes=[
            pltpu.VMEM((6, own_rows, 128), jnp.float32),
            pltpu.VMEM((3, own_rows, 128), jnp.float32),
        ],
        cost_estimate=pl.CostEstimate(
            flops=90 * own_rows * sources,
            transcendentals=own_rows * sources,
            bytes_accessed=4 * (9 * sources + 3 * own_rows * 128),
        ),
    )(positions, places, forces, own_forces)

def gather_all(block, devices):
    rows, width = block.shape
    spread = jnp.broadcast_to(block[None], (devices, rows, width))
    spread = lax.all_to_all(spread, AXES, 0, 0, tiled=True)
    return spread.transpose(1, 0, 2).reshape(rows, devices * width)


def scatter_sum(full, devices):
    rows, length = full.shape
    width = length // devices
    pieces = full.reshape(rows, devices, width).transpose(1, 0, 2)
    pieces = lax.all_to_all(pieces, AXES, 0, 0, tiled=True)
    return jnp.sum(pieces, 0)


def per_device(
    positions, contact_bodies, contact_frame, gaps, impulse_now, impulse_prev, step_sizes
):
    devices = lax.axis_size("src") * lax.axis_size("tgt")
    me = lax.axis_index("src") * lax.axis_size("tgt") + lax.axis_index("tgt")
    own_rows = positions.shape[1]
    body_count = own_rows * devices
    gaps_row = gaps.reshape(1, -1)
    state = (impulse_now.reshape(1, -1), impulse_prev.reshape(1, -1))
    (pieces,) = contact_step(0, devices, own_rows, contact_bodies, contact_frame, state, gaps_row, step_sizes)
    own_velocity = jnp.zeros((6, own_rows), jnp.float32)
    for k in range(ITERS):
        pieces = lax.all_to_all(pieces, AXES, 0, 0, tiled=True)
        own_forces = jnp.sum(pieces, 0).reshape(6, own_rows)
        if k == 0:
            block = jnp.concatenate([0.75 * own_forces, positions]).reshape(1, 1, 9 * own_rows)
            places = lax.all_to_all(
                jnp.broadcast_to(block, (devices, 1, 9 * own_rows)), AXES, 0, 0, tiled=True
            )
            forces = places
        else:
            block = (0.75 * own_forces).reshape(1, 1, 6 * own_rows)
            forces = lax.all_to_all(
                jnp.broadcast_to(block, (devices, 1, 6 * own_rows)), AXES, 0, 0, tiled=True
            )
        own_velocity = mobility_own(positions, places, forces, own_forces)
        every = jnp.broadcast_to(own_velocity.reshape(1, 6 * own_rows), (devices, 6 * own_rows))
        every = lax.all_to_all(every, AXES, 0, 0, tiled=True)
        last = k == ITERS - 1
        result = contact_step(
            k, devices, own_rows, contact_bodies, contact_frame, state, gaps_row, step_sizes, split_two(every.T), scatter=not last
        )
        state = result[:2]
        if not last:
            pieces = result[2]
    current = state[0].reshape(-1)
    return (current, own_velocity)


def solution(mesh):
    placed = (
        P(None, AXES),
        P(None, AXES),
        P(None, AXES),
        P(AXES),
        P(AXES),
        P(AXES),
        P(),
    )
    return jax.shard_map(
        per_device,
        mesh=mesh,
        in_specs=placed,
        out_specs=(P(AXES), P(None, AXES)),
        check_vma=False,
    )
```

```python
import functools

import jax
import jax.numpy as jnp
from jax import lax
from jax.experimental import pallas as pl
from jax.experimental.pallas import tpu as pltpu
from jax.sharding import PartitionSpec as P

ITERS = 2
MOMENTUM = 0.4
AXES = ("src", "tgt")
SOURCE_BLOCK = 1024


def cross_product(first, second):
    return jnp.stack(
        [
            first[1] * second[2] - first[2] * second[1],
            first[2] * second[0] - first[0] * second[2],
            first[0] * second[1] - first[1] * second[0],
        ]
    )


def contact_rows(frame):
    normal = frame[0:3]
    lever_first = cross_product(frame[3:6], normal)
    lever_second = cross_product(frame[6:9], normal)
    return (jnp.concatenate([-normal, -lever_first]), jnp.concatenate([normal, lever_second]))


def pair_block(target_pos, target_ids, source_pos, source_ids, forces):
    delta_x = target_pos[0][None, :] - source_pos[0][:, None]
    delta_y = target_pos[1][None, :] - source_pos[1][:, None]
    delta_z = target_pos[2][None, :] - source_pos[2][:, None]
    coincide = target_ids[None, :] == source_ids[:, None]
    dist_sq = jnp.where(coincide, 1.0, delta_x * delta_x + delta_y * delta_y + delta_z * delta_z)
    inverse = jnp.where(coincide, 0.0, lax.rsqrt(dist_sq))
    self_term = jnp.where(coincide, 1.0, 0.0)
    unit_x = delta_x * inverse
    unit_y = delta_y * inverse
    unit_z = delta_z * inverse
    force_x, force_y, force_z = (forces[0][:, None], forces[1][:, None], forces[2][:, None])
    torque_x, torque_y, torque_z = (forces[3][:, None], forces[4][:, None], forces[5][:, None])
    inverse_sq = inverse * inverse
    c_one = 0.75 * inverse
    c_two = 0.75 * inverse_sq
    c_three = 0.375 * inverse_sq * inverse
    along_force = unit_x * force_x + unit_y * force_y + unit_z * force_z
    along_torque = unit_x * torque_x + unit_y * torque_y + unit_z * torque_z
    isotropic = c_one * (1.0 + inverse_sq * (2.0 / 3.0)) + self_term
    dyadic = c_one * (1.0 - 2.0 * inverse_sq) * along_force
    vel_x = isotropic * force_x + dyadic * unit_x + c_two * (torque_y * unit_z - torque_z * unit_y)
    vel_y = isotropic * force_y + dyadic * unit_y + c_two * (torque_z * unit_x - torque_x * unit_z)
    vel_z = isotropic * force_z + dyadic * unit_z + c_two * (torque_x * unit_y - torque_y * unit_x)
    spin_self = 0.75 * self_term - c_three
    spin_x = (
        c_two * (force_y * unit_z - force_z * unit_y)
        + c_three * 3.0 * unit_x * along_torque
        + spin_self * torque_x
    )
    spin_y = (
        c_two * (force_z * unit_x - force_x * unit_z)
        + c_three * 3.0 * unit_y * along_torque
        + spin_self * torque_y
    )
    spin_z = (
        c_two * (force_x * unit_y - force_y * unit_x)
        + c_three * 3.0 * unit_z * along_torque
        + spin_self * torque_z
    )
    return jnp.stack(
        [
            jnp.sum(vel_x, 0),
            jnp.sum(vel_y, 0),
            jnp.sum(vel_z, 0),
            jnp.sum(spin_x, 0),
            jnp.sum(spin_y, 0),
            jnp.sum(spin_z, 0),
        ]
    )


def split_two(value):
    high = lax.reduce_precision(value, exponent_bits=8, mantissa_bits=7)
    low = value - high
    return jnp.stack([high, low]).astype(jnp.bfloat16)


def scatter_kernel(owner_ref, slot_ref, parts_ref, out_ref):
    slots = slot_ref.shape[0]
    owner = owner_ref[...]
    slot = slot_ref[...]
    for k in range(6):
        total = None
        for p in range(2):
            weighted = slot * parts_ref[p, k : k + 1, :]
            term = lax.dot_general(
                owner, weighted, (((1,), (1,)), ((), ())), preferred_element_type=jnp.float32
            )
            total = term if total is None else total + term
        out_ref[:, 0, k * slots : (k + 1) * slots] = total


def gather_kernel(owner_ref, slot_ref, parts_ref, out_ref):
    slots = slot_ref.shape[0]
    owner = owner_ref[...]
    slot = slot_ref[...].astype(jnp.float32)
    for k in range(6):
        picked = None
        for p in range(2):
            part = parts_ref[p, k * slots : (k + 1) * slots, :]
            term = jnp.dot(part, owner, preferred_element_type=jnp.float32)
            picked = term if picked is None else picked + term
        out_ref[k : k + 1, :] = jnp.sum(picked * slot, axis=0, keepdims=True)


def scatter_forces(owner_t, slot_t, end_force):
    owners, ends = owner_t.shape
    slots = slot_t.shape[0]
    parts = split_two(end_force)
    return pl.pallas_call(
        scatter_kernel,
        out_shape=jax.ShapeDtypeStruct((owners, 1, 6 * slots), jnp.float32),
        cost_estimate=pl.CostEstimate(
            flops=2 * 12 * owners * slots * ends, transcendentals=0, bytes_accessed=4 * ends * 300
        ),
    )(owner_t, slot_t, parts)


def gather_velocity(owner_t, slot_t, table):
    owners, ends = owner_t.shape
    slots = slot_t.shape[0]
    return pl.pallas_call(
        gather_kernel,
        out_shape=jax.ShapeDtypeStruct((6, ends), jnp.float32),
        cost_estimate=pl.CostEstimate(
            flops=2 * 12 * owners * slots * ends, transcendentals=0, bytes_accessed=4 * ends * 300
        ),
    )(owner_t, slot_t, split_two(table))


def split_pair(value):
    high = value.astype(jnp.bfloat16)
    low = (value - high.astype(jnp.float32)).astype(jnp.bfloat16)
    return (high, low)


def contact_kernel(step, gather, scatter, *refs):
    bodies_ref, frame_ref, current_ref, other_ref, gaps_ref, steps_ref = refs[:6]
    refs = refs[6:]
    if gather:
        table_ref, refs = refs[0], refs[1:]
    outs = refs
    contacts = frame_ref.shape[1]
    owners = outs[-1].shape[0] if scatter else table_ref.shape[1]
    slots = outs[-1].shape[2] // 6 if scatter else table_ref.shape[0] // 6
    frame = frame_ref[...]
    normal = (frame[0:1], frame[1:2], frame[2:3])

    def crossed(arm):
        return (
            arm[1] * normal[2] - arm[2] * normal[1],
            arm[2] * normal[0] - arm[0] * normal[2],
            arm[0] * normal[1] - arm[1] * normal[0],
        )

    first_lever = crossed((frame[3:4], frame[4:5], frame[5:6]))
    second_lever = crossed((frame[6:7], frame[7:8], frame[8:9]))
    rows = (
        tuple(-v for v in normal) + tuple(-v for v in first_lever),
        normal + second_lever,
    )
    owner_ids = lax.broadcasted_iota(jnp.int32, (owners, contacts), 0)
    slot_ids = lax.broadcasted_iota(jnp.int32, (slots, contacts), 0)
    owner_hot, slot_hot = [], []
    for side in range(2):
        body = bodies_ref[side : side + 1, :]
        owner_hot.append((owner_ids == body // slots).astype(jnp.bfloat16))
        slot_hot.append((slot_ids == body % slots).astype(jnp.bfloat16))
    current = current_ref[...]
    if step == 0:
        shifted = current + MOMENTUM * (current - other_ref[...])
    else:
        shifted = other_ref[...]
    if gather:
        rate = None
        for side in range(2):
            slot_mask = slot_hot[side] > 0
            for k in range(6):
                picked = None
                for part in split_pair(table_ref[k * slots : (k + 1) * slots, :]):
                    term = jnp.dot(part, owner_hot[side], preferred_element_type=jnp.float32)
                    picked = term if picked is None else picked + term
                velocity = jnp.sum(jnp.where(slot_mask, picked, 0.0), axis=0, keepdims=True)
                term = rows[side][k] * velocity
                rate = term if rate is None else rate + term
        updated = jnp.maximum(shifted - steps_ref[step] * (gaps_ref[...] + rate), 0.0)
        shifted = updated + MOMENTUM * (updated - current)
        outs[0][...] = updated
        if scatter:
            outs[1][...] = shifted
        outs = outs[1 + int(scatter):]
    if scatter:
        out_ref = outs[0]
        for k in range(6):
            total = None
            for side in range(2):
                for part in split_pair(rows[side][k] * shifted):
                    weighted = slot_hot[side] * part
                    term = lax.dot_general(
                        owner_hot[side], weighted, (((1,), (1,)), ((), ())),
                        preferred_element_type=jnp.float32,
                    )
                    total = term if total is None else total + term
            out_ref[:, 0, k * slots : (k + 1) * slots] = total


def contact_step(step, owners, slots, bodies, frame, state, gaps, steps, table=None, scatter=True):
    contacts = frame.shape[1]
    gather = table is not None
    shapes = []
    if gather:
        shapes += [jax.ShapeDtypeStruct((1, contacts), jnp.float32)] * (1 + int(scatter))
    if scatter:
        shapes.append(jax.ShapeDtypeStruct((owners, 1, 6 * slots), jnp.float32))
    args = (bodies, frame) + tuple(state) + (gaps, steps) + ((table,) if gather else ())
    vmem = pl.BlockSpec(memory_space=pltpu.VMEM)
    specs = [vmem] * 5 + [pl.BlockSpec(memory_space=pltpu.SMEM)] + [vmem] * int(gather)
    return pl.pallas_call(
        functools.partial(contact_kernel, step, gather, scatter),
        out_shape=tuple(shapes),
        in_specs=specs,
        out_specs=tuple(vmem for _ in shapes),
        cost_estimate=pl.CostEstimate(
            flops=2 * 12 * owners * slots * 2 * contacts * (int(gather) + int(scatter)),
            transcendentals=0,
            bytes_accessed=4 * contacts * 600,
        ),
    )(*args)

def pair_kernel(position_ref, place_ref, force_ref, own_ref, out_ref, sums_ref, target_ref):
    targets = target_ref.shape[1]
    chunks = place_ref.shape[0]
    for c in range(3):
        row = position_ref[c : c + 1, :]
        target_ref[c] = jnp.broadcast_to(row, (128, targets)).T
    first_place = place_ref.shape[2] // 128 - 3

    def group(g, carry):
        rows = pl.ds(pl.multiple_of(g * 8, 8), 8)
        target_x = target_ref[0, rows, :]
        target_y = target_ref[1, rows, :]
        target_z = target_ref[2, rows, :]

        def chunk(j, sums):
            place = place_ref[j]
            force = force_ref[j]

            def lane_row(block, row):
                return block[:, row * 128 : (row + 1) * 128]

            r_x = target_x - lane_row(place, first_place)
            r_y = target_y - lane_row(place, first_place + 1)
            r_z = target_z - lane_row(place, first_place + 2)
            f_x, f_y, f_z = (lane_row(force, 0), lane_row(force, 1), lane_row(force, 2))
            t_x, t_y, t_z = (lane_row(force, 3), lane_row(force, 4), lane_row(force, 5))
            dist_sq = r_x * r_x + r_y * r_y + r_z * r_z
            inverse = lax.rsqrt(jnp.maximum(dist_sq, 1.0))
            inverse_sq = inverse * inverse
            c_cross = inverse_sq * inverse
            inverse_fifth = c_cross * inverse_sq
            c_iso = inverse + (2.0 / 3.0) * c_cross
            c_dyad = c_cross - 2.0 * inverse_fifth
            c_spin = 1.5 * inverse_fifth
            c_self = 0.5 * c_cross
            dyad = c_dyad * (r_x * f_x + r_y * f_y + r_z * f_z)
            spin = c_spin * (r_x * t_x + r_y * t_y + r_z * t_z)
            s_x = c_cross * r_x
            s_y = c_cross * r_y
            s_z = c_cross * r_z
            return (
                sums[0] + (c_iso * f_x + dyad * r_x + (t_y * s_z - t_z * s_y)),
                sums[1] + (c_iso * f_y + dyad * r_y + (t_z * s_x - t_x * s_z)),
                sums[2] + (c_iso * f_z + dyad * r_z + (t_x * s_y - t_y * s_x)),
                sums[3] + ((f_y * s_z - f_z * s_y) + spin * r_x - c_self * t_x),
                sums[4] + ((f_z * s_x - f_x * s_z) + spin * r_y - c_self * t_y),
                sums[5] + ((f_x * s_y - f_y * s_x) + spin * r_z - c_self * t_z),
            )

        zero = jnp.zeros((8, 128), jnp.float32)
        sums = lax.fori_loop(0, chunks, chunk, (zero,) * 6, unroll=64)
        for k in range(6):
            sums_ref[k, rows, :] = sums[k]
        return carry

    lax.fori_loop(0, targets // 8, group, 0)
    ones = jnp.ones((8, 128), jnp.bfloat16)
    for k in range(6):
        value = sums_ref[k]
        high = value.astype(jnp.bfloat16)
        rest = value - high.astype(jnp.float32)
        middle = rest.astype(jnp.bfloat16)
        low = (rest - middle.astype(jnp.float32)).astype(jnp.bfloat16)
        total = None
        for part in (high, middle, low):
            term = lax.dot_general(
                ones, part, (((1,), (1,)), ((), ())), preferred_element_type=jnp.float32
            )
            total = term if total is None else total + term
        scale = -0.25 if k < 3 else 1.125
        out_ref[k : k + 1, :] = total[0:1, :] + scale * own_ref[k : k + 1, :]


def mobility_own(positions, places, forces, own_forces):
    own_rows = own_forces.shape[1]
    sources = places.shape[0] * 128
    return pl.pallas_call(
        pair_kernel,
        out_shape=jax.ShapeDtypeStruct((6, own_rows), jnp.float32),
        scratch_shapes=[
            pltpu.VMEM((6, own_rows, 128), jnp.float32),
            pltpu.VMEM((3, own_rows, 128), jnp.float32),
        ],
        cost_estimate=pl.CostEstimate(
            flops=90 * own_rows * sources,
            transcendentals=own_rows * sources,
            bytes_accessed=4 * (9 * sources + 3 * own_rows * 128),
        ),
    )(positions, places, forces, own_forces)

def gather_all(block, devices):
    rows, width = block.shape
    spread = jnp.broadcast_to(block[None], (devices, rows, width))
    spread = lax.all_to_all(spread, AXES, 0, 0, tiled=True)
    return spread.transpose(1, 0, 2).reshape(rows, devices * width)


def scatter_sum(full, devices):
    rows, length = full.shape
    width = length // devices
    pieces = full.reshape(rows, devices, width).transpose(1, 0, 2)
    pieces = lax.all_to_all(pieces, AXES, 0, 0, tiled=True)
    return jnp.sum(pieces, 0)


def per_device(
    positions, contact_bodies, contact_frame, gaps, impulse_now, impulse_prev, step_sizes
):
    devices = lax.axis_size("src") * lax.axis_size("tgt")
    me = lax.axis_index("src") * lax.axis_size("tgt") + lax.axis_index("tgt")
    own_rows = positions.shape[1]
    body_count = own_rows * devices
    gaps_row = gaps.reshape(1, -1)
    state = (impulse_now.reshape(1, -1), impulse_prev.reshape(1, -1))
    (pieces,) = contact_step(0, devices, own_rows, contact_bodies, contact_frame, state, gaps_row, step_sizes)
    own_velocity = jnp.zeros((6, own_rows), jnp.float32)
    for k in range(ITERS):
        pieces = lax.all_to_all(pieces, AXES, 0, 0, tiled=True)
        own_forces = jnp.sum(pieces, 0).reshape(6, own_rows)
        if k == 0:
            block = jnp.concatenate([0.75 * own_forces, positions]).reshape(1, 1, 9 * own_rows)
            places = lax.all_to_all(
                jnp.broadcast_to(block, (devices, 1, 9 * own_rows)), AXES, 0, 0, tiled=True
            )
            forces = places
        else:
            block = (0.75 * own_forces).reshape(1, 1, 6 * own_rows)
            forces = lax.all_to_all(
                jnp.broadcast_to(block, (devices, 1, 6 * own_rows)), AXES, 0, 0, tiled=True
            )
        own_velocity = mobility_own(positions, places, forces, own_forces)
        every = jnp.broadcast_to(own_velocity.reshape(1, 6 * own_rows), (devices, 6 * own_rows))
        every = lax.all_to_all(every, AXES, 0, 0, tiled=True)
        last = k == ITERS - 1
        result = contact_step(
            k, devices, own_rows, contact_bodies, contact_frame, state, gaps_row, step_sizes, every.T, scatter=not last
        )
        state = result[:2]
        if not last:
            pieces = result[2]
    current = state[0].reshape(-1)
    return (current, own_velocity)


def solution(mesh):
    placed = (
        P(None, AXES),
        P(None, AXES),
        P(None, AXES),
        P(AXES),
        P(AXES),
        P(AXES),
        P(),
    )
    return jax.shard_map(
        per_device,
        mesh=mesh,
        in_specs=placed,
        out_specs=(P(AXES), P(None, AXES)),
        check_vma=False,
    )
```
